32 devices in a mesh: section: 2 (over core), row: 4 (over y, x), col: 4 (over z).
Axes of the slice: x: 2, y: 2, z: 4, core: 2. Of those that a mesh axis runs over, the one named last changes fastest.
Arguments:
- checkpoints: bfloat16 [2, 4, 64, 128, 128], P('section', None, 'row', 'col'), may hold values from -1 to 1
- kernels: bfloat16 [4, 3, 3, 128, 128], P('section'), may hold values from -0.25 to 0.25
- cotangent: bfloat16 [4, 64, 128, 128], P(None, 'row', 'col'), may hold values from -1.5 to 1.5
- plan: int32 [4], replicated, may hold values from 0 to 3, each once
Outputs:
- boundary_grad: bfloat16 [2, 4, 64, 128, 128], P('section', None, 'row', 'col')
- kernel_grad: float32 [4, 3, 3, 128, 128], P('section')
The draws below stay inside these ranges and needn't reach their ends.
Inputs may be any that keep to these rules, and one draw needn't show every extreme that they name: plan names each of the 4 microbatches exactly once; slot k of cotangent belongs to microbatch plan[k].
All inputs are finite; a program needn't handle non-finite values.
Results may differ from the reference program's by a relative error of at most 0.015.
Values may be sent and summed in bfloat16 or wider, within the bound.
No kernel may reach another device: no remote copies, remote signals or barrier semaphores. Data moves between devices by JAX's collectives and lax.ppermute only.
A program may use at most 64 MiB of HBM per device.

```python
import jax
import jax.numpy as jnp
from jax import lax

CHANNELS = 128
SECTION_LAYERS = 2
MICROBATCHES = 4
SECTIONS = 2
LAYERS = 4
IMAGE_ROWS = 64
IMAGE_COLS = 128


def block_levels(own_key, dims, shards, low, largest):
    factor_of, own = 1.0, jax.random.fold_in(own_key, 6)
    for dim, blocks in shards:
        heights = jnp.exp(jax.random.uniform(jax.random.fold_in(own, dim), (blocks,), jnp.float32, low / len(shards), largest / len(shards)))
        factor_of = factor_of * jnp.repeat(heights, dims[dim] // blocks).reshape([-1 if axis == dim else 1 for axis in range(len(dims))])
    return factor_of


def scatter_about(stream_key, extent, width, limit, pieces=(), held_as=jnp.bfloat16):
    gain = block_levels(stream_key, extent, pieces, -0.22, 0.18) if pieces else 1.0
    entries = jax.random.normal(stream_key, extent, jnp.float32) * width * gain
    return jnp.minimum(jnp.maximum(entries, -limit), limit).astype(held_as)


def setup_inputs(seed: int = 0) -> dict:
    splits = jax.random.split(jax.random.key(seed), 5)
    checkpoints = jnp.clip(jax.random.uniform(splits[0], (SECTIONS, MICROBATCHES, IMAGE_ROWS, IMAGE_COLS, CHANNELS), jnp.float32, -1.0, 1.0) * block_levels(splits[0], (SECTIONS, MICROBATCHES, IMAGE_ROWS, IMAGE_COLS, CHANNELS), ((0, 2), (2, 4), (3, 4)), -0.4, 0.0), -1.0, 1.0).astype(jnp.bfloat16)
    kernels = scatter_about(splits[1], (LAYERS, 3, 3, CHANNELS, CHANNELS), (4 * CHANNELS) ** -0.5, 0.25, ((0, 2),))
    cotangent = scatter_about(splits[2], (MICROBATCHES, IMAGE_ROWS, IMAGE_COLS, CHANNELS), 0.25, 1.5, ((1, 4), (2, 4)))
    plan = jax.random.permutation(splits[3], MICROBATCHES).astype(jnp.int32)
    return dict(checkpoints=checkpoints, kernels=kernels, cotangent=cotangent, plan=plan)


def convolve(padded, kernel):
    return lax.conv_general_dilated(padded.astype(jnp.float32), kernel.astype(jnp.float32), (1, 1), "VALID", dimension_numbers=("NHWC", "HWIO", "NHWC"), precision=lax.Precision.HIGHEST)


def pad_rim(values_in):
    return jnp.pad(values_in, ((0, 0), (1, 1), (1, 1), (0, 0)))


def kernel_terms(padded, signal):
    rows_out = []
    for a in range(3):
        tap_row = []
        for b in range(3):
            window = padded[:, a:a + signal.shape[1], b:b + signal.shape[2]].astype(jnp.float32)
            tap_row.append(jnp.einsum("nhwi,nhwo->io", window, signal.astype(jnp.float32), precision=lax.Precision.HIGHEST))
        rows_out.append(jnp.stack(tap_row))
    return jnp.stack(rows_out)


def reference(checkpoints, kernels, cotangent, plan):
    incoming = cotangent
    boundary_list = []
    kernel_list = []
    for section_idx in reversed(range(SECTIONS)):
        current = jnp.take(checkpoints[section_idx], plan, axis=0)
        inputs_list = []
        outputs_list = []
        for layer_idx in range(SECTION_LAYERS):
            padded = pad_rim(current)
            inputs_list.append(padded)
            current = jnp.tanh(convolve(padded, kernels[section_idx * SECTION_LAYERS + layer_idx])).astype(jnp.bfloat16)
            outputs_list.append(current)
        gradient = incoming.astype(jnp.float32)
        layer_terms = [None] * SECTION_LAYERS
        for layer_idx in reversed(range(SECTION_LAYERS)):
            output = outputs_list[layer_idx].astype(jnp.float32)
            signal = (gradient * (1.0 - output * output)).astype(jnp.bfloat16)
            layer_terms[layer_idx] = kernel_terms(inputs_list[layer_idx], signal)
            flipped = jnp.transpose(kernels[section_idx * SECTION_LAYERS + layer_idx][::-1, ::-1], (0, 1, 3, 2))
            gradient = convolve(pad_rim(signal), flipped)
        incoming = gradient.astype(jnp.bfloat16)
        boundary_list.insert(0, jnp.zeros_like(incoming).at[plan].set(incoming))
        kernel_list = layer_terms + kernel_list
    boundary_grad = jnp.stack(boundary_list)
    kernel_grad = jnp.stack(kernel_list) / MICROBATCHES
    return boundary_grad, kernel_grad
```

```python
import jax
import jax.numpy as jnp
from jax import lax
from jax.sharding import PartitionSpec as P

AXES = ("section", "row", "col")


def sizes():
    return tuple(lax.axis_size(axis) for axis in AXES)


def flat_index(position, shape):
    section, row, col = position
    return (section * shape[1] + row) * shape[2] + col


def rim_piece(block, width, dr, dc):
    rows, cols = block.shape[1], block.shape[2]
    row_span = {-1: (rows - width, rows), 0: (0, rows), 1: (0, width)}[dr]
    col_span = {-1: (cols - width, cols), 0: (0, cols), 1: (0, width)}[dc]
    return block[:, row_span[0] : row_span[1], col_span[0] : col_span[1]]


def with_rim(block, width, from_section, sections_used):
    shape = sizes()
    bands = []
    for dr in (-1, 0, 1):
        band = []
        for dc in (-1, 0, 1):
            piece = rim_piece(block, width, dr, dc)
            if from_section == 0 and dr == 0 and dc == 0:
                band.append(piece)
                continue
            pairs = []
            for s in sections_used:
                for r in range(shape[1]):
                    for c in range(shape[2]):
                        source = (s + from_section, r + dr, c + dc)
                        if 0 <= source[0] < shape[0] and 0 <= source[1] < shape[1] and 0 <= source[2] < shape[2]:
                            pairs.append((flat_index(source, shape), flat_index((s, r, c), shape)))
            band.append(lax.ppermute(piece, AXES, pairs))
        bands.append(jnp.concatenate(band, axis=2))
    return jnp.concatenate(bands, axis=1)


def inside_mask(tile_rows, tile_cols, width):
    image_rows = tile_rows * lax.axis_size("row")
    image_cols = tile_cols * lax.axis_size("col")
    rows = lax.axis_index("row") * tile_rows - width + jnp.arange(tile_rows + 2 * width)
    cols = lax.axis_index("col") * tile_cols - width + jnp.arange(tile_cols + 2 * width)
    row_ok = (rows >= 0) & (rows < image_rows)
    col_ok = (cols >= 0) & (cols < image_cols)
    return (row_ok[:, None] & col_ok[None, :])[None, :, :, None]


def convolve(padded, kernel):
    return lax.conv_general_dilated(
        padded,
        kernel,
        (1, 1),
        "VALID",
        dimension_numbers=("NHWC", "HWIO", "NHWC"),
        preferred_element_type=jnp.float32,
    )


def kernel_terms(padded, signal):
    channels = signal.shape[3]
    flat_signal = signal.reshape(-1, channels)
    rows_out = []
    for a in range(3):
        tap_row = []
        for b in range(3):
            window = padded[:, a : a + signal.shape[1], b : b + signal.shape[2]].reshape(-1, channels)
            tap_row.append(
                lax.dot_general(
                    window,
                    flat_signal,
                    (((0,), (0,)), ((), ())),
                    preferred_element_type=jnp.float32,
                )
            )
        rows_out.append(jnp.stack(tap_row))
    return jnp.stack(rows_out)


def crop(block, width):
    return block[:, width : block.shape[1] - width, width : block.shape[2] - width]


def summed_over_tiles(grads, section):
    shape = sizes()
    steps = []
    for axis, dim in (("row", 1), ("col", 2)):
        distance = 1
        while distance < shape[dim]:
            steps.append((axis, dim, distance))
            distance *= 2

    def exchange(values, dim, distance):
        pairs = []
        sections_used = range(shape[0]) if section is None else (section,)
        for s in sections_used:
            for r in range(shape[1]):
                for c in range(shape[2]):
                    position = [s, r, c]
                    partner = list(position)
                    partner[dim] = position[dim] ^ distance
                    pairs.append((flat_index(position, shape), flat_index(partner, shape)))
        return lax.ppermute(values, AXES, pairs)

    current = grads.reshape(-1)
    kept = []
    for axis, dim, distance in steps:
        half = current.shape[0] // 2
        upper = (lax.axis_index(axis) // distance) % 2 == 1
        low, high = current[:half], current[half:]
        send = jnp.where(upper, low, high).astype(jnp.bfloat16)
        mine = jnp.where(upper, high, low).astype(jnp.bfloat16)
        other = exchange(send, dim, distance)
        current = mine.astype(jnp.float32) + other.astype(jnp.float32)
        kept.append((dim, distance, upper))
    current = current.astype(jnp.bfloat16)
    for dim, distance, upper in reversed(kept):
        other = exchange(current, dim, distance)
        current = jnp.where(
            upper, jnp.concatenate([other, current]), jnp.concatenate([current, other])
        )
    return current.astype(jnp.float32).reshape(grads.shape)


def local(checkpoints, kernels, cotangent, plan):
    sections_count, row_count, col_count = sizes()
    section_index = lax.axis_index("section")
    batches, tile_rows, tile_cols, channels = checkpoints.shape[1:]
    layer_count = kernels.shape[0]
    flipped = jnp.transpose(kernels[:, ::-1, ::-1], (0, 1, 2, 4, 3))
    inverse = jnp.sum(
        jnp.arange(batches)[:, None] * (plan[:, None] == jnp.arange(batches)[None, :]), axis=0
    )
    top_cotangent = jnp.take(cotangent, inverse, axis=0)

    rim = 2 * layer_count
    first = with_rim(checkpoints[0], rim, 0, range(sections_count))
    inputs_list = [first]
    current = first
    for layer_idx in range(layer_count):
        width = rim - layer_idx - 1
        current = jnp.tanh(convolve(current, kernels[layer_idx]))
        current = jnp.where(inside_mask(tile_rows, tile_cols, width), current, 0.0)
        current = current.astype(jnp.bfloat16)
        inputs_list.append(current)

    def backward(top_ext):
        gradient = top_ext.astype(jnp.float32)
        terms = [None] * layer_count
        for layer_idx in reversed(range(layer_count)):
            width = layer_idx
            output = crop(inputs_list[layer_idx + 1], 2 * (layer_count - layer_idx - 1))
            output = output.astype(jnp.float32)
            signal = gradient * (1.0 - output * output)
            signal = jnp.where(inside_mask(tile_rows, tile_cols, width + 1), signal, 0.0)
            signal = signal.astype(jnp.bfloat16)
            terms[layer_idx] = kernel_terms(
                crop(inputs_list[layer_idx], 2 * layer_count - layer_idx - 1),
                crop(signal, width + 1),
            )
            gradient = convolve(signal, flipped[layer_idx])
        return gradient.astype(jnp.bfloat16), jnp.stack(terms)

    top_ext = with_rim(top_cotangent, layer_count, 0, (sections_count - 1,))
    boundary = jnp.zeros((batches, tile_rows, tile_cols, channels), jnp.bfloat16)
    gathered = jnp.zeros((layer_count, 3, 3, channels, channels), jnp.float32)
    for tick in range(sections_count):
        active = sections_count - 1 - tick
        result, terms = backward(top_ext)
        is_active = section_index == active
        boundary = jnp.where(is_active, result, boundary)
        reduced = summed_over_tiles(terms, active)
        gathered = jnp.where(is_active, reduced, gathered)
        if tick + 1 < sections_count:
            top_ext = with_rim(result, layer_count, 1, (active - 1,))
    kernel_grad = gathered / batches
    return (boundary[None], kernel_grad)


def solution(mesh):
    return jax.shard_map(
        local,
        mesh=mesh,
        in_specs=(
            P("section", None, "row", "col", None),
            P("section", None, None, None, None),
            P(None, "row", "col", None),
            P(),
        ),
        out_specs=(P("section", None, "row", "col", None), P("section", None, None, None, None)),
        check_vma=False,
    )
```

```python
import jax
import jax.numpy as jnp
from jax import lax
from jax.sharding import PartitionSpec as P

AXES = ("section", "row", "col")


def sizes():
    return tuple(lax.axis_size(axis) for axis in AXES)


def flat_index(position, shape):
    section, row, col = position
    return (section * shape[1] + row) * shape[2] + col


def rim_piece(block, width, dr, dc):
    rows, cols = block.shape[1], block.shape[2]
    row_span = {-1: (rows - width, rows), 0: (0, rows), 1: (0, width)}[dr]
    col_span = {-1: (cols - width, cols), 0: (0, cols), 1: (0, width)}[dc]
    return block[:, row_span[0] : row_span[1], col_span[0] : col_span[1]]


def from_neighbours(block, width, dim, from_section, sections_used):
    shape = sizes()
    parts = []
    for step in (-1, 0, 1):
        size = block.shape[dim]
        span = {-1: (size - width, size), 0: (0, size), 1: (0, width)}[step]
        piece = lax.slice_in_dim(block, span[0], span[1], axis=dim)
        if from_section == 0 and step == 0:
            parts.append(piece)
            continue
        pairs = []
        for s in sections_used:
            for r in range(shape[1]):
                for c in range(shape[2]):
                    source = [s + from_section, r, c]
                    source[dim] += step
                    if all(0 <= source[k] < shape[k] for k in range(3)):
                        pairs.append((flat_index(source, shape), flat_index((s, r, c), shape)))
        parts.append(lax.ppermute(piece, AXES, pairs))
    return jnp.concatenate(parts, axis=dim)


def with_rim(block, width, from_section, sections_used):
    rows_done = from_neighbours(block, width, 1, from_section, sections_used)
    return from_neighbours(rows_done, width, 2, 0, sections_used)


def inside_mask(tile_rows, tile_cols, width):
    image_rows = tile_rows * lax.axis_size("row")
    image_cols = tile_cols * lax.axis_size("col")
    rows = lax.axis_index("row") * tile_rows - width + jnp.arange(tile_rows + 2 * width)
    cols = lax.axis_index("col") * tile_cols - width + jnp.arange(tile_cols + 2 * width)
    row_ok = (rows >= 0) & (rows < image_rows)
    col_ok = (cols >= 0) & (cols < image_cols)
    return (row_ok[:, None] & col_ok[None, :])[None, :, :, None]


def convolve(padded, kernel):
    return lax.conv_general_dilated(
        padded,
        kernel,
        (1, 1),
        "VALID",
        dimension_numbers=("NHWC", "HWIO", "NHWC"),
        preferred_element_type=jnp.float32,
    )


def kernel_terms(padded, signal):
    channels = signal.shape[3]
    flat_signal = signal.reshape(-1, channels)
    rows_out = []
    for a in range(3):
        tap_row = []
        for b in range(3):
            window = padded[:, a : a + signal.shape[1], b : b + signal.shape[2]].reshape(-1, channels)
            tap_row.append(
                lax.dot_general(
                    window,
                    flat_signal,
                    (((0,), (0,)), ((), ())),
                    preferred_element_type=jnp.float32,
                )
            )
        rows_out.append(jnp.stack(tap_row))
    return jnp.stack(rows_out)


def crop(block, width):
    return block[:, width : block.shape[1] - width, width : block.shape[2] - width]


def summed_over_tiles(grads, section):
    shape = sizes()
    steps = []
    for axis, dim in (("row", 1), ("col", 2)):
        distance = 1
        while distance < shape[dim]:
            steps.append((axis, dim, distance))
            distance *= 2

    def exchange(values, dim, distance):
        pairs = []
        sections_used = range(shape[0]) if section is None else (section,)
        for s in sections_used:
            for r in range(shape[1]):
                for c in range(shape[2]):
                    position = [s, r, c]
                    partner = list(position)
                    partner[dim] = position[dim] ^ distance
                    pairs.append((flat_index(position, shape), flat_index(partner, shape)))
        return lax.ppermute(values, AXES, pairs)

    current = grads.reshape(-1)
    kept = []
    for axis, dim, distance in steps:
        half = current.shape[0] // 2
        upper = (lax.axis_index(axis) // distance) % 2 == 1
        low, high = current[:half], current[half:]
        send = jnp.where(upper, low, high).astype(jnp.bfloat16)
        mine = jnp.where(upper, high, low).astype(jnp.bfloat16)
        other = exchange(send, dim, distance)
        current = mine.astype(jnp.float32) + other.astype(jnp.float32)
        kept.append((dim, distance, upper))
    current = current.astype(jnp.bfloat16)
    for dim, distance, upper in reversed(kept):
        other = exchange(current, dim, distance)
        current = jnp.where(
            upper, jnp.concatenate([other, current]), jnp.concatenate([current, other])
        )
    return current.astype(jnp.float32).reshape(grads.shape)


def local(checkpoints, kernels, cotangent, plan):
    sections_count, row_count, col_count = sizes()
    section_index = lax.axis_index("section")
    batches, tile_rows, tile_cols, channels = checkpoints.shape[1:]
    layer_count = kernels.shape[0]
    flipped = jnp.transpose(kernels[:, ::-1, ::-1], (0, 1, 2, 4, 3))
    inverse = jnp.sum(
        jnp.arange(batches)[:, None] * (plan[:, None] == jnp.arange(batches)[None, :]), axis=0
    )
    top_cotangent = jnp.take(cotangent, inverse, axis=0)

    deep = layer_count * (sections_count + 1) <= min(tile_rows, tile_cols)
    if deep:
        top_rim = [layer_count * (s + 1) for s in range(sections_count)]
    else:
        top_rim = [layer_count] * sections_count
    rim = top_rim[-1] + layer_count
    both = jnp.concatenate([checkpoints[0], top_cotangent], axis=3)
    both = with_rim(both, rim, 0, range(sections_count))
    first = both[..., :channels]
    top_ext = crop(both[..., channels:], rim - top_rim[-1])
    inputs_list = [first]
    current = first
    for layer_idx in range(layer_count):
        width = rim - layer_idx - 1
        current = jnp.tanh(convolve(current, kernels[layer_idx]))
        current = jnp.where(inside_mask(tile_rows, tile_cols, width), current, 0.0)
        current = current.astype(jnp.bfloat16)
        inputs_list.append(current)

    def backward(top_ext, top_width):
        gradient = top_ext.astype(jnp.float32)
        terms = [None] * layer_count
        for layer_idx in reversed(range(layer_count)):
            width = top_width - (layer_count - 1 - layer_idx)
            output = crop(inputs_list[layer_idx + 1], rim - layer_idx - 1 - width)
            output = output.astype(jnp.float32)
            signal = gradient * (1.0 - output * output)
            signal = jnp.where(inside_mask(tile_rows, tile_cols, width), signal, 0.0)
            signal = signal.astype(jnp.bfloat16)
            terms[layer_idx] = kernel_terms(
                crop(inputs_list[layer_idx], rim - layer_idx - 1), crop(signal, width)
            )
            gradient = convolve(signal, flipped[layer_idx])
        return gradient.astype(jnp.bfloat16), jnp.stack(terms)

    boundary = jnp.zeros((batches, tile_rows, tile_cols, channels), jnp.bfloat16)
    gathered = jnp.zeros((layer_count, 3, 3, channels, channels), jnp.float32)
    for tick in range(sections_count):
        active = sections_count - 1 - tick
        result, terms = backward(top_ext, top_rim[active])
        is_active = section_index == active
        result_width = top_rim[active] - layer_count
        boundary = jnp.where(is_active, crop(result, result_width), boundary)
        if tick + 1 < sections_count:
            if deep:
                pairs = [
                    (flat_index((active, r, c), sizes()), flat_index((active - 1, r, c), sizes()))
                    for r in range(row_count)
                    for c in range(col_count)
                ]
                top_ext = lax.ppermute(result, AXES, pairs)
            else:
                top_ext = with_rim(result, layer_count, 1, (active - 1,))
            top_ext, terms = lax.optimization_barrier((top_ext, terms))
        reduced = summed_over_tiles(terms, active)
        gathered = jnp.where(is_active, reduced, gathered)
    kernel_grad = gathered / batches
    return (boundary[None], kernel_grad)


def solution(mesh):
    return jax.shard_map(
        local,
        mesh=mesh,
        in_specs=(
            P("section", None, "row", "col", None),
            P("section", None, None, None, None),
            P(None, "row", "col", None),
            P(),
        ),
        out_specs=(P("section", None, "row", "col", None), P("section", None, None, None, None)),
        check_vma=False,
    )
```

```python
import jax
import jax.numpy as jnp
from jax import lax
from jax.sharding import PartitionSpec as P

AXES = ("section", "row", "col")


def sizes():
    return tuple(lax.axis_size(axis) for axis in AXES)


def flat_index(position, shape):
    section, row, col = position
    return (section * shape[1] + row) * shape[2] + col


def rim_piece(block, width, dr, dc):
    rows, cols = block.shape[1], block.shape[2]
    row_span = {-1: (rows - width, rows), 0: (0, rows), 1: (0, width)}[dr]
    col_span = {-1: (cols - width, cols), 0: (0, cols), 1: (0, width)}[dc]
    return block[:, row_span[0] : row_span[1], col_span[0] : col_span[1]]


def from_neighbours(block, width, dim, from_section, sections_used):
    shape = sizes()
    parts = []
    for step in (-1, 0, 1):
        size = block.shape[dim]
        span = {-1: (size - width, size), 0: (0, size), 1: (0, width)}[step]
        piece = lax.slice_in_dim(block, span[0], span[1], axis=dim)
        if from_section == 0 and step == 0:
            parts.append(piece)
            continue
        pairs = []
        for s in sections_used:
            for r in range(shape[1]):
                for c in range(shape[2]):
                    source = [s + from_section, r, c]
                    source[dim] += step
                    if all(0 <= source[k] < shape[k] for k in range(3)):
                        pairs.append((flat_index(source, shape), flat_index((s, r, c), shape)))
        parts.append(lax.ppermute(piece, AXES, pairs))
    return jnp.concatenate(parts, axis=dim)


def with_rim(block, width, from_section, sections_used):
    rows_done = from_neighbours(block, width, 1, from_section, sections_used)
    return from_neighbours(rows_done, width, 2, 0, sections_used)


def inside_mask(tile_rows, tile_cols, width):
    image_rows = tile_rows * lax.axis_size("row")
    image_cols = tile_cols * lax.axis_size("col")
    rows = lax.axis_index("row") * tile_rows - width + jnp.arange(tile_rows + 2 * width)
    cols = lax.axis_index("col") * tile_cols - width + jnp.arange(tile_cols + 2 * width)
    row_ok = (rows >= 0) & (rows < image_rows)
    col_ok = (cols >= 0) & (cols < image_cols)
    return (row_ok[:, None] & col_ok[None, :])[None, :, :, None]


def convolve(padded, kernel):
    return lax.conv_general_dilated(
        padded,
        kernel,
        (1, 1),
        "VALID",
        dimension_numbers=("NHWC", "HWIO", "NHWC"),
        preferred_element_type=jnp.float32,
    )


def kernel_terms(padded, signal):
    terms = lax.conv_general_dilated(
        padded,
        signal,
        (1, 1),
        "VALID",
        dimension_numbers=("CHWN", "IHWO", "NHWC"),
        preferred_element_type=jnp.float32,
    )
    return jnp.transpose(terms, (1, 2, 0, 3))


def crop(block, width):
    return block[:, width : block.shape[1] - width, width : block.shape[2] - width]


def summed_over_tiles(grads):
    shape = sizes()

    def distances(count):
        found, distance = [], 1
        while distance < count:
            found.append(distance)
            distance *= 2
        return found

    def exchange(values, axis, distance):
        count = lax.axis_size(axis)
        return lax.ppermute(values, axis, [(i, i ^ distance) for i in range(count)])

    current = grads.reshape(-1)
    kept = []
    for distance in distances(shape[1]):
        half = current.shape[0] // 2
        upper = (lax.axis_index("row") // distance) % 2 == 1
        low, high = current[:half], current[half:]
        send = jnp.where(upper, low, high).astype(jnp.bfloat16)
        mine = jnp.where(upper, high, low).astype(jnp.bfloat16)
        other = exchange(send, "row", distance)
        current = mine.astype(jnp.float32) + other.astype(jnp.float32)
        kept.append((distance, upper))
    for distance in distances(shape[2]):
        rounded = current.astype(jnp.bfloat16)
        other = exchange(rounded, "col", distance)
        upper = (lax.axis_index("col") // distance) % 2 == 1
        first = jnp.where(upper, other, rounded).astype(jnp.float32)
        second = jnp.where(upper, rounded, other).astype(jnp.float32)
        current = first + second
    current = current.astype(jnp.bfloat16)
    for distance, upper in reversed(kept):
        other = exchange(current, "row", distance)
        current = jnp.where(
            upper, jnp.concatenate([other, current]), jnp.concatenate([current, other])
        )
    return current.astype(jnp.float32).reshape(grads.shape)


def local(checkpoints, kernels, cotangent, plan):
    sections_count, row_count, col_count = sizes()
    section_index = lax.axis_index("section")
    batches, tile_rows, tile_cols, channels = checkpoints.shape[1:]
    layer_count = kernels.shape[0]
    flipped = jnp.transpose(kernels[:, ::-1, ::-1], (0, 1, 2, 4, 3))
    inverse = jnp.sum(
        jnp.arange(batches)[:, None] * (plan[:, None] == jnp.arange(batches)[None, :]), axis=0
    )
    top_cotangent = jnp.take(cotangent, inverse, axis=0)

    deep = layer_count * (sections_count + 1) <= min(tile_rows, tile_cols)
    if deep:
        top_rim = [layer_count * (s + 1) for s in range(sections_count)]
    else:
        top_rim = [layer_count] * sections_count
    rim = top_rim[-1] + layer_count
    both = jnp.concatenate([checkpoints[0], top_cotangent], axis=3)
    both = with_rim(both, rim, 0, range(sections_count))
    first = both[..., :channels]
    top_ext = crop(both[..., channels:], rim - top_rim[-1])
    inputs_list = [first]
    current = first
    for layer_idx in range(layer_count):
        width = rim - layer_idx - 1
        current = jnp.tanh(convolve(current, kernels[layer_idx]))
        current = jnp.where(inside_mask(tile_rows, tile_cols, width), current, 0.0)
        current = current.astype(jnp.bfloat16)
        inputs_list.append(current)

    def backward(top_ext, top_width):
        gradient = top_ext.astype(jnp.float32)
        terms = [None] * layer_count
        for layer_idx in reversed(range(layer_count)):
            width = top_width - (layer_count - 1 - layer_idx)
            output = crop(inputs_list[layer_idx + 1], rim - layer_idx - 1 - width)
            output = output.astype(jnp.float32)
            signal = gradient * (1.0 - output * output)
            signal = jnp.where(inside_mask(tile_rows, tile_cols, width), signal, 0.0)
            signal = signal.astype(jnp.bfloat16)
            terms[layer_idx] = kernel_terms(
                crop(inputs_list[layer_idx], rim - layer_idx - 1), crop(signal, width)
            )
            gradient = convolve(signal, flipped[layer_idx])
        return gradient.astype(jnp.bfloat16), jnp.stack(terms)

    boundary = jnp.zeros((batches, tile_rows, tile_cols, channels), jnp.bfloat16)
    gathered = jnp.zeros((layer_count, 3, 3, channels, channels), jnp.float32)
    for tick in range(sections_count):
        active = sections_count - 1 - tick
        result, terms = backward(top_ext, top_rim[active])
        is_active = section_index == active
        result_width = top_rim[active] - layer_count
        boundary = jnp.where(is_active, crop(result, result_width), boundary)
        if tick + 1 < sections_count:
            if deep:
                pairs = [
                    (flat_index((active, r, c), sizes()), flat_index((active - 1, r, c), sizes()))
                    for r in range(row_count)
                    for c in range(col_count)
                ]
                top_ext = lax.ppermute(result, AXES, pairs)
            else:
                top_ext = with_rim(result, layer_count, 1, (active - 1,))
        gathered = jnp.where(is_active, terms, gathered)
    gathered = summed_over_tiles(gathered)
    kernel_grad = gathered / batches
    return (boundary[None], kernel_grad)


def solution(mesh):
    return jax.shard_map(
        local,
        mesh=mesh,
        in_specs=(
            P("section", None, "row", "col", None),
            P("section", None, None, None, None),
            P(None, "row", "col", None),
            P(),
        ),
        out_specs=(P("section", None, "row", "col", None), P("section", None, None, None, None)),
        check_vma=False,
    )
```

```python
import jax
import jax.numpy as jnp
from jax import lax
from jax.sharding import PartitionSpec as P

AXES = ("section", "row", "col")


def sizes():
    return tuple(lax.axis_size(axis) for axis in AXES)


def flat_index(position, shape):
    section, row, col = position
    return (section * shape[1] + row) * shape[2] + col


def rim_piece(block, width, dr, dc):
    rows, cols = block.shape[1], block.shape[2]
    row_span = {-1: (rows - width, rows), 0: (0, rows), 1: (0, width)}[dr]
    col_span = {-1: (cols - width, cols), 0: (0, cols), 1: (0, width)}[dc]
    return block[:, row_span[0] : row_span[1], col_span[0] : col_span[1]]


def from_neighbours(block, width, dim, from_section, sections_used):
    shape = sizes()
    parts = []
    for step in (-1, 0, 1):
        size = block.shape[dim]
        span = {-1: (size - width, size), 0: (0, size), 1: (0, width)}[step]
        piece = lax.slice_in_dim(block, span[0], span[1], axis=dim)
        if from_section == 0 and step == 0:
            parts.append(piece)
            continue
        pairs = []
        for s in sections_used:
            for r in range(shape[1]):
                for c in range(shape[2]):
                    source = [s + from_section, r, c]
                    source[dim] += step
                    if all(0 <= source[k] < shape[k] for k in range(3)):
                        pairs.append((flat_index(source, shape), flat_index((s, r, c), shape)))
        parts.append(lax.ppermute(piece, AXES, pairs))
    return jnp.concatenate(parts, axis=dim)


def with_rim(block, width, from_section, sections_used):
    rows_done = from_neighbours(block, width, 1, from_section, sections_used)
    return from_neighbours(rows_done, width, 2, 0, sections_used)


def inside_mask(tile_rows, tile_cols, width):
    image_rows = tile_rows * lax.axis_size("row")
    image_cols = tile_cols * lax.axis_size("col")
    rows = lax.axis_index("row") * tile_rows - width + jnp.arange(tile_rows + 2 * width)
    cols = lax.axis_index("col") * tile_cols - width + jnp.arange(tile_cols + 2 * width)
    row_ok = (rows >= 0) & (rows < image_rows)
    col_ok = (cols >= 0) & (cols < image_cols)
    return (row_ok[:, None] & col_ok[None, :])[None, :, :, None]


def convolve(padded, kernel):
    return lax.conv_general_dilated(
        padded,
        kernel,
        (1, 1),
        "VALID",
        dimension_numbers=("NHWC", "HWIO", "NHWC"),
        preferred_element_type=jnp.float32,
    )


def kernel_terms(padded, signal):
    terms = lax.conv_general_dilated(
        padded,
        signal,
        (1, 1),
        "VALID",
        dimension_numbers=("CHWN", "IHWO", "NHWC"),
        preferred_element_type=jnp.float32,
    )
    return jnp.transpose(terms, (1, 2, 0, 3))


def crop(block, width):
    return block[:, width : block.shape[1] - width, width : block.shape[2] - width]


def summed_over_tiles(grads):
    shape = sizes()

    def distances(count):
        found, distance = [], 1
        while distance < count:
            found.append(distance)
            distance *= 2
        return found

    def exchange(values, axis, distance):
        count = lax.axis_size(axis)
        return lax.ppermute(values, axis, [(i, i ^ distance) for i in range(count)])

    current = grads.reshape(-1)
    kept = []
    for distance in distances(shape[1]):
        half = current.shape[0] // 2
        upper = (lax.axis_index("row") // distance) % 2 == 1
        low, high = current[:half], current[half:]
        send = jnp.where(upper, low, high).astype(jnp.bfloat16)
        mine = jnp.where(upper, high, low).astype(jnp.bfloat16)
        other = exchange(send, "row", distance)
        current = mine.astype(jnp.float32) + other.astype(jnp.float32)
        kept.append((distance, upper))
    for distance in distances(shape[2]):
        rounded = current.astype(jnp.bfloat16)
        other = exchange(rounded, "col", distance)
        upper = (lax.axis_index("col") // distance) % 2 == 1
        first = jnp.where(upper, other, rounded).astype(jnp.float32)
        second = jnp.where(upper, rounded, other).astype(jnp.float32)
        current = first + second
    current = current.astype(jnp.bfloat16)
    for distance, upper in reversed(kept):
        other = exchange(current, "row", distance)
        current = jnp.where(
            upper, jnp.concatenate([other, current]), jnp.concatenate([current, other])
        )
    return current.astype(jnp.float32).reshape(grads.shape)


def local(checkpoints, kernels, cotangent, plan):
    sections_count, row_count, col_count = sizes()
    section_index = lax.axis_index("section")
    batches, tile_rows, tile_cols, channels = checkpoints.shape[1:]
    layer_count = kernels.shape[0]
    flipped = jnp.transpose(kernels[:, ::-1, ::-1], (0, 1, 2, 4, 3))
    inverse = jnp.sum(
        jnp.arange(batches)[:, None] * (plan[:, None] == jnp.arange(batches)[None, :]), axis=0
    )
    top_cotangent = jnp.take(cotangent, inverse, axis=0)

    deep = layer_count * (sections_count + 1) <= min(tile_rows, tile_cols)
    if deep:
        top_rim = [layer_count * (s + 1) for s in range(sections_count)]
    else:
        top_rim = [layer_count] * sections_count
    rim = top_rim[-1] + layer_count
    first = with_rim(checkpoints[0], rim, 0, range(sections_count))
    top_ext = with_rim(top_cotangent, top_rim[-1], 0, (sections_count - 1,))
    inputs_list = [first]
    current = first
    for layer_idx in range(layer_count):
        width = rim - layer_idx - 1
        current = jnp.tanh(convolve(current, kernels[layer_idx]))
        current = jnp.where(inside_mask(tile_rows, tile_cols, width), current, 0.0)
        current = current.astype(jnp.bfloat16)
        inputs_list.append(current)

    def backward(top_ext, top_width):
        gradient = top_ext.astype(jnp.float32)
        terms = [None] * layer_count
        for layer_idx in reversed(range(layer_count)):
            width = top_width - (layer_count - 1 - layer_idx)
            output = crop(inputs_list[layer_idx + 1], rim - layer_idx - 1 - width)
            output = output.astype(jnp.float32)
            signal = gradient * (1.0 - output * output)
            signal = jnp.where(inside_mask(tile_rows, tile_cols, width), signal, 0.0)
            signal = signal.astype(jnp.bfloat16)
            terms[layer_idx] = kernel_terms(
                crop(inputs_list[layer_idx], rim - layer_idx - 1), crop(signal, width)
            )
            gradient = convolve(signal, flipped[layer_idx])
        return gradient.astype(jnp.bfloat16), jnp.stack(terms)

    boundary = jnp.zeros((batches, tile_rows, tile_cols, channels), jnp.bfloat16)
    gathered = jnp.zeros((layer_count, 3, 3, channels, channels), jnp.float32)
    for tick in range(sections_count):
        active = sections_count - 1 - tick
        result, terms = backward(top_ext, top_rim[active])
        is_active = section_index == active
        result_width = top_rim[active] - layer_count
        boundary = jnp.where(is_active, crop(result, result_width), boundary)
        if tick + 1 < sections_count:
            if deep:
                pairs = [
                    (flat_index((active, r, c), sizes()), flat_index((active - 1, r, c), sizes()))
                    for r in range(row_count)
                    for c in range(col_count)
                ]
                top_ext = lax.ppermute(result, AXES, pairs)
            else:
                top_ext = with_rim(result, layer_count, 1, (active - 1,))
        gathered = jnp.where(is_active, terms, gathered)
    gathered = summed_over_tiles(gathered)
    kernel_grad = gathered / batches
    return (boundary[None], kernel_grad)


def solution(mesh):
    return jax.shard_map(
        local,
        mesh=mesh,
        in_specs=(
            P("section", None, "row", "col", None),
            P("section", None, None, None, None),
            P(None, "row", "col", None),
            P(),
        ),
        out_specs=(P("section", None, "row", "col", None), P("section", None, None, None, None)),
        check_vma=False,
    )
```

```python
import jax
import jax.numpy as jnp
from jax import lax
from jax.sharding import PartitionSpec as P

AXES = ("section", "row", "col")


def sizes():
    return tuple(lax.axis_size(axis) for axis in AXES)


def flat_index(position, shape):
    section, row, col = position
    return (section * shape[1] + row) * shape[2] + col


def rim_piece(block, width, dr, dc):
    rows, cols = block.shape[1], block.shape[2]
    row_span = {-1: (rows - width, rows), 0: (0, rows), 1: (0, width)}[dr]
    col_span = {-1: (cols - width, cols), 0: (0, cols), 1: (0, width)}[dc]
    return block[:, row_span[0] : row_span[1], col_span[0] : col_span[1]]


def from_neighbours(block, width, dim, from_section, sections_used):
    shape = sizes()
    parts = []
    for step in (-1, 0, 1):
        size = block.shape[dim]
        span = {-1: (size - width, size), 0: (0, size), 1: (0, width)}[step]
        piece = lax.slice_in_dim(block, span[0], span[1], axis=dim)
        if from_section == 0 and step == 0:
            parts.append(piece)
            continue
        pairs = []
        for s in sections_used:
            for r in range(shape[1]):
                for c in range(shape[2]):
                    source = [s + from_section, r, c]
                    source[dim] += step
                    if all(0 <= source[k] < shape[k] for k in range(3)):
                        pairs.append((flat_index(source, shape), flat_index((s, r, c), shape)))
        parts.append(lax.ppermute(piece, AXES, pairs))
    return jnp.concatenate(parts, axis=dim)


def with_rim(block, width, from_section, sections_used):
    rows_done = from_neighbours(block, width, 1, from_section, sections_used)
    return from_neighbours(rows_done, width, 2, 0, sections_used)


def inside_mask(tile_rows, tile_cols, width):
    image_rows = tile_rows * lax.axis_size("row")
    image_cols = tile_cols * lax.axis_size("col")
    rows = lax.axis_index("row") * tile_rows - width + jnp.arange(tile_rows + 2 * width)
    cols = lax.axis_index("col") * tile_cols - width + jnp.arange(tile_cols + 2 * width)
    row_ok = (rows >= 0) & (rows < image_rows)
    col_ok = (cols >= 0) & (cols < image_cols)
    return (row_ok[:, None] & col_ok[None, :])[None, :, :, None]


def convolve(padded, kernel):
    return lax.conv_general_dilated(
        padded,
        kernel,
        (1, 1),
        "VALID",
        dimension_numbers=("NHWC", "HWIO", "NHWC"),
        preferred_element_type=jnp.float32,
    )


def kernel_terms(padded, signal):
    terms = lax.conv_general_dilated(
        padded,
        signal,
        (1, 1),
        "VALID",
        dimension_numbers=("CHWN", "IHWO", "NHWC"),
        preferred_element_type=jnp.float32,
    )
    return jnp.transpose(terms, (1, 2, 0, 3))


def crop(block, width):
    return block[:, width : block.shape[1] - width, width : block.shape[2] - width]


def summed_over_tiles(grads):
    shape = sizes()

    def distances(count):
        found, distance = [], 1
        while distance < count:
            found.append(distance)
            distance *= 2
        return found

    def exchange(values, axis, distance):
        count = lax.axis_size(axis)
        return lax.ppermute(values, axis, [(i, i ^ distance) for i in range(count)])

    current = grads.reshape(-1)
    kept = []
    for distance in distances(shape[1]):
        half = current.shape[0] // 2
        upper = (lax.axis_index("row") // distance) % 2 == 1
        low, high = current[:half], current[half:]
        send = jnp.where(upper, low, high).astype(jnp.bfloat16)
        mine = jnp.where(upper, high, low).astype(jnp.bfloat16)
        other = exchange(send, "row", distance)
        current = mine.astype(jnp.float32) + other.astype(jnp.float32)
        kept.append((distance, upper))
    for distance in distances(shape[2]):
        rounded = current.astype(jnp.bfloat16)
        other = exchange(rounded, "col", distance)
        upper = (lax.axis_index("col") // distance) % 2 == 1
        first = jnp.where(upper, other, rounded).astype(jnp.float32)
        second = jnp.where(upper, rounded, other).astype(jnp.float32)
        current = first + second
    current = current.astype(jnp.bfloat16)
    for distance, upper in reversed(kept):
        other = exchange(current, "row", distance)
        current = jnp.where(
            upper, jnp.concatenate([other, current]), jnp.concatenate([current, other])
        )
    return current.astype(jnp.float32).reshape(grads.shape)


def local(checkpoints, kernels, cotangent, plan):
    sections_count, row_count, col_count = sizes()
    section_index = lax.axis_index("section")
    batches, tile_rows, tile_cols, channels = checkpoints.shape[1:]
    layer_count = kernels.shape[0]
    flipped = jnp.transpose(kernels[:, ::-1, ::-1], (0, 1, 2, 4, 3))
    inverse = jnp.sum(
        jnp.arange(batches)[:, None] * (plan[:, None] == jnp.arange(batches)[None, :]), axis=0
    )
    top_cotangent = jnp.take(cotangent, inverse, axis=0)

    deep = layer_count * (sections_count + 1) <= min(tile_rows, tile_cols)
    if deep:
        top_rim = [layer_count * (s + 1) for s in range(sections_count)]
    else:
        top_rim = [layer_count] * sections_count
    rim = top_rim[-1] + layer_count
    first = with_rim(checkpoints[0], rim, 0, range(sections_count))
    top_ext = with_rim(top_cotangent, top_rim[-1], 0, (sections_count - 1,))
    inputs_list = [first]
    current = first
    for layer_idx in range(layer_count):
        width = rim - layer_idx - 1
        current = jnp.tanh(convolve(current, kernels[layer_idx]))
        current = jnp.where(inside_mask(tile_rows, tile_cols, width), current, 0.0)
        current = current.astype(jnp.bfloat16)
        inputs_list.append(current)

    def backward(top_ext, top_width):
        gradient = top_ext.astype(jnp.float32)
        terms = [None] * layer_count
        for layer_idx in reversed(range(layer_count)):
            width = top_width - (layer_count - 1 - layer_idx)
            output = crop(inputs_list[layer_idx + 1], rim - layer_idx - 1 - width)
            output = output.astype(jnp.float32)
            signal = gradient * (1.0 - output * output)
            signal = jnp.where(inside_mask(tile_rows, tile_cols, width), signal, 0.0)
            signal = signal.astype(jnp.bfloat16)
            terms[layer_idx] = (
                crop(inputs_list[layer_idx], rim - layer_idx - 1),
                crop(signal, width),
            )
            gradient = convolve(signal, flipped[layer_idx])
        return gradient.astype(jnp.bfloat16), terms

    boundary = jnp.zeros((batches, tile_rows, tile_cols, channels), jnp.bfloat16)
    gathered = jnp.zeros((layer_count, 3, 3, channels, channels), jnp.float32)
    for tick in range(sections_count):
        active = sections_count - 1 - tick
        result, term_inputs = backward(top_ext, top_rim[active])
        is_active = section_index == active
        result_width = top_rim[active] - layer_count
        boundary = jnp.where(is_active, crop(result, result_width), boundary)
        if tick + 1 < sections_count:
            if deep:
                pairs = [
                    (flat_index((active, r, c), sizes()), flat_index((active - 1, r, c), sizes()))
                    for r in range(row_count)
                    for c in range(col_count)
                ]
                top_ext = lax.ppermute(result, AXES, pairs)
            else:
                top_ext = with_rim(result, layer_count, 1, (active - 1,))
            top_ext, term_inputs = lax.optimization_barrier((top_ext, term_inputs))
        terms = jnp.stack([kernel_terms(padded, signal) for padded, signal in term_inputs])
        gathered = jnp.where(is_active, terms, gathered)
    gathered = summed_over_tiles(gathered)
    kernel_grad = gathered / batches
    return (boundary[None], kernel_grad)


def solution(mesh):
    return jax.shard_map(
        local,
        mesh=mesh,
        in_specs=(
            P("section", None, "row", "col", None),
            P("section", None, None, None, None),
            P(None, "row", "col", None),
            P(),
        ),
        out_specs=(P("section", None, "row", "col", None), P("section", None, None, None, None)),
        check_vma=False,
    )
```

```python
import jax
import jax.numpy as jnp
from jax import lax
from jax.sharding import PartitionSpec as P

AXES = ("section", "row", "col")


def sizes():
    return tuple(lax.axis_size(axis) for axis in AXES)


def flat_index(position, shape):
    section, row, col = position
    return (section * shape[1] + row) * shape[2] + col


def rim_piece(block, width, dr, dc):
    rows, cols = block.shape[1], block.shape[2]
    row_span = {-1: (rows - width, rows), 0: (0, rows), 1: (0, width)}[dr]
    col_span = {-1: (cols - width, cols), 0: (0, cols), 1: (0, width)}[dc]
    return block[:, row_span[0] : row_span[1], col_span[0] : col_span[1]]


def from_neighbours(block, width, dim, from_section, sections_used):
    shape = sizes()
    parts = []
    for step in (-1, 0, 1):
        size = block.shape[dim]
        span = {-1: (size - width, size), 0: (0, size), 1: (0, width)}[step]
        piece = lax.slice_in_dim(block, span[0], span[1], axis=dim)
        if from_section == 0 and step == 0:
            parts.append(piece)
            continue
        pairs = []
        for s in sections_used:
            for r in range(shape[1]):
                for c in range(shape[2]):
                    source = [s + from_section, r, c]
                    source[dim] += step
                    if all(0 <= source[k] < shape[k] for k in range(3)):
                        pairs.append((flat_index(source, shape), flat_index((s, r, c), shape)))
        parts.append(lax.ppermute(piece, AXES, pairs))
    return jnp.concatenate(parts, axis=dim)


def with_rim(block, width, from_section, sections_used):
    rows_done = from_neighbours(block, width, 1, from_section, sections_used)
    return from_neighbours(rows_done, width, 2, 0, sections_used)


def inside_mask(tile_rows, tile_cols, width):
    image_rows = tile_rows * lax.axis_size("row")
    image_cols = tile_cols * lax.axis_size("col")
    rows = lax.axis_index("row") * tile_rows - width + jnp.arange(tile_rows + 2 * width)
    cols = lax.axis_index("col") * tile_cols - width + jnp.arange(tile_cols + 2 * width)
    row_ok = (rows >= 0) & (rows < image_rows)
    col_ok = (cols >= 0) & (cols < image_cols)
    return (row_ok[:, None] & col_ok[None, :])[None, :, :, None]


def convolve(padded, kernel):
    return lax.conv_general_dilated(
        padded,
        kernel,
        (1, 1),
        "VALID",
        dimension_numbers=("NHWC", "HWIO", "NHWC"),
        preferred_element_type=jnp.float32,
    )


def kernel_terms(padded, signal):
    terms = lax.conv_general_dilated(
        padded,
        signal,
        (1, 1),
        "VALID",
        dimension_numbers=("CHWN", "IHWO", "NHWC"),
        preferred_element_type=jnp.float32,
    )
    return jnp.transpose(terms, (1, 2, 0, 3))


def crop(block, width):
    return block[:, width : block.shape[1] - width, width : block.shape[2] - width]


def summed_over_tiles(grads):
    shape = sizes()

    def distances(count):
        found, distance = [], 1
        while distance < count:
            found.append(distance)
            distance *= 2
        return found

    def exchange(values, axis, distance):
        count = lax.axis_size(axis)
        return lax.ppermute(values, axis, [(i, i ^ distance) for i in range(count)])

    current = grads.reshape(-1)
    kept = []
    for distance in distances(shape[1]):
        half = current.shape[0] // 2
        upper = (lax.axis_index("row") // distance) % 2 == 1
        low, high = current[:half], current[half:]
        send = jnp.where(upper, low, high).astype(jnp.bfloat16)
        mine = jnp.where(upper, high, low).astype(jnp.bfloat16)
        other = exchange(send, "row", distance)
        current = mine.astype(jnp.float32) + other.astype(jnp.float32)
        kept.append((distance, upper))
    for distance in distances(shape[2]):
        rounded = current.astype(jnp.bfloat16)
        other = exchange(rounded, "col", distance)
        upper = (lax.axis_index("col") // distance) % 2 == 1
        first = jnp.where(upper, other, rounded).astype(jnp.float32)
        second = jnp.where(upper, rounded, other).astype(jnp.float32)
        current = first + second
    current = current.astype(jnp.bfloat16)
    for distance, upper in reversed(kept):
        other = exchange(current, "row", distance)
        current = jnp.where(
            upper, jnp.concatenate([other, current]), jnp.concatenate([current, other])
        )
    return current.astype(jnp.float32).reshape(grads.shape)


def local(checkpoints, kernels, cotangent, plan):
    sections_count, row_count, col_count = sizes()
    section_index = lax.axis_index("section")
    batches, tile_rows, tile_cols, channels = checkpoints.shape[1:]
    layer_count = kernels.shape[0]
    flipped = jnp.transpose(kernels[:, ::-1, ::-1], (0, 1, 2, 4, 3))
    inverse = jnp.sum(
        jnp.arange(batches)[:, None] * (plan[:, None] == jnp.arange(batches)[None, :]), axis=0
    )
    top_cotangent = jnp.take(cotangent, inverse, axis=0)

    deep = layer_count * (sections_count + 1) <= min(tile_rows, tile_cols)
    if deep:
        top_rim = [layer_count * (s + 1) for s in range(sections_count)]
    else:
        top_rim = [layer_count] * sections_count
    rim = top_rim[-1] + layer_count
    first = with_rim(checkpoints[0], rim, 0, range(sections_count))
    top_ext = with_rim(top_cotangent, top_rim[-1], 0, (sections_count - 1,))
    inputs_list = [first]
    current = first
    for layer_idx in range(layer_count):
        width = rim - layer_idx - 1
        current = jnp.tanh(convolve(current, kernels[layer_idx]))
        current = jnp.where(inside_mask(tile_rows, tile_cols, width), current, 0.0)
        current = current.astype(jnp.bfloat16)
        inputs_list.append(current)

    def backward(top_ext, top_width):
        gradient = top_ext.astype(jnp.float32)
        terms = [None] * layer_count
        for layer_idx in reversed(range(layer_count)):
            width = top_width - (layer_count - 1 - layer_idx)
            output = crop(inputs_list[layer_idx + 1], rim - layer_idx - 1 - width)
            output = output.astype(jnp.float32)
            signal = gradient * (1.0 - output * output)
            signal = jnp.where(inside_mask(tile_rows, tile_cols, width), signal, 0.0)
            signal = signal.astype(jnp.bfloat16)
            terms[layer_idx] = crop(signal, width)
            gradient = convolve(signal, flipped[layer_idx])
        return gradient.astype(jnp.bfloat16), terms

    def products(signals):
        return jnp.stack(
            [
                kernel_terms(crop(inputs_list[layer_idx], rim - layer_idx - 1), signals[layer_idx])
                for layer_idx in range(layer_count)
            ]
        )

    def nothing_like(*values):
        return lambda *unused: jax.tree.map(lambda v: jnp.zeros(v.shape, v.dtype), values)

    boundary = jnp.zeros((batches, tile_rows, tile_cols, channels), jnp.bfloat16)
    gathered = jnp.zeros((layer_count, 3, 3, channels, channels), jnp.float32)
    for tick in range(sections_count):
        active = sections_count - 1 - tick
        is_active = section_index == active
        skipping = sections_count <= 4
        if skipping:
            shapes = jax.eval_shape(lambda top: backward(top, top_rim[active]), top_ext)
            result, signals = lax.cond(
                is_active,
                lambda top: backward(top, top_rim[active]),
                lambda top: nothing_like(*shapes)(),
                top_ext,
            )
        else:
            result, signals = backward(top_ext, top_rim[active])
        result_width = top_rim[active] - layer_count
        boundary = jnp.where(is_active, crop(result, result_width), boundary)
        if tick + 1 < sections_count:
            if deep:
                pairs = [
                    (flat_index((active, r, c), sizes()), flat_index((active - 1, r, c), sizes()))
                    for r in range(row_count)
                    for c in range(col_count)
                ]
                top_ext = lax.ppermute(result, AXES, pairs)
            else:
                top_ext = with_rim(result, layer_count, 1, (active - 1,))
            top_ext, signals = lax.optimization_barrier((top_ext, signals))
        if skipping:
            terms = lax.cond(
                is_active, products, lambda unused: jnp.zeros_like(gathered), signals
            )
        else:
            terms = products(signals)
        gathered = jnp.where(is_active, terms, gathered)
    gathered = summed_over_tiles(gathered)
    kernel_grad = gathered / batches
    return (boundary[None], kernel_grad)


def solution(mesh):
    return jax.shard_map(
        local,
        mesh=mesh,
        in_specs=(
            P("section", None, "row", "col", None),
            P("section", None, None, None, None),
            P(None, "row", "col", None),
            P(),
        ),
        out_specs=(P("section", None, "row", "col", None), P("section", None, None, None, None)),
        check_vma=False,
    )
```

```python
import jax
import jax.numpy as jnp
from jax import lax
from jax.sharding import PartitionSpec as P

AXES = ("section", "row", "col")


def sizes():
    return tuple(lax.axis_size(axis) for axis in AXES)


def flat_index(position, shape):
    section, row, col = position
    return (section * shape[1] + row) * shape[2] + col


def rim_piece(block, width, dr, dc):
    rows, cols = block.shape[1], block.shape[2]
    row_span = {-1: (rows - width, rows), 0: (0, rows), 1: (0, width)}[dr]
    col_span = {-1: (cols - width, cols), 0: (0, cols), 1: (0, width)}[dc]
    return block[:, row_span[0] : row_span[1], col_span[0] : col_span[1]]


def from_neighbours(block, width, dim, from_section, sections_used):
    shape = sizes()
    parts = []
    for step in (-1, 0, 1):
        size = block.shape[dim]
        span = {-1: (size - width, size), 0: (0, size), 1: (0, width)}[step]
        piece = lax.slice_in_dim(block, span[0], span[1], axis=dim)
        if from_section == 0 and step == 0:
            parts.append(piece)
            continue
        pairs = []
        for s in sections_used:
            for r in range(shape[1]):
                for c in range(shape[2]):
                    source = [s + from_section, r, c]
                    source[dim] += step
                    if all(0 <= source[k] < shape[k] for k in range(3)):
                        pairs.append((flat_index(source, shape), flat_index((s, r, c), shape)))
        parts.append(lax.ppermute(piece, AXES, pairs))
    return jnp.concatenate(parts, axis=dim)


def with_rim(block, width, from_section, sections_used):
    rows_done = from_neighbours(block, width, 1, from_section, sections_used)
    return from_neighbours(rows_done, width, 2, 0, sections_used)


def inside_mask(tile_rows, tile_cols, width):
    image_rows = tile_rows * lax.axis_size("row")
    image_cols = tile_cols * lax.axis_size("col")
    rows = lax.axis_index("row") * tile_rows - width + jnp.arange(tile_rows + 2 * width)
    cols = lax.axis_index("col") * tile_cols - width + jnp.arange(tile_cols + 2 * width)
    row_ok = (rows >= 0) & (rows < image_rows)
    col_ok = (cols >= 0) & (cols < image_cols)
    return (row_ok[:, None] & col_ok[None, :])[None, :, :, None]


def convolve(padded, kernel):
    return lax.conv_general_dilated(
        padded,
        kernel,
        (1, 1),
        "VALID",
        dimension_numbers=("NHWC", "HWIO", "NHWC"),
        preferred_element_type=jnp.float32,
    )


def kernel_terms(padded, signal):
    terms = lax.conv_general_dilated(
        padded,
        signal,
        (1, 1),
        "VALID",
        dimension_numbers=("CHWN", "IHWO", "NHWC"),
        preferred_element_type=jnp.float32,
    )
    return jnp.transpose(terms, (1, 2, 0, 3))


def crop(block, width):
    return block[:, width : block.shape[1] - width, width : block.shape[2] - width]


def summed_over_tiles(grads):
    shape = sizes()

    def distances(count):
        found, distance = [], 1
        while distance < count:
            found.append(distance)
            distance *= 2
        return found

    def exchange(values, axis, distance):
        count = lax.axis_size(axis)
        return lax.ppermute(values, axis, [(i, i ^ distance) for i in range(count)])

    current = grads.reshape(-1)
    kept = []
    for distance in distances(shape[1]):
        half = current.shape[0] // 2
        upper = (lax.axis_index("row") // distance) % 2 == 1
        low, high = current[:half], current[half:]
        send = jnp.where(upper, low, high).astype(jnp.bfloat16)
        mine = jnp.where(upper, high, low).astype(jnp.bfloat16)
        other = exchange(send, "row", distance)
        current = mine.astype(jnp.float32) + other.astype(jnp.float32)
        kept.append((distance, upper))
    for distance in distances(shape[2]):
        rounded = current.astype(jnp.bfloat16)
        other = exchange(rounded, "col", distance)
        upper = (lax.axis_index("col") // distance) % 2 == 1
        first = jnp.where(upper, other, rounded).astype(jnp.float32)
        second = jnp.where(upper, rounded, other).astype(jnp.float32)
        current = first + second
    current = current.astype(jnp.bfloat16)
    for distance, upper in reversed(kept):
        other = exchange(current, "row", distance)
        current = jnp.where(
            upper, jnp.concatenate([other, current]), jnp.concatenate([current, other])
        )
    return current.astype(jnp.float32).reshape(grads.shape)


def local_plain(checkpoints, kernels, cotangent, plan):
    sections_count, row_count, col_count = sizes()
    section_index = lax.axis_index("section")
    batches, tile_rows, tile_cols, channels = checkpoints.shape[1:]
    layer_count = kernels.shape[0]
    flipped = jnp.transpose(kernels[:, ::-1, ::-1], (0, 1, 2, 4, 3))
    inverse = jnp.sum(
        jnp.arange(batches)[:, None] * (plan[:, None] == jnp.arange(batches)[None, :]), axis=0
    )
    top_cotangent = jnp.take(cotangent, inverse, axis=0)

    deep = layer_count * (sections_count + 1) <= min(tile_rows, tile_cols)
    if deep:
        top_rim = [layer_count * (s + 1) for s in range(sections_count)]
    else:
        top_rim = [layer_count] * sections_count
    rim = top_rim[-1] + layer_count
    first = with_rim(checkpoints[0], rim, 0, range(sections_count))
    top_ext = with_rim(top_cotangent, top_rim[-1], 0, (sections_count - 1,))
    inputs_list = [first]
    current = first
    for layer_idx in range(layer_count):
        width = rim - layer_idx - 1
        current = jnp.tanh(convolve(current, kernels[layer_idx]))
        current = jnp.where(inside_mask(tile_rows, tile_cols, width), current, 0.0)
        current = current.astype(jnp.bfloat16)
        inputs_list.append(current)

    def backward(top_ext, top_width):
        gradient = top_ext.astype(jnp.float32)
        terms = [None] * layer_count
        for layer_idx in reversed(range(layer_count)):
            width = top_width - (layer_count - 1 - layer_idx)
            output = crop(inputs_list[layer_idx + 1], rim - layer_idx - 1 - width)
            output = output.astype(jnp.float32)
            signal = gradient * (1.0 - output * output)
            signal = jnp.where(inside_mask(tile_rows, tile_cols, width), signal, 0.0)
            signal = signal.astype(jnp.bfloat16)
            terms[layer_idx] = kernel_terms(
                crop(inputs_list[layer_idx], rim - layer_idx - 1), crop(signal, width)
            )
            gradient = convolve(signal, flipped[layer_idx])
        return gradient.astype(jnp.bfloat16), jnp.stack(terms)

    boundary = jnp.zeros((batches, tile_rows, tile_cols, channels), jnp.bfloat16)
    gathered = jnp.zeros((layer_count, 3, 3, channels, channels), jnp.float32)
    for tick in range(sections_count):
        active = sections_count - 1 - tick
        result, terms = backward(top_ext, top_rim[active])
        is_active = section_index == active
        result_width = top_rim[active] - layer_count
        boundary = jnp.where(is_active, crop(result, result_width), boundary)
        if tick + 1 < sections_count:
            if deep:
                pairs = [
                    (flat_index((active, r, c), sizes()), flat_index((active - 1, r, c), sizes()))
                    for r in range(row_count)
                    for c in range(col_count)
                ]
                top_ext = lax.ppermute(result, AXES, pairs)
            else:
                top_ext = with_rim(result, layer_count, 1, (active - 1,))
        gathered = jnp.where(is_active, terms, gathered)
    gathered = summed_over_tiles(gathered)
    kernel_grad = gathered / batches
    return (boundary[None], kernel_grad)


def packed(block, stride):
    batches, rows, cols, channels = block.shape
    shrink = stride - cols
    block = jnp.pad(block, ((0, 0), (0, 0), (0, shrink), (0, 0)))
    block = jnp.transpose(block, (1, 0, 2, 3)).reshape(1, rows, batches * stride, channels)
    return block[:, :, : batches * stride - shrink]


def unpacked(block, stride, batches):
    _, rows, width, channels = block.shape
    shrink = batches * stride - width
    block = jnp.pad(block, ((0, 0), (0, 0), (0, shrink), (0, 0)))
    block = block.reshape(rows, batches, stride, channels)[:, :, : stride - shrink]
    return jnp.transpose(block, (1, 0, 2, 3))


def packed_crop(block, width):
    return block[:, width : block.shape[1] - width, width : block.shape[2] - width]


def local(checkpoints, kernels, cotangent, plan):
    sections_count, row_count, col_count = sizes()
    section_index = lax.axis_index("section")
    batches, tile_rows, tile_cols, channels = checkpoints.shape[1:]
    layer_count = kernels.shape[0]
    flipped = jnp.transpose(kernels[:, ::-1, ::-1], (0, 1, 2, 4, 3))
    inverse = jnp.sum(
        jnp.arange(batches)[:, None] * (plan[:, None] == jnp.arange(batches)[None, :]), axis=0
    )
    top_cotangent = jnp.take(cotangent, inverse, axis=0)

    deep = layer_count * (sections_count + 1) <= min(tile_rows, tile_cols)
    if not deep:
        return local_plain(checkpoints, kernels, cotangent, plan)
    top_rim = [layer_count * (s + 1) for s in range(sections_count)]
    rim = top_rim[-1] + layer_count
    stride = tile_cols + 2 * rim

    def mask(width):
        image_rows = tile_rows * row_count
        image_cols = tile_cols * col_count
        rows = lax.axis_index("row") * tile_rows - width + jnp.arange(tile_rows + 2 * width)
        within = jnp.arange(batches * stride - 2 * (rim - width)) % stride
        cols = lax.axis_index("col") * tile_cols - width + within
        row_ok = (rows >= 0) & (rows < image_rows)
        col_ok = (cols >= 0) & (cols < image_cols) & (within < tile_cols + 2 * width)
        return (row_ok[:, None] & col_ok[None, :])[None, :, :, None]

    def tile_mask(width):
        within = jnp.arange(batches * stride - 2 * rim) % stride
        return (within < tile_cols)[None, None, :, None]

    first = packed(with_rim(checkpoints[0], rim, 0, range(sections_count)), stride)
    top_ext = with_rim(top_cotangent, top_rim[-1], 0, (sections_count - 1,))
    top_ext = packed(top_ext, stride)
    inputs_list = [first]
    current = first
    for layer_idx in range(layer_count):
        width = rim - layer_idx - 1
        current = jnp.tanh(convolve(current, kernels[layer_idx]))
        current = jnp.where(mask(width), current, 0.0)
        current = current.astype(jnp.bfloat16)
        inputs_list.append(current)

    def backward(top_ext, top_width):
        gradient = top_ext.astype(jnp.float32)
        signals = [None] * layer_count
        for layer_idx in reversed(range(layer_count)):
            width = top_width - (layer_count - 1 - layer_idx)
            output = packed_crop(inputs_list[layer_idx + 1], rim - layer_idx - 1 - width)
            output = output.astype(jnp.float32)
            signal = gradient * (1.0 - output * output)
            signal = jnp.where(mask(width), signal, 0.0)
            signal = signal.astype(jnp.bfloat16)
            signals[layer_idx] = jnp.where(
                tile_mask(width), packed_crop(signal, width), jnp.zeros((), jnp.bfloat16)
            )
            gradient = convolve(signal, flipped[layer_idx])
        return gradient.astype(jnp.bfloat16), signals

    def products(signals):
        return jnp.stack(
            [
                kernel_terms(
                    packed_crop(inputs_list[layer_idx], rim - layer_idx - 1), signals[layer_idx]
                )
                for layer_idx in range(layer_count)
            ]
        )

    boundary = jnp.zeros((batches, tile_rows, tile_cols, channels), jnp.bfloat16)
    gathered = jnp.zeros((layer_count, 3, 3, channels, channels), jnp.float32)
    for tick in range(sections_count):
        active = sections_count - 1 - tick
        is_active = section_index == active
        result, signals = backward(top_ext, top_rim[active])
        result_width = top_rim[active] - layer_count
        back = crop(unpacked(result, stride, batches), result_width)
        boundary = jnp.where(is_active, back, boundary)
        if tick + 1 < sections_count:
            if deep:
                pairs = [
                    (flat_index((active, r, c), sizes()), flat_index((active - 1, r, c), sizes()))
                    for r in range(row_count)
                    for c in range(col_count)
                ]
                top_ext = lax.ppermute(result, AXES, pairs)
            else:
                top_ext = packed(with_rim(back, layer_count, 1, (active - 1,)), stride)
        gathered = jnp.where(is_active, products(signals), gathered)
    gathered = summed_over_tiles(gathered)
    kernel_grad = gathered / batches
    return (boundary[None], kernel_grad)


def solution(mesh):
    return jax.shard_map(
        local,
        mesh=mesh,
        in_specs=(
            P("section", None, "row", "col", None),
            P("section", None, None, None, None),
            P(None, "row", "col", None),
            P(),
        ),
        out_specs=(P("section", None, "row", "col", None), P("section", None, None, None, None)),
        check_vma=False,
    )
```

```python
import jax
import jax.numpy as jnp
from jax import lax
from jax.sharding import PartitionSpec as P

AXES = ("section", "row", "col")


def sizes():
    return tuple(lax.axis_size(axis) for axis in AXES)


def flat_index(position, shape):
    section, row, col = position
    return (section * shape[1] + row) * shape[2] + col


def rim_piece(block, width, dr, dc):
    rows, cols = block.shape[1], block.shape[2]
    row_span = {-1: (rows - width, rows), 0: (0, rows), 1: (0, width)}[dr]
    col_span = {-1: (cols - width, cols), 0: (0, cols), 1: (0, width)}[dc]
    return block[:, row_span[0] : row_span[1], col_span[0] : col_span[1]]


def from_neighbours(block, width, dim, from_section, sections_used):
    shape = sizes()
    parts = []
    for step in (-1, 0, 1):
        size = block.shape[dim]
        span = {-1: (size - width, size), 0: (0, size), 1: (0, width)}[step]
        piece = lax.slice_in_dim(block, span[0], span[1], axis=dim)
        if from_section == 0 and step == 0:
            parts.append(piece)
            continue
        pairs = []
        for s in sections_used:
            for r in range(shape[1]):
                for c in range(shape[2]):
                    source = [s + from_section, r, c]
                    source[dim] += step
                    if all(0 <= source[k] < shape[k] for k in range(3)):
                        pairs.append((flat_index(source, shape), flat_index((s, r, c), shape)))
        parts.append(lax.ppermute(piece, AXES, pairs))
    return jnp.concatenate(parts, axis=dim)


def with_rim(block, width, from_section, sections_used):
    rows_done = from_neighbours(block, width, 1, from_section, sections_used)
    return from_neighbours(rows_done, width, 2, 0, sections_used)


def inside_mask(tile_rows, tile_cols, width):
    image_rows = tile_rows * lax.axis_size("row")
    image_cols = tile_cols * lax.axis_size("col")
    rows = lax.axis_index("row") * tile_rows - width + jnp.arange(tile_rows + 2 * width)
    cols = lax.axis_index("col") * tile_cols - width + jnp.arange(tile_cols + 2 * width)
    row_ok = (rows >= 0) & (rows < image_rows)
    col_ok = (cols >= 0) & (cols < image_cols)
    return (row_ok[:, None] & col_ok[None, :])[None, :, :, None]


def convolve(padded, kernel):
    return lax.conv_general_dilated(
        padded,
        kernel,
        (1, 1),
        "VALID",
        dimension_numbers=("NHWC", "HWIO", "NHWC"),
        preferred_element_type=jnp.float32,
    )


def kernel_terms(padded, signal):
    terms = lax.conv_general_dilated(
        padded,
        signal,
        (1, 1),
        "VALID",
        dimension_numbers=("CHWN", "IHWO", "NHWC"),
        preferred_element_type=jnp.float32,
    )
    return jnp.transpose(terms, (1, 2, 0, 3))


def crop(block, width):
    return block[:, width : block.shape[1] - width, width : block.shape[2] - width]


def summed_over_tiles(grads):
    shape = sizes()

    def distances(count):
        found, distance = [], 1
        while distance < count:
            found.append(distance)
            distance *= 2
        return found

    def exchange(values, axis, distance):
        count = lax.axis_size(axis)
        return lax.ppermute(values, axis, [(i, i ^ distance) for i in range(count)])

    current = grads.reshape(-1)
    kept = []
    for distance in distances(shape[1]):
        half = current.shape[0] // 2
        upper = (lax.axis_index("row") // distance) % 2 == 1
        low, high = current[:half], current[half:]
        send = jnp.where(upper, low, high).astype(jnp.bfloat16)
        mine = jnp.where(upper, high, low).astype(jnp.bfloat16)
        other = exchange(send, "row", distance)
        current = mine.astype(jnp.float32) + other.astype(jnp.float32)
        kept.append((distance, upper))
    for distance in distances(shape[2]):
        rounded = current.astype(jnp.bfloat16)
        other = exchange(rounded, "col", distance)
        upper = (lax.axis_index("col") // distance) % 2 == 1
        first = jnp.where(upper, other, rounded).astype(jnp.float32)
        second = jnp.where(upper, rounded, other).astype(jnp.float32)
        current = first + second
    current = current.astype(jnp.bfloat16)
    for distance, upper in reversed(kept):
        other = exchange(current, "row", distance)
        current = jnp.where(
            upper, jnp.concatenate([other, current]), jnp.concatenate([current, other])
        )
    return current.astype(jnp.float32).reshape(grads.shape)


def local(checkpoints, kernels, cotangent, plan):
    sections_count, row_count, col_count = sizes()
    section_index = lax.axis_index("section")
    batches, tile_rows, tile_cols, channels = checkpoints.shape[1:]
    layer_count = kernels.shape[0]
    flipped = jnp.transpose(kernels[:, ::-1, ::-1], (0, 1, 2, 4, 3))
    inverse = jnp.sum(
        jnp.arange(batches)[:, None] * (plan[:, None] == jnp.arange(batches)[None, :]), axis=0
    )
    top_cotangent = jnp.take(cotangent, inverse, axis=0)

    deep = layer_count * (sections_count + 1) <= min(tile_rows, tile_cols)
    if deep:
        top_rim = [layer_count * (s + 1) for s in range(sections_count)]
    else:
        top_rim = [layer_count] * sections_count
    rim = top_rim[-1] + layer_count
    first = with_rim(checkpoints[0], rim, 0, range(sections_count))
    top_ext = with_rim(top_cotangent, top_rim[-1], 0, (sections_count - 1,))
    inputs_list = [first]
    current = first
    for layer_idx in range(layer_count):
        width = rim - layer_idx - 1
        current = jnp.tanh(convolve(current, kernels[layer_idx]))
        current = jnp.where(inside_mask(tile_rows, tile_cols, width), current, 0.0)
        current = current.astype(jnp.bfloat16)
        inputs_list.append(current)

    def backward(top_ext, top_width):
        gradient = top_ext.astype(jnp.float32)
        terms = [None] * layer_count
        for layer_idx in reversed(range(layer_count)):
            width = top_width - (layer_count - 1 - layer_idx)
            output = crop(inputs_list[layer_idx + 1], rim - layer_idx - 1 - width)
            output = output.astype(jnp.float32)
            signal = gradient * (1.0 - output * output)
            signal = jnp.where(inside_mask(tile_rows, tile_cols, width), signal, 0.0)
            signal = signal.astype(jnp.bfloat16)
            terms[layer_idx] = crop(signal, width)
            gradient = convolve(signal, flipped[layer_idx])
        return gradient.astype(jnp.bfloat16), terms

    def products(signals):
        return jnp.stack(
            [
                kernel_terms(crop(inputs_list[layer_idx], rim - layer_idx - 1), signals[layer_idx])
                for layer_idx in range(layer_count)
            ]
        )

    boundary = jnp.zeros((batches, tile_rows, tile_cols, channels), jnp.bfloat16)
    gathered = jnp.zeros((layer_count, 3, 3, channels, channels), jnp.float32)
    for tick in range(sections_count):
        active = sections_count - 1 - tick
        is_active = section_index == active
        if tick + 1 < sections_count or sections_count > 4:
            result, signals = backward(top_ext, top_rim[active])
        else:
            shapes = jax.eval_shape(lambda top: backward(top, top_rim[active]), top_ext)
            result, signals = lax.cond(
                is_active,
                lambda top: backward(top, top_rim[active]),
                lambda top: jax.tree.map(lambda v: jnp.zeros(v.shape, v.dtype), shapes),
                top_ext,
            )
        result_width = top_rim[active] - layer_count
        boundary = jnp.where(is_active, crop(result, result_width), boundary)
        if tick + 1 < sections_count:
            if deep:
                pairs = [
                    (flat_index((active, r, c), sizes()), flat_index((active - 1, r, c), sizes()))
                    for r in range(row_count)
                    for c in range(col_count)
                ]
                top_ext = lax.ppermute(result, AXES, pairs)
            else:
                top_ext = with_rim(result, layer_count, 1, (active - 1,))
        if sections_count > 4:
            terms = products(signals)
        else:
            terms = lax.cond(
                is_active, products, lambda unused: jnp.zeros_like(gathered), signals
            )
        gathered = jnp.where(is_active, terms, gathered)
    gathered = summed_over_tiles(gathered)
    kernel_grad = gathered / batches
    return (boundary[None], kernel_grad)


def solution(mesh):
    return jax.shard_map(
        local,
        mesh=mesh,
        in_specs=(
            P("section", None, "row", "col", None),
            P("section", None, None, None, None),
            P(None, "row", "col", None),
            P(),
        ),
        out_specs=(P("section", None, "row", "col", None), P("section", None, None, None, None)),
        check_vma=False,
    )
```

```python
import jax
import jax.numpy as jnp
from jax import lax
from jax.sharding import PartitionSpec as P

AXES = ("section", "row", "col")


def sizes():
    return tuple(lax.axis_size(axis) for axis in AXES)


def flat_index(position, shape):
    section, row, col = position
    return (section * shape[1] + row) * shape[2] + col


def rim_piece(block, width, dr, dc):
    rows, cols = block.shape[1], block.shape[2]
    row_span = {-1: (rows - width, rows), 0: (0, rows), 1: (0, width)}[dr]
    col_span = {-1: (cols - width, cols), 0: (0, cols), 1: (0, width)}[dc]
    return block[:, row_span[0] : row_span[1], col_span[0] : col_span[1]]


def from_neighbours(block, width, dim, from_section, sections_used):
    shape = sizes()
    parts = []
    for step in (-1, 0, 1):
        size = block.shape[dim]
        span = {-1: (size - width, size), 0: (0, size), 1: (0, width)}[step]
        piece = lax.slice_in_dim(block, span[0], span[1], axis=dim)
        if from_section == 0 and step == 0:
            parts.append(piece)
            continue
        pairs = []
        for s in sections_used:
            for r in range(shape[1]):
                for c in range(shape[2]):
                    source = [s + from_section, r, c]
                    source[dim] += step
                    if all(0 <= source[k] < shape[k] for k in range(3)):
                        pairs.append((flat_index(source, shape), flat_index((s, r, c), shape)))
        parts.append(lax.ppermute(piece, AXES, pairs))
    return jnp.concatenate(parts, axis=dim)


def with_rim(block, width, from_section, sections_used):
    rows_done = from_neighbours(block, width, 1, from_section, sections_used)
    return from_neighbours(rows_done, width, 2, 0, sections_used)


def with_rim_at_once(block, width, sections_used):
    shape = sizes()
    bands = []
    for dr in (-1, 0, 1):
        band = []
        for dc in (-1, 0, 1):
            rows, cols = block.shape[1], block.shape[2]
            row_span = {-1: (rows - width, rows), 0: (0, rows), 1: (0, width)}[dr]
            col_span = {-1: (cols - width, cols), 0: (0, cols), 1: (0, width)}[dc]
            piece = block[:, row_span[0] : row_span[1], col_span[0] : col_span[1]]
            if dr == 0 and dc == 0:
                band.append(piece)
                continue
            pairs = []
            for s in sections_used:
                for r in range(shape[1]):
                    for c in range(shape[2]):
                        source = (s, r + dr, c + dc)
                        if 0 <= source[1] < shape[1] and 0 <= source[2] < shape[2]:
                            pairs.append((flat_index(source, shape), flat_index((s, r, c), shape)))
            band.append(lax.ppermute(piece, AXES, pairs))
        bands.append(jnp.concatenate(band, axis=2))
    return jnp.concatenate(bands, axis=1)


def inside_mask(tile_rows, tile_cols, width):
    image_rows = tile_rows * lax.axis_size("row")
    image_cols = tile_cols * lax.axis_size("col")
    rows = lax.axis_index("row") * tile_rows - width + jnp.arange(tile_rows + 2 * width)
    cols = lax.axis_index("col") * tile_cols - width + jnp.arange(tile_cols + 2 * width)
    row_ok = (rows >= 0) & (rows < image_rows)
    col_ok = (cols >= 0) & (cols < image_cols)
    return (row_ok[:, None] & col_ok[None, :])[None, :, :, None]


def convolve(padded, kernel):
    return lax.conv_general_dilated(
        padded,
        kernel,
        (1, 1),
        "VALID",
        dimension_numbers=("NHWC", "HWIO", "NHWC"),
        preferred_element_type=jnp.float32,
    )


def kernel_terms(padded, signal):
    terms = lax.conv_general_dilated(
        padded,
        signal,
        (1, 1),
        "VALID",
        dimension_numbers=("CHWN", "IHWO", "NHWC"),
        preferred_element_type=jnp.float32,
    )
    return jnp.transpose(terms, (1, 2, 0, 3))


def crop(block, width):
    return block[:, width : block.shape[1] - width, width : block.shape[2] - width]


def summed_over_tiles(grads):
    shape = sizes()

    def distances(count):
        found, distance = [], 1
        while distance < count:
            found.append(distance)
            distance *= 2
        return found

    def exchange(values, axis, distance):
        count = lax.axis_size(axis)
        return lax.ppermute(values, axis, [(i, i ^ distance) for i in range(count)])

    current = grads.reshape(-1)
    kept = []
    for distance in distances(shape[1]):
        half = current.shape[0] // 2
        upper = (lax.axis_index("row") // distance) % 2 == 1
        low, high = current[:half], current[half:]
        send = jnp.where(upper, low, high).astype(jnp.bfloat16)
        mine = jnp.where(upper, high, low).astype(jnp.bfloat16)
        other = exchange(send, "row", distance)
        current = mine.astype(jnp.float32) + other.astype(jnp.float32)
        kept.append((distance, upper))
    for distance in distances(shape[2]):
        rounded = current.astype(jnp.bfloat16)
        other = exchange(rounded, "col", distance)
        upper = (lax.axis_index("col") // distance) % 2 == 1
        first = jnp.where(upper, other, rounded).astype(jnp.float32)
        second = jnp.where(upper, rounded, other).astype(jnp.float32)
        current = first + second
    current = current.astype(jnp.bfloat16)
    for distance, upper in reversed(kept):
        other = exchange(current, "row", distance)
        current = jnp.where(
            upper, jnp.concatenate([other, current]), jnp.concatenate([current, other])
        )
    return current.astype(jnp.float32).reshape(grads.shape)


def local(checkpoints, kernels, cotangent, plan):
    sections_count, row_count, col_count = sizes()
    section_index = lax.axis_index("section")
    batches, tile_rows, tile_cols, channels = checkpoints.shape[1:]
    layer_count = kernels.shape[0]
    flipped = jnp.transpose(kernels[:, ::-1, ::-1], (0, 1, 2, 4, 3))
    inverse = jnp.sum(
        jnp.arange(batches)[:, None] * (plan[:, None] == jnp.arange(batches)[None, :]), axis=0
    )
    top_cotangent = jnp.take(cotangent, inverse, axis=0)

    deep = layer_count * (sections_count + 1) <= min(tile_rows, tile_cols)
    if deep:
        top_rim = [layer_count * (s + 1) for s in range(sections_count)]
    else:
        top_rim = [layer_count] * sections_count
    rim = top_rim[-1] + layer_count
    first = with_rim_at_once(checkpoints[0], rim, range(sections_count))
    top_ext = with_rim(top_cotangent, top_rim[-1], 0, (sections_count - 1,))
    inputs_list = [first]
    current = first
    for layer_idx in range(layer_count):
        width = rim - layer_idx - 1
        current = jnp.tanh(convolve(current, kernels[layer_idx]))
        current = jnp.where(inside_mask(tile_rows, tile_cols, width), current, 0.0)
        current = current.astype(jnp.bfloat16)
        inputs_list.append(current)

    def backward(top_ext, top_width):
        gradient = top_ext.astype(jnp.float32)
        terms = [None] * layer_count
        for layer_idx in reversed(range(layer_count)):
            width = top_width - (layer_count - 1 - layer_idx)
            output = crop(inputs_list[layer_idx + 1], rim - layer_idx - 1 - width)
            output = output.astype(jnp.float32)
            signal = gradient * (1.0 - output * output)
            signal = jnp.where(inside_mask(tile_rows, tile_cols, width), signal, 0.0)
            signal = signal.astype(jnp.bfloat16)
            terms[layer_idx] = crop(signal, width)
            gradient = convolve(signal, flipped[layer_idx])
        return gradient.astype(jnp.bfloat16), terms

    def products(signals):
        return jnp.stack(
            [
                kernel_terms(crop(inputs_list[layer_idx], rim - layer_idx - 1), signals[layer_idx])
                for layer_idx in range(layer_count)
            ]
        )

    boundary = jnp.zeros((batches, tile_rows, tile_cols, channels), jnp.bfloat16)
    gathered = jnp.zeros((layer_count, 3, 3, channels, channels), jnp.float32)
    for tick in range(sections_count):
        active = sections_count - 1 - tick
        is_active = section_index == active
        if tick + 1 < sections_count or sections_count > 4:
            result, signals = backward(top_ext, top_rim[active])
        else:
            shapes = jax.eval_shape(lambda top: backward(top, top_rim[active]), top_ext)
            result, signals = lax.cond(
                is_active,
                lambda top: backward(top, top_rim[active]),
                lambda top: jax.tree.map(lambda v: jnp.zeros(v.shape, v.dtype), shapes),
                top_ext,
            )
        result_width = top_rim[active] - layer_count
        boundary = jnp.where(is_active, crop(result, result_width), boundary)
        if tick + 1 < sections_count:
            if deep:
                pairs = [
                    (flat_index((active, r, c), sizes()), flat_index((active - 1, r, c), sizes()))
                    for r in range(row_count)
                    for c in range(col_count)
                ]
                top_ext = lax.ppermute(result, AXES, pairs)
            else:
                top_ext = with_rim(result, layer_count, 1, (active - 1,))
        if sections_count > 4:
            terms = products(signals)
        else:
            terms = lax.cond(
                is_active, products, lambda unused: jnp.zeros_like(gathered), signals
            )
        gathered = jnp.where(is_active, terms, gathered)
    gathered = summed_over_tiles(gathered)
    kernel_grad = gathered / batches
    return (boundary[None], kernel_grad)


def solution(mesh):
    return jax.shard_map(
        local,
        mesh=mesh,
        in_specs=(
            P("section", None, "row", "col", None),
            P("section", None, None, None, None),
            P(None, "row", "col", None),
            P(),
        ),
        out_specs=(P("section", None, "row", "col", None), P("section", None, None, None, None)),
        check_vma=False,
    )
```

```python
import jax
import jax.numpy as jnp
from jax import lax
from jax.sharding import PartitionSpec as P

AXES = ("section", "row", "col")


def sizes():
    return tuple(lax.axis_size(axis) for axis in AXES)


def flat_index(position, shape):
    section, row, col = position
    return (section * shape[1] + row) * shape[2] + col


def rim_piece(block, width, dr, dc):
    rows, cols = block.shape[1], block.shape[2]
    row_span = {-1: (rows - width, rows), 0: (0, rows), 1: (0, width)}[dr]
    col_span = {-1: (cols - width, cols), 0: (0, cols), 1: (0, width)}[dc]
    return block[:, row_span[0] : row_span[1], col_span[0] : col_span[1]]


def from_neighbours(block, width, dim, from_section, sections_used):
    shape = sizes()
    parts = []
    for step in (-1, 0, 1):
        size = block.shape[dim]
        span = {-1: (size - width, size), 0: (0, size), 1: (0, width)}[step]
        piece = lax.slice_in_dim(block, span[0], span[1], axis=dim)
        if from_section == 0 and step == 0:
            parts.append(piece)
            continue
        pairs = []
        for s in sections_used:
            for r in range(shape[1]):
                for c in range(shape[2]):
                    source = [s + from_section, r, c]
                    source[dim] += step
                    if all(0 <= source[k] < shape[k] for k in range(3)):
                        pairs.append((flat_index(source, shape), flat_index((s, r, c), shape)))
        parts.append(lax.ppermute(piece, AXES, pairs))
    return jnp.concatenate(parts, axis=dim)


def with_rim(block, width, from_section, sections_used):
    rows_done = from_neighbours(block, width, 1, from_section, sections_used)
    return from_neighbours(rows_done, width, 2, 0, sections_used)


def inside_mask(tile_rows, tile_cols, width):
    image_rows = tile_rows * lax.axis_size("row")
    image_cols = tile_cols * lax.axis_size("col")
    rows = lax.axis_index("row") * tile_rows - width + jnp.arange(tile_rows + 2 * width)
    cols = lax.axis_index("col") * tile_cols - width + jnp.arange(tile_cols + 2 * width)
    row_ok = (rows >= 0) & (rows < image_rows)
    col_ok = (cols >= 0) & (cols < image_cols)
    return (row_ok[:, None] & col_ok[None, :])[None, :, :, None]


def convolve(padded, kernel):
    return lax.conv_general_dilated(
        padded,
        kernel,
        (1, 1),
        "VALID",
        dimension_numbers=("NHWC", "HWIO", "NHWC"),
        preferred_element_type=jnp.float32,
    )


def kernel_terms(padded, signal):
    terms = lax.conv_general_dilated(
        padded,
        signal,
        (1, 1),
        "VALID",
        dimension_numbers=("CHWN", "IHWO", "NHWC"),
        preferred_element_type=jnp.float32,
    )
    return jnp.transpose(terms, (1, 2, 0, 3))


def crop(block, width):
    return block[:, width : block.shape[1] - width, width : block.shape[2] - width]


def summed_over_tiles(grads):
    shape = sizes()

    def distances(count):
        found, distance = [], 1
        while distance < count:
            found.append(distance)
            distance *= 2
        return found

    def exchange(values, axis, distance):
        count = lax.axis_size(axis)
        return lax.ppermute(values, axis, [(i, i ^ distance) for i in range(count)])

    current = grads.reshape(-1)
    kept = []
    for distance in distances(shape[1]):
        half = current.shape[0] // 2
        upper = (lax.axis_index("row") // distance) % 2 == 1
        low, high = current[:half], current[half:]
        send = jnp.where(upper, low, high).astype(jnp.bfloat16)
        mine = jnp.where(upper, high, low).astype(jnp.bfloat16)
        other = exchange(send, "row", distance)
        current = mine.astype(jnp.float32) + other.astype(jnp.float32)
        kept.append((distance, upper))
    for distance in distances(shape[2]):
        rounded = current.astype(jnp.bfloat16)
        other = exchange(rounded, "col", distance)
        upper = (lax.axis_index("col") // distance) % 2 == 1
        first = jnp.where(upper, other, rounded).astype(jnp.float32)
        second = jnp.where(upper, rounded, other).astype(jnp.float32)
        current = first + second
    current = current.astype(jnp.bfloat16)
    for distance, upper in reversed(kept):
        other = exchange(current, "row", distance)
        current = jnp.where(
            upper, jnp.concatenate([other, current]), jnp.concatenate([current, other])
        )
    return current.astype(jnp.float32).reshape(grads.shape)


def local(checkpoints, kernels, cotangent, plan):
    sections_count, row_count, col_count = sizes()
    section_index = lax.axis_index("section")
    batches, tile_rows, tile_cols, channels = checkpoints.shape[1:]
    layer_count = kernels.shape[0]
    flipped = jnp.transpose(kernels[:, ::-1, ::-1], (0, 1, 2, 4, 3))
    inverse = jnp.sum(
        jnp.arange(batches)[:, None] * (plan[:, None] == jnp.arange(batches)[None, :]), axis=0
    )
    top_cotangent = jnp.take(cotangent, inverse, axis=0)

    deep = layer_count * (sections_count + 1) <= min(tile_rows, tile_cols)
    if deep and sections_count == 2 and batches % 2 == 0:
        return local_split(checkpoints, kernels, cotangent, plan)
    if deep:
        top_rim = [layer_count * (s + 1) for s in range(sections_count)]
    else:
        top_rim = [layer_count] * sections_count
    rim = top_rim[-1] + layer_count
    first = with_rim(checkpoints[0], rim, 0, range(sections_count))
    top_ext = with_rim(top_cotangent, top_rim[-1], 0, (sections_count - 1,))
    inputs_list = [first]
    current = first
    for layer_idx in range(layer_count):
        width = rim - layer_idx - 1
        current = jnp.tanh(convolve(current, kernels[layer_idx]))
        current = jnp.where(inside_mask(tile_rows, tile_cols, width), current, 0.0)
        current = current.astype(jnp.bfloat16)
        inputs_list.append(current)

    def backward(top_ext, top_width):
        gradient = top_ext.astype(jnp.float32)
        terms = [None] * layer_count
        for layer_idx in reversed(range(layer_count)):
            width = top_width - (layer_count - 1 - layer_idx)
            output = crop(inputs_list[layer_idx + 1], rim - layer_idx - 1 - width)
            output = output.astype(jnp.float32)
            signal = gradient * (1.0 - output * output)
            signal = jnp.where(inside_mask(tile_rows, tile_cols, width), signal, 0.0)
            signal = signal.astype(jnp.bfloat16)
            terms[layer_idx] = crop(signal, width)
            gradient = convolve(signal, flipped[layer_idx])
        return gradient.astype(jnp.bfloat16), terms

    def products(signals):
        return jnp.stack(
            [
                kernel_terms(crop(inputs_list[layer_idx], rim - layer_idx - 1), signals[layer_idx])
                for layer_idx in range(layer_count)
            ]
        )

    boundary = jnp.zeros((batches, tile_rows, tile_cols, channels), jnp.bfloat16)
    gathered = jnp.zeros((layer_count, 3, 3, channels, channels), jnp.float32)
    for tick in range(sections_count):
        active = sections_count - 1 - tick
        is_active = section_index == active
        if tick + 1 < sections_count or sections_count > 4:
            result, signals = backward(top_ext, top_rim[active])
        else:
            shapes = jax.eval_shape(lambda top: backward(top, top_rim[active]), top_ext)
            result, signals = lax.cond(
                is_active,
                lambda top: backward(top, top_rim[active]),
                lambda top: jax.tree.map(lambda v: jnp.zeros(v.shape, v.dtype), shapes),
                top_ext,
            )
        result_width = top_rim[active] - layer_count
        boundary = jnp.where(is_active, crop(result, result_width), boundary)
        if tick + 1 < sections_count:
            if deep:
                pairs = [
                    (flat_index((active, r, c), sizes()), flat_index((active - 1, r, c), sizes()))
                    for r in range(row_count)
                    for c in range(col_count)
                ]
                top_ext = lax.ppermute(result, AXES, pairs)
            else:
                top_ext = with_rim(result, layer_count, 1, (active - 1,))
        if sections_count > 4:
            terms = products(signals)
        else:
            terms = lax.cond(
                is_active, products, lambda unused: jnp.zeros_like(gathered), signals
            )
        gathered = jnp.where(is_active, terms, gathered)
    gathered = summed_over_tiles(gathered)
    kernel_grad = gathered / batches
    return (boundary[None], kernel_grad)


def section_chain(top_ext, top_width, inputs_list, rim, flipped_kernels):
    layer_count = len(flipped_kernels)
    tile_rows = inputs_list[0].shape[1] - 2 * rim
    tile_cols = inputs_list[0].shape[2] - 2 * rim
    gradient = top_ext.astype(jnp.float32)
    signals = [None] * layer_count
    for layer_idx in reversed(range(layer_count)):
        width = top_width - (layer_count - 1 - layer_idx)
        output = crop(inputs_list[layer_idx + 1], rim - layer_idx - 1 - width)
        output = output.astype(jnp.float32)
        signal = gradient * (1.0 - output * output)
        signal = jnp.where(inside_mask(tile_rows, tile_cols, width), signal, 0.0)
        signal = signal.astype(jnp.bfloat16)
        signals[layer_idx] = crop(signal, width)
        gradient = convolve(signal, flipped_kernels[layer_idx])
    return gradient.astype(jnp.bfloat16), signals


def local_split(checkpoints, kernels, cotangent, plan):
    section_index = lax.axis_index("section")
    batches, tile_rows, tile_cols, channels = checkpoints.shape[1:]
    layer_count = kernels.shape[0]
    half = batches // 2
    inverse = jnp.sum(
        jnp.arange(batches)[:, None] * (plan[:, None] == jnp.arange(batches)[None, :]), axis=0
    )
    top_cotangent = jnp.take(cotangent, inverse, axis=0)

    def swap(values):
        return lax.ppermute(values, "section", [(0, 1), (1, 0)])

    def by_section(mine, theirs, section):
        return jnp.where(section_index == section, mine, theirs)

    own = checkpoints[0]
    mine = lax.dynamic_slice_in_dim(own, section_index * half, half, 0)
    theirs = swap(lax.dynamic_slice_in_dim(own, (1 - section_index) * half, half, 0))
    other_kernels = swap(kernels)
    section_kernels = [by_section(kernels, other_kernels, s) for s in range(2)]

    top_rim = [layer_count * (s + 1) for s in range(2)]
    rims = [r + layer_count for r in top_rim]
    stacked = jnp.concatenate([by_section(mine, theirs, s) for s in range(2)], axis=0)
    stacked = with_rim(stacked, rims[1], 0, range(2))
    firsts = [crop(stacked[:half], rims[1] - rims[0]), stacked[half:]]
    group_cotangent = lax.dynamic_slice_in_dim(top_cotangent, section_index * half, half, 0)
    top_ext = with_rim(group_cotangent, top_rim[1], 0, range(2))

    results, partials = [None, None], [None, None]
    for s in (1, 0):
        rim = rims[s]
        inputs_list = [firsts[s]]
        current = firsts[s]
        for layer_idx in range(layer_count):
            current = jnp.tanh(convolve(current, section_kernels[s][layer_idx]))
            current = jnp.where(
                inside_mask(tile_rows, tile_cols, rim - layer_idx - 1), current, 0.0
            )
            current = current.astype(jnp.bfloat16)
            inputs_list.append(current)
        flipped = jnp.transpose(section_kernels[s][:, ::-1, ::-1], (0, 1, 2, 4, 3))
        top_ext, signals = section_chain(top_ext, top_rim[s], inputs_list, rim, flipped)
        results[s] = crop(top_ext, top_rim[s] - layer_count)
        partials[s] = jnp.stack(
            [
                kernel_terms(crop(inputs_list[layer_idx], rim - layer_idx - 1), signals[layer_idx])
                for layer_idx in range(layer_count)
            ]
        )

    mine_terms = by_section(partials[0], partials[1], 0)
    other_terms = by_section(partials[1], partials[0], 0)
    gathered = summed_over_tiles(mine_terms + swap(other_terms))
    mine_back = by_section(results[0], results[1], 0)
    other_back = swap(by_section(results[1], results[0], 0))
    boundary = jnp.where(
        section_index == 0,
        jnp.concatenate([mine_back, other_back], axis=0),
        jnp.concatenate([other_back, mine_back], axis=0),
    )
    return (boundary[None], gathered / batches)


def solution(mesh):
    return jax.shard_map(
        local,
        mesh=mesh,
        in_specs=(
            P("section", None, "row", "col", None),
            P("section", None, None, None, None),
            P(None, "row", "col", None),
            P(),
        ),
        out_specs=(P("section", None, "row", "col", None), P("section", None, None, None, None)),
        check_vma=False,
    )
```

```python
import jax
import jax.numpy as jnp
from jax import lax
from jax.sharding import PartitionSpec as P

AXES = ("section", "row", "col")


def sizes():
    return tuple(lax.axis_size(axis) for axis in AXES)


def flat_index(position, shape):
    section, row, col = position
    return (section * shape[1] + row) * shape[2] + col


def rim_piece(block, width, dr, dc):
    rows, cols = block.shape[1], block.shape[2]
    row_span = {-1: (rows - width, rows), 0: (0, rows), 1: (0, width)}[dr]
    col_span = {-1: (cols - width, cols), 0: (0, cols), 1: (0, width)}[dc]
    return block[:, row_span[0] : row_span[1], col_span[0] : col_span[1]]


def from_neighbours(block, width, dim, from_section, sections_used):
    shape = sizes()
    parts = []
    for step in (-1, 0, 1):
        size = block.shape[dim]
        span = {-1: (size - width, size), 0: (0, size), 1: (0, width)}[step]
        piece = lax.slice_in_dim(block, span[0], span[1], axis=dim)
        if from_section == 0 and step == 0:
            parts.append(piece)
            continue
        pairs = []
        for s in sections_used:
            for r in range(shape[1]):
                for c in range(shape[2]):
                    source = [s + from_section, r, c]
                    source[dim] += step
                    if all(0 <= source[k] < shape[k] for k in range(3)):
                        pairs.append((flat_index(source, shape), flat_index((s, r, c), shape)))
        parts.append(lax.ppermute(piece, AXES, pairs))
    return jnp.concatenate(parts, axis=dim)


def with_rim(block, width, from_section, sections_used):
    rows_done = from_neighbours(block, width, 1, from_section, sections_used)
    return from_neighbours(rows_done, width, 2, 0, sections_used)


def inside_mask(tile_rows, tile_cols, width):
    image_rows = tile_rows * lax.axis_size("row")
    image_cols = tile_cols * lax.axis_size("col")
    rows = lax.axis_index("row") * tile_rows - width + jnp.arange(tile_rows + 2 * width)
    cols = lax.axis_index("col") * tile_cols - width + jnp.arange(tile_cols + 2 * width)
    row_ok = (rows >= 0) & (rows < image_rows)
    col_ok = (cols >= 0) & (cols < image_cols)
    return (row_ok[:, None] & col_ok[None, :])[None, :, :, None]


def convolve(padded, kernel):
    return lax.conv_general_dilated(
        padded,
        kernel,
        (1, 1),
        "VALID",
        dimension_numbers=("NHWC", "HWIO", "NHWC"),
        preferred_element_type=jnp.float32,
    )


def kernel_terms(padded, signal):
    terms = lax.conv_general_dilated(
        padded,
        signal,
        (1, 1),
        "VALID",
        dimension_numbers=("CHWN", "IHWO", "NHWC"),
        preferred_element_type=jnp.float32,
    )
    return jnp.transpose(terms, (1, 2, 0, 3))


def crop(block, width):
    return block[:, width : block.shape[1] - width, width : block.shape[2] - width]


def summed_over_tiles(grads):
    shape = sizes()

    def distances(count):
        found, distance = [], 1
        while distance < count:
            found.append(distance)
            distance *= 2
        return found

    def exchange(values, axis, distance):
        count = lax.axis_size(axis)
        return lax.ppermute(values, axis, [(i, i ^ distance) for i in range(count)])

    current = grads.reshape(-1)
    kept = []
    for distance in distances(shape[1]):
        half = current.shape[0] // 2
        upper = (lax.axis_index("row") // distance) % 2 == 1
        low, high = current[:half], current[half:]
        send = jnp.where(upper, low, high).astype(jnp.bfloat16)
        mine = jnp.where(upper, high, low).astype(jnp.bfloat16)
        other = exchange(send, "row", distance)
        current = mine.astype(jnp.float32) + other.astype(jnp.float32)
        kept.append((distance, upper))
    for distance in distances(shape[2]):
        rounded = current.astype(jnp.bfloat16)
        other = exchange(rounded, "col", distance)
        upper = (lax.axis_index("col") // distance) % 2 == 1
        first = jnp.where(upper, other, rounded).astype(jnp.float32)
        second = jnp.where(upper, rounded, other).astype(jnp.float32)
        current = first + second
    current = current.astype(jnp.bfloat16)
    for distance, upper in reversed(kept):
        other = exchange(current, "row", distance)
        current = jnp.where(
            upper, jnp.concatenate([other, current]), jnp.concatenate([current, other])
        )
    return current.astype(jnp.float32).reshape(grads.shape)


def local(checkpoints, kernels, cotangent, plan):
    sections_count, row_count, col_count = sizes()
    section_index = lax.axis_index("section")
    batches, tile_rows, tile_cols, channels = checkpoints.shape[1:]
    layer_count = kernels.shape[0]
    flipped = jnp.transpose(kernels[:, ::-1, ::-1], (0, 1, 2, 4, 3))
    inverse = jnp.sum(
        jnp.arange(batches)[:, None] * (plan[:, None] == jnp.arange(batches)[None, :]), axis=0
    )
    top_cotangent = jnp.take(cotangent, inverse, axis=0)

    deep = layer_count * (sections_count + 1) <= min(tile_rows, tile_cols)
    if deep and sections_count == 2 and batches % 2 == 0:
        return local_split(checkpoints, kernels, cotangent, plan)
    if deep:
        top_rim = [layer_count * (s + 1) for s in range(sections_count)]
    else:
        top_rim = [layer_count] * sections_count
    rim = top_rim[-1] + layer_count
    first = with_rim(checkpoints[0], rim, 0, range(sections_count))
    top_ext = with_rim(top_cotangent, top_rim[-1], 0, (sections_count - 1,))
    inputs_list = [first]
    current = first
    for layer_idx in range(layer_count):
        width = rim - layer_idx - 1
        current = jnp.tanh(convolve(current, kernels[layer_idx]))
        current = jnp.where(inside_mask(tile_rows, tile_cols, width), current, 0.0)
        current = current.astype(jnp.bfloat16)
        inputs_list.append(current)

    def backward(top_ext, top_width):
        gradient = top_ext.astype(jnp.float32)
        terms = [None] * layer_count
        for layer_idx in reversed(range(layer_count)):
            width = top_width - (layer_count - 1 - layer_idx)
            output = crop(inputs_list[layer_idx + 1], rim - layer_idx - 1 - width)
            output = output.astype(jnp.float32)
            signal = gradient * (1.0 - output * output)
            signal = jnp.where(inside_mask(tile_rows, tile_cols, width), signal, 0.0)
            signal = signal.astype(jnp.bfloat16)
            terms[layer_idx] = crop(signal, width)
            gradient = convolve(signal, flipped[layer_idx])
        return gradient.astype(jnp.bfloat16), terms

    def products(signals):
        return jnp.stack(
            [
                kernel_terms(crop(inputs_list[layer_idx], rim - layer_idx - 1), signals[layer_idx])
                for layer_idx in range(layer_count)
            ]
        )

    boundary = jnp.zeros((batches, tile_rows, tile_cols, channels), jnp.bfloat16)
    gathered = jnp.zeros((layer_count, 3, 3, channels, channels), jnp.float32)
    for tick in range(sections_count):
        active = sections_count - 1 - tick
        is_active = section_index == active
        if tick + 1 < sections_count or sections_count > 4:
            result, signals = backward(top_ext, top_rim[active])
        else:
            shapes = jax.eval_shape(lambda top: backward(top, top_rim[active]), top_ext)
            result, signals = lax.cond(
                is_active,
                lambda top: backward(top, top_rim[active]),
                lambda top: jax.tree.map(lambda v: jnp.zeros(v.shape, v.dtype), shapes),
                top_ext,
            )
        result_width = top_rim[active] - layer_count
        boundary = jnp.where(is_active, crop(result, result_width), boundary)
        if tick + 1 < sections_count:
            if deep:
                pairs = [
                    (flat_index((active, r, c), sizes()), flat_index((active - 1, r, c), sizes()))
                    for r in range(row_count)
                    for c in range(col_count)
                ]
                top_ext = lax.ppermute(result, AXES, pairs)
            else:
                top_ext = with_rim(result, layer_count, 1, (active - 1,))
        if sections_count > 4:
            terms = products(signals)
        else:
            terms = lax.cond(
                is_active, products, lambda unused: jnp.zeros_like(gathered), signals
            )
        gathered = jnp.where(is_active, terms, gathered)
    gathered = summed_over_tiles(gathered)
    kernel_grad = gathered / batches
    return (boundary[None], kernel_grad)


def section_chain(top_ext, top_width, inputs_list, rim, flipped_kernels):
    layer_count = len(flipped_kernels)
    tile_rows = inputs_list[0].shape[1] - 2 * rim
    tile_cols = inputs_list[0].shape[2] - 2 * rim
    gradient = top_ext.astype(jnp.float32)
    signals = [None] * layer_count
    for layer_idx in reversed(range(layer_count)):
        width = top_width - (layer_count - 1 - layer_idx)
        output = crop(inputs_list[layer_idx + 1], rim - layer_idx - 1 - width)
        output = output.astype(jnp.float32)
        signal = gradient * (1.0 - output * output)
        signal = jnp.where(inside_mask(tile_rows, tile_cols, width), signal, 0.0)
        signal = lax.optimization_barrier(signal.astype(jnp.bfloat16))
        signals[layer_idx] = crop(signal, width)
        gradient = convolve(signal, flipped_kernels[layer_idx])
    return gradient.astype(jnp.bfloat16), signals


def local_split(checkpoints, kernels, cotangent, plan):
    section_index = lax.axis_index("section")
    batches, tile_rows, tile_cols, channels = checkpoints.shape[1:]
    layer_count = kernels.shape[0]
    half = batches // 2
    inverse = jnp.sum(
        jnp.arange(batches)[:, None] * (plan[:, None] == jnp.arange(batches)[None, :]), axis=0
    )
    top_cotangent = jnp.take(cotangent, inverse, axis=0)

    def swap(values):
        return lax.ppermute(values, "section", [(0, 1), (1, 0)])

    def by_section(mine, theirs, section):
        return jnp.where(section_index == section, mine, theirs)

    own = checkpoints[0]
    mine = lax.dynamic_slice_in_dim(own, section_index * half, half, 0)
    theirs = swap(lax.dynamic_slice_in_dim(own, (1 - section_index) * half, half, 0))
    other_kernels = swap(kernels)
    section_kernels = [by_section(kernels, other_kernels, s) for s in range(2)]

    top_rim = [layer_count * (s + 1) for s in range(2)]
    rims = [r + layer_count for r in top_rim]
    stacked = jnp.concatenate([by_section(mine, theirs, s) for s in range(2)], axis=0)
    stacked = with_rim(stacked, rims[1], 0, range(2))
    firsts = [crop(stacked[:half], rims[1] - rims[0]), stacked[half:]]
    group_cotangent = lax.dynamic_slice_in_dim(top_cotangent, section_index * half, half, 0)
    top_ext = with_rim(group_cotangent, top_rim[1], 0, range(2))

    results, partials = [None, None], [None, None]
    for s in (1, 0):
        rim = rims[s]
        inputs_list = [firsts[s]]
        current = firsts[s]
        for layer_idx in range(layer_count):
            current = jnp.tanh(convolve(current, section_kernels[s][layer_idx]))
            current = jnp.where(
                inside_mask(tile_rows, tile_cols, rim - layer_idx - 1), current, 0.0
            )
            current = lax.optimization_barrier(current.astype(jnp.bfloat16))
            inputs_list.append(current)
        flipped = jnp.transpose(section_kernels[s][:, ::-1, ::-1], (0, 1, 2, 4, 3))
        top_ext, signals = section_chain(top_ext, top_rim[s], inputs_list, rim, flipped)
        results[s] = crop(top_ext, top_rim[s] - layer_count)
        partials[s] = jnp.stack(
            [
                kernel_terms(crop(inputs_list[layer_idx], rim - layer_idx - 1), signals[layer_idx])
                for layer_idx in range(layer_count)
            ]
        )

    mine_terms = by_section(partials[0], partials[1], 0)
    other_terms = by_section(partials[1], partials[0], 0)
    gathered = summed_over_tiles(mine_terms + swap(other_terms))
    mine_back = by_section(results[0], results[1], 0)
    other_back = swap(by_section(results[1], results[0], 0))
    boundary = jnp.where(
        section_index == 0,
        jnp.concatenate([mine_back, other_back], axis=0),
        jnp.concatenate([other_back, mine_back], axis=0),
    )
    return (boundary[None], gathered / batches)


def solution(mesh):
    return jax.shard_map(
        local,
        mesh=mesh,
        in_specs=(
            P("section", None, "row", "col", None),
            P("section", None, None, None, None),
            P(None, "row", "col", None),
            P(),
        ),
        out_specs=(P("section", None, "row", "col", None), P("section", None, None, None, None)),
        check_vma=False,
    )
```

```python
import jax
import jax.numpy as jnp
from jax import lax
from jax.sharding import PartitionSpec as P

AXES = ("section", "row", "col")


def sizes():
    return tuple(lax.axis_size(axis) for axis in AXES)


def flat_index(position, shape):
    section, row, col = position
    return (section * shape[1] + row) * shape[2] + col


def rim_piece(block, width, dr, dc):
    rows, cols = block.shape[1], block.shape[2]
    row_span = {-1: (rows - width, rows), 0: (0, rows), 1: (0, width)}[dr]
    col_span = {-1: (cols - width, cols), 0: (0, cols), 1: (0, width)}[dc]
    return block[:, row_span[0] : row_span[1], col_span[0] : col_span[1]]


def from_neighbours(block, width, dim, from_section, sections_used):
    shape = sizes()
    parts = []
    for step in (-1, 0, 1):
        size = block.shape[dim]
        span = {-1: (size - width, size), 0: (0, size), 1: (0, width)}[step]
        piece = lax.slice_in_dim(block, span[0], span[1], axis=dim)
        if from_section == 0 and step == 0:
            parts.append(piece)
            continue
        pairs = []
        for s in sections_used:
            for r in range(shape[1]):
                for c in range(shape[2]):
                    source = [s + from_section, r, c]
                    source[dim] += step
                    if all(0 <= source[k] < shape[k] for k in range(3)):
                        pairs.append((flat_index(source, shape), flat_index((s, r, c), shape)))
        parts.append(lax.ppermute(piece, AXES, pairs))
    return jnp.concatenate(parts, axis=dim)


def with_rim(block, width, from_section, sections_used):
    rows_done = from_neighbours(block, width, 1, from_section, sections_used)
    return from_neighbours(rows_done, width, 2, 0, sections_used)


def inside_mask(tile_rows, tile_cols, width):
    image_rows = tile_rows * lax.axis_size("row")
    image_cols = tile_cols * lax.axis_size("col")
    rows = lax.axis_index("row") * tile_rows - width + jnp.arange(tile_rows + 2 * width)
    cols = lax.axis_index("col") * tile_cols - width + jnp.arange(tile_cols + 2 * width)
    row_ok = (rows >= 0) & (rows < image_rows)
    col_ok = (cols >= 0) & (cols < image_cols)
    return (row_ok[:, None] & col_ok[None, :])[None, :, :, None]


def convolve(padded, kernel):
    return lax.conv_general_dilated(
        padded,
        kernel,
        (1, 1),
        "VALID",
        dimension_numbers=("NHWC", "HWIO", "NHWC"),
        preferred_element_type=jnp.float32,
    )


def kernel_terms(padded, signal):
    terms = lax.conv_general_dilated(
        padded,
        signal,
        (1, 1),
        "VALID",
        dimension_numbers=("CHWN", "IHWO", "NHWC"),
        preferred_element_type=jnp.float32,
    )
    return jnp.transpose(terms, (1, 2, 0, 3))


def crop(block, width):
    return block[:, width : block.shape[1] - width, width : block.shape[2] - width]


def summed_over_tiles(grads):
    shape = sizes()

    def distances(count):
        found, distance = [], 1
        while distance < count:
            found.append(distance)
            distance *= 2
        return found

    def exchange(values, axis, distance):
        count = lax.axis_size(axis)
        return lax.ppermute(values, axis, [(i, i ^ distance) for i in range(count)])

    current = grads.reshape(-1)
    kept = []
    for distance in distances(shape[1]):
        half = current.shape[0] // 2
        upper = (lax.axis_index("row") // distance) % 2 == 1
        low, high = current[:half], current[half:]
        send = jnp.where(upper, low, high).astype(jnp.bfloat16)
        mine = jnp.where(upper, high, low).astype(jnp.bfloat16)
        other = exchange(send, "row", distance)
        current = mine.astype(jnp.float32) + other.astype(jnp.float32)
        kept.append((distance, upper))
    for distance in distances(shape[2]):
        rounded = current.astype(jnp.bfloat16)
        other = exchange(rounded, "col", distance)
        upper = (lax.axis_index("col") // distance) % 2 == 1
        first = jnp.where(upper, other, rounded).astype(jnp.float32)
        second = jnp.where(upper, rounded, other).astype(jnp.float32)
        current = first + second
    current = current.astype(jnp.bfloat16)
    for distance, upper in reversed(kept):
        other = exchange(current, "row", distance)
        current = jnp.where(
            upper, jnp.concatenate([other, current]), jnp.concatenate([current, other])
        )
    return current.astype(jnp.float32).reshape(grads.shape)


def local(checkpoints, kernels, cotangent, plan):
    sections_count, row_count, col_count = sizes()
    section_index = lax.axis_index("section")
    batches, tile_rows, tile_cols, channels = checkpoints.shape[1:]
    layer_count = kernels.shape[0]
    flipped = jnp.transpose(kernels[:, ::-1, ::-1], (0, 1, 2, 4, 3))
    inverse = jnp.sum(
        jnp.arange(batches)[:, None] * (plan[:, None] == jnp.arange(batches)[None, :]), axis=0
    )
    top_cotangent = jnp.take(cotangent, inverse, axis=0)

    deep = layer_count * (sections_count + 1) <= min(tile_rows, tile_cols)
    if deep and sections_count == 2 and batches % 2 == 0:
        return local_split(checkpoints, kernels, cotangent, plan)
    if deep:
        top_rim = [layer_count * (s + 1) for s in range(sections_count)]
    else:
        top_rim = [layer_count] * sections_count
    rim = top_rim[-1] + layer_count
    first = with_rim(checkpoints[0], rim, 0, range(sections_count))
    top_ext = with_rim(top_cotangent, top_rim[-1], 0, (sections_count - 1,))
    inputs_list = [first]
    current = first
    for layer_idx in range(layer_count):
        width = rim - layer_idx - 1
        current = jnp.tanh(convolve(current, kernels[layer_idx]))
        current = jnp.where(inside_mask(tile_rows, tile_cols, width), current, 0.0)
        current = current.astype(jnp.bfloat16)
        inputs_list.append(current)

    def backward(top_ext, top_width):
        gradient = top_ext.astype(jnp.float32)
        terms = [None] * layer_count
        for layer_idx in reversed(range(layer_count)):
            width = top_width - (layer_count - 1 - layer_idx)
            output = crop(inputs_list[layer_idx + 1], rim - layer_idx - 1 - width)
            output = output.astype(jnp.float32)
            signal = gradient * (1.0 - output * output)
            signal = jnp.where(inside_mask(tile_rows, tile_cols, width), signal, 0.0)
            signal = signal.astype(jnp.bfloat16)
            terms[layer_idx] = crop(signal, width)
            gradient = convolve(signal, flipped[layer_idx])
        return gradient.astype(jnp.bfloat16), terms

    def products(signals):
        return jnp.stack(
            [
                kernel_terms(crop(inputs_list[layer_idx], rim - layer_idx - 1), signals[layer_idx])
                for layer_idx in range(layer_count)
            ]
        )

    boundary = jnp.zeros((batches, tile_rows, tile_cols, channels), jnp.bfloat16)
    gathered = jnp.zeros((layer_count, 3, 3, channels, channels), jnp.float32)
    for tick in range(sections_count):
        active = sections_count - 1 - tick
        is_active = section_index == active
        if tick + 1 < sections_count or sections_count > 4:
            result, signals = backward(top_ext, top_rim[active])
        else:
            shapes = jax.eval_shape(lambda top: backward(top, top_rim[active]), top_ext)
            result, signals = lax.cond(
                is_active,
                lambda top: backward(top, top_rim[active]),
                lambda top: jax.tree.map(lambda v: jnp.zeros(v.shape, v.dtype), shapes),
                top_ext,
            )
        result_width = top_rim[active] - layer_count
        boundary = jnp.where(is_active, crop(result, result_width), boundary)
        if tick + 1 < sections_count:
            if deep:
                pairs = [
                    (flat_index((active, r, c), sizes()), flat_index((active - 1, r, c), sizes()))
                    for r in range(row_count)
                    for c in range(col_count)
                ]
                top_ext = lax.ppermute(result, AXES, pairs)
            else:
                top_ext = with_rim(result, layer_count, 1, (active - 1,))
        if sections_count > 4:
            terms = products(signals)
        else:
            terms = lax.cond(
                is_active, products, lambda unused: jnp.zeros_like(gathered), signals
            )
        gathered = jnp.where(is_active, terms, gathered)
    gathered = summed_over_tiles(gathered)
    kernel_grad = gathered / batches
    return (boundary[None], kernel_grad)


def section_chain(top_ext, top_width, inputs_list, rim, flipped_kernels):
    layer_count = len(flipped_kernels)
    tile_rows = inputs_list[0].shape[1] - 2 * rim
    tile_cols = inputs_list[0].shape[2] - 2 * rim
    gradient = top_ext.astype(jnp.float32)
    signals = [None] * layer_count
    for layer_idx in reversed(range(layer_count)):
        width = top_width - (layer_count - 1 - layer_idx)
        output = crop(inputs_list[layer_idx + 1], rim - layer_idx - 1 - width)
        output = output.astype(jnp.float32)
        signal = gradient * (1.0 - output * output)
        signal = jnp.where(inside_mask(tile_rows, tile_cols, width), signal, 0.0)
        signal = signal.astype(jnp.bfloat16)
        signals[layer_idx] = crop(signal, width)
        gradient = convolve(signal, flipped_kernels[layer_idx])
    return gradient.astype(jnp.bfloat16), signals


def local_split(checkpoints, kernels, cotangent, plan):
    section_index = lax.axis_index("section")
    batches, tile_rows, tile_cols, channels = checkpoints.shape[1:]
    layer_count = kernels.shape[0]
    half = batches // 2
    inverse = jnp.sum(
        jnp.arange(batches)[:, None] * (plan[:, None] == jnp.arange(batches)[None, :]), axis=0
    )
    top_cotangent = jnp.take(cotangent, inverse, axis=0)

    def swap(values):
        return lax.ppermute(values, "section", [(0, 1), (1, 0)])

    def by_section(mine, theirs, section):
        return jnp.where(section_index == section, mine, theirs)

    own = checkpoints[0]
    mine = lax.dynamic_slice_in_dim(own, section_index * half, half, 0)
    theirs = swap(lax.dynamic_slice_in_dim(own, (1 - section_index) * half, half, 0))
    other_kernels = swap(kernels)
    section_kernels = [by_section(kernels, other_kernels, s) for s in range(2)]

    top_rim = [layer_count * (s + 1) for s in range(2)]
    rims = [r + layer_count for r in top_rim]
    stacked = jnp.concatenate([by_section(mine, theirs, s) for s in range(2)], axis=0)
    stacked = with_rim(stacked, rims[1], 0, range(2))
    group_cotangent = lax.dynamic_slice_in_dim(top_cotangent, section_index * half, half, 0)
    stacked, group_cotangent = lax.optimization_barrier((stacked, group_cotangent))
    top_ext = with_rim(group_cotangent, top_rim[1], 0, range(2))
    firsts = [crop(stacked[:half], rims[1] - rims[0]), stacked[half:]]

    results, partials = [None, None], [None, None]
    for s in (1, 0):
        rim = rims[s]
        inputs_list = [firsts[s]]
        current = firsts[s]
        for layer_idx in range(layer_count):
            current = jnp.tanh(convolve(current, section_kernels[s][layer_idx]))
            current = jnp.where(
                inside_mask(tile_rows, tile_cols, rim - layer_idx - 1), current, 0.0
            )
            current = current.astype(jnp.bfloat16)
            inputs_list.append(current)
        flipped = jnp.transpose(section_kernels[s][:, ::-1, ::-1], (0, 1, 2, 4, 3))
        top_ext, signals = section_chain(top_ext, top_rim[s], inputs_list, rim, flipped)
        results[s] = crop(top_ext, top_rim[s] - layer_count)
        partials[s] = jnp.stack(
            [
                kernel_terms(crop(inputs_list[layer_idx], rim - layer_idx - 1), signals[layer_idx])
                for layer_idx in range(layer_count)
            ]
        )

    mine_terms = by_section(partials[0], partials[1], 0)
    other_terms = by_section(partials[1], partials[0], 0)
    gathered = summed_over_tiles(mine_terms + swap(other_terms))
    mine_back = by_section(results[0], results[1], 0)
    other_back = swap(by_section(results[1], results[0], 0))
    boundary = jnp.where(
        section_index == 0,
        jnp.concatenate([mine_back, other_back], axis=0),
        jnp.concatenate([other_back, mine_back], axis=0),
    )
    return (boundary[None], gathered / batches)


def solution(mesh):
    return jax.shard_map(
        local,
        mesh=mesh,
        in_specs=(
            P("section", None, "row", "col", None),
            P("section", None, None, None, None),
            P(None, "row", "col", None),
            P(),
        ),
        out_specs=(P("section", None, "row", "col", None), P("section", None, None, None, None)),
        check_vma=False,
    )
```

```python
import jax
import jax.numpy as jnp
from jax import lax
from jax.sharding import PartitionSpec as P

AXES = ("section", "row", "col")


def sizes():
    return tuple(lax.axis_size(axis) for axis in AXES)


def flat_index(position, shape):
    section, row, col = position
    return (section * shape[1] + row) * shape[2] + col


def rim_piece(block, width, dr, dc):
    rows, cols = block.shape[1], block.shape[2]
    row_span = {-1: (rows - width, rows), 0: (0, rows), 1: (0, width)}[dr]
    col_span = {-1: (cols - width, cols), 0: (0, cols), 1: (0, width)}[dc]
    return block[:, row_span[0] : row_span[1], col_span[0] : col_span[1]]


def from_neighbours(block, width, dim, from_section, sections_used):
    shape = sizes()
    parts = []
    for step in (-1, 0, 1):
        size = block.shape[dim]
        span = {-1: (size - width, size), 0: (0, size), 1: (0, width)}[step]
        piece = lax.slice_in_dim(block, span[0], span[1], axis=dim)
        if from_section == 0 and step == 0:
            parts.append(piece)
            continue
        pairs = []
        for s in sections_used:
            for r in range(shape[1]):
                for c in range(shape[2]):
                    source = [s + from_section, r, c]
                    source[dim] += step
                    if all(0 <= source[k] < shape[k] for k in range(3)):
                        pairs.append((flat_index(source, shape), flat_index((s, r, c), shape)))
        parts.append(lax.ppermute(piece, AXES, pairs))
    return jnp.concatenate(parts, axis=dim)


def with_rim(block, width, from_section, sections_used):
    rows_done = from_neighbours(block, width, 1, from_section, sections_used)
    return from_neighbours(rows_done, width, 2, 0, sections_used)


def inside_mask(tile_rows, tile_cols, width):
    image_rows = tile_rows * lax.axis_size("row")
    image_cols = tile_cols * lax.axis_size("col")
    rows = lax.axis_index("row") * tile_rows - width + jnp.arange(tile_rows + 2 * width)
    cols = lax.axis_index("col") * tile_cols - width + jnp.arange(tile_cols + 2 * width)
    row_ok = (rows >= 0) & (rows < image_rows)
    col_ok = (cols >= 0) & (cols < image_cols)
    return (row_ok[:, None] & col_ok[None, :])[None, :, :, None]


def convolve(padded, kernel):
    return lax.conv_general_dilated(
        padded,
        kernel,
        (1, 1),
        "VALID",
        dimension_numbers=("NHWC", "HWIO", "NHWC"),
        preferred_element_type=jnp.float32,
    )


def kernel_terms(padded, signal):
    terms = lax.conv_general_dilated(
        padded,
        signal,
        (1, 1),
        "VALID",
        dimension_numbers=("CHWN", "IHWO", "NHWC"),
        preferred_element_type=jnp.float32,
    )
    return jnp.transpose(terms, (1, 2, 0, 3))


def crop(block, width):
    return block[:, width : block.shape[1] - width, width : block.shape[2] - width]


def summed_over_tiles(grads):
    shape = sizes()

    def distances(count):
        found, distance = [], 1
        while distance < count:
            found.append(distance)
            distance *= 2
        return found

    def exchange(values, axis, distance):
        count = lax.axis_size(axis)
        return lax.ppermute(values, axis, [(i, i ^ distance) for i in range(count)])

    current = grads.reshape(-1)
    kept = []
    for distance in distances(shape[1]):
        half = current.shape[0] // 2
        upper = (lax.axis_index("row") // distance) % 2 == 1
        low, high = current[:half], current[half:]
        send = jnp.where(upper, low, high).astype(jnp.bfloat16)
        mine = jnp.where(upper, high, low).astype(jnp.bfloat16)
        other = exchange(send, "row", distance)
        current = mine.astype(jnp.float32) + other.astype(jnp.float32)
        kept.append((distance, upper))
    for distance in distances(shape[2]):
        rounded = current.astype(jnp.bfloat16)
        other = exchange(rounded, "col", distance)
        upper = (lax.axis_index("col") // distance) % 2 == 1
        first = jnp.where(upper, other, rounded).astype(jnp.float32)
        second = jnp.where(upper, rounded, other).astype(jnp.float32)
        current = first + second
    current = current.astype(jnp.bfloat16)
    for distance, upper in reversed(kept):
        other = exchange(current, "row", distance)
        current = jnp.where(
            upper, jnp.concatenate([other, current]), jnp.concatenate([current, other])
        )
    return current.astype(jnp.float32).reshape(grads.shape)


def local(checkpoints, kernels, cotangent, plan):
    sections_count, row_count, col_count = sizes()
    section_index = lax.axis_index("section")
    batches, tile_rows, tile_cols, channels = checkpoints.shape[1:]
    layer_count = kernels.shape[0]
    flipped = jnp.transpose(kernels[:, ::-1, ::-1], (0, 1, 2, 4, 3))
    inverse = jnp.sum(
        jnp.arange(batches)[:, None] * (plan[:, None] == jnp.arange(batches)[None, :]), axis=0
    )
    top_cotangent = jnp.take(cotangent, inverse, axis=0)

    deep = layer_count * (sections_count + 1) <= min(tile_rows, tile_cols)
    if deep and sections_count == 2 and batches % 2 == 0:
        return local_split(checkpoints, kernels, cotangent, plan)
    if deep:
        top_rim = [layer_count * (s + 1) for s in range(sections_count)]
    else:
        top_rim = [layer_count] * sections_count
    rim = top_rim[-1] + layer_count
    first = with_rim(checkpoints[0], rim, 0, range(sections_count))
    top_ext = with_rim(top_cotangent, top_rim[-1], 0, (sections_count - 1,))
    inputs_list = [first]
    current = first
    for layer_idx in range(layer_count):
        width = rim - layer_idx - 1
        current = jnp.tanh(convolve(current, kernels[layer_idx]))
        current = jnp.where(inside_mask(tile_rows, tile_cols, width), current, 0.0)
        current = current.astype(jnp.bfloat16)
        inputs_list.append(current)

    def backward(top_ext, top_width):
        gradient = top_ext.astype(jnp.float32)
        terms = [None] * layer_count
        for layer_idx in reversed(range(layer_count)):
            width = top_width - (layer_count - 1 - layer_idx)
            output = crop(inputs_list[layer_idx + 1], rim - layer_idx - 1 - width)
            output = output.astype(jnp.float32)
            signal = gradient * (1.0 - output * output)
            signal = jnp.where(inside_mask(tile_rows, tile_cols, width), signal, 0.0)
            signal = signal.astype(jnp.bfloat16)
            terms[layer_idx] = crop(signal, width)
            gradient = convolve(signal, flipped[layer_idx])
        return gradient.astype(jnp.bfloat16), terms

    def products(signals):
        return jnp.stack(
            [
                kernel_terms(crop(inputs_list[layer_idx], rim - layer_idx - 1), signals[layer_idx])
                for layer_idx in range(layer_count)
            ]
        )

    boundary = jnp.zeros((batches, tile_rows, tile_cols, channels), jnp.bfloat16)
    gathered = jnp.zeros((layer_count, 3, 3, channels, channels), jnp.float32)
    for tick in range(sections_count):
        active = sections_count - 1 - tick
        is_active = section_index == active
        if tick + 1 < sections_count or sections_count > 4:
            result, signals = backward(top_ext, top_rim[active])
        else:
            shapes = jax.eval_shape(lambda top: backward(top, top_rim[active]), top_ext)
            result, signals = lax.cond(
                is_active,
                lambda top: backward(top, top_rim[active]),
                lambda top: jax.tree.map(lambda v: jnp.zeros(v.shape, v.dtype), shapes),
                top_ext,
            )
        result_width = top_rim[active] - layer_count
        boundary = jnp.where(is_active, crop(result, result_width), boundary)
        if tick + 1 < sections_count:
            if deep:
                pairs = [
                    (flat_index((active, r, c), sizes()), flat_index((active - 1, r, c), sizes()))
                    for r in range(row_count)
                    for c in range(col_count)
                ]
                top_ext = lax.ppermute(result, AXES, pairs)
            else:
                top_ext = with_rim(result, layer_count, 1, (active - 1,))
        if sections_count > 4:
            terms = products(signals)
        else:
            terms = lax.cond(
                is_active, products, lambda unused: jnp.zeros_like(gathered), signals
            )
        gathered = jnp.where(is_active, terms, gathered)
    gathered = summed_over_tiles(gathered)
    kernel_grad = gathered / batches
    return (boundary[None], kernel_grad)


def section_chain(top_ext, top_width, inputs_list, rim, flipped_kernels):
    layer_count = len(flipped_kernels)
    tile_rows = inputs_list[0].shape[1] - 2 * rim
    tile_cols = inputs_list[0].shape[2] - 2 * rim
    gradient = top_ext.astype(jnp.float32)
    signals = [None] * layer_count
    for layer_idx in reversed(range(layer_count)):
        width = top_width - (layer_count - 1 - layer_idx)
        output = crop(inputs_list[layer_idx + 1], rim - layer_idx - 1 - width)
        output = output.astype(jnp.float32)
        signal = gradient * (1.0 - output * output)
        signal = jnp.where(inside_mask(tile_rows, tile_cols, width), signal, 0.0)
        signal = signal.astype(jnp.bfloat16)
        signals[layer_idx] = crop(signal, width)
        gradient = convolve(signal, flipped_kernels[layer_idx])
    return gradient.astype(jnp.bfloat16), signals


def local_split(checkpoints, kernels, cotangent, plan):
    section_index = lax.axis_index("section")
    batches, tile_rows, tile_cols, channels = checkpoints.shape[1:]
    layer_count = kernels.shape[0]
    half = batches // 2
    inverse = jnp.sum(
        jnp.arange(batches)[:, None] * (plan[:, None] == jnp.arange(batches)[None, :]), axis=0
    )
    top_cotangent = jnp.take(cotangent, inverse, axis=0)

    def swap(values):
        return lax.ppermute(values, "section", [(0, 1), (1, 0)])

    def by_section(mine, theirs, section):
        return jnp.where(section_index == section, mine, theirs)

    own = checkpoints[0]
    mine = lax.dynamic_slice_in_dim(own, section_index * half, half, 0)
    theirs = swap(lax.dynamic_slice_in_dim(own, (1 - section_index) * half, half, 0))
    other_kernels = swap(kernels)
    section_kernels = [by_section(kernels, other_kernels, s) for s in range(2)]

    top_rim = [layer_count * (s + 1) for s in range(2)]
    rims = [r + layer_count for r in top_rim]
    group_cotangent = lax.dynamic_slice_in_dim(top_cotangent, section_index * half, half, 0)
    stacked = [by_section(mine, theirs, s) for s in range(2)] + [group_cotangent]
    stacked = with_rim(jnp.concatenate(stacked, axis=0), rims[1], 0, range(2))
    firsts = [crop(stacked[:half], rims[1] - rims[0]), stacked[half : 2 * half]]
    top_ext = crop(stacked[2 * half :], rims[1] - top_rim[1])

    results, partials = [None, None], [None, None]
    for s in (1, 0):
        rim = rims[s]
        inputs_list = [firsts[s]]
        current = firsts[s]
        for layer_idx in range(layer_count):
            current = jnp.tanh(convolve(current, section_kernels[s][layer_idx]))
            current = jnp.where(
                inside_mask(tile_rows, tile_cols, rim - layer_idx - 1), current, 0.0
            )
            current = current.astype(jnp.bfloat16)
            inputs_list.append(current)
        flipped = jnp.transpose(section_kernels[s][:, ::-1, ::-1], (0, 1, 2, 4, 3))
        top_ext, signals = section_chain(top_ext, top_rim[s], inputs_list, rim, flipped)
        results[s] = crop(top_ext, top_rim[s] - layer_count)
        partials[s] = jnp.stack(
            [
                kernel_terms(crop(inputs_list[layer_idx], rim - layer_idx - 1), signals[layer_idx])
                for layer_idx in range(layer_count)
            ]
        )

    mine_terms = by_section(partials[0], partials[1], 0)
    other_terms = by_section(partials[1], partials[0], 0)
    gathered = summed_over_tiles(mine_terms + swap(other_terms))
    mine_back = by_section(results[0], results[1], 0)
    other_back = swap(by_section(results[1], results[0], 0))
    boundary = jnp.where(
        section_index == 0,
        jnp.concatenate([mine_back, other_back], axis=0),
        jnp.concatenate([other_back, mine_back], axis=0),
    )
    return (boundary[None], gathered / batches)


def solution(mesh):
    return jax.shard_map(
        local,
        mesh=mesh,
        in_specs=(
            P("section", None, "row", "col", None),
            P("section", None, None, None, None),
            P(None, "row", "col", None),
            P(),
        ),
        out_specs=(P("section", None, "row", "col", None), P("section", None, None, None, None)),
        check_vma=False,
    )
```

```python
import jax
import jax.numpy as jnp
from jax import lax
from jax.sharding import PartitionSpec as P

AXES = ("section", "row", "col")


def sizes():
    return tuple(lax.axis_size(axis) for axis in AXES)


def flat_index(position, shape):
    section, row, col = position
    return (section * shape[1] + row) * shape[2] + col


def rim_piece(block, width, dr, dc):
    rows, cols = block.shape[1], block.shape[2]
    row_span = {-1: (rows - width, rows), 0: (0, rows), 1: (0, width)}[dr]
    col_span = {-1: (cols - width, cols), 0: (0, cols), 1: (0, width)}[dc]
    return block[:, row_span[0] : row_span[1], col_span[0] : col_span[1]]


def from_neighbours(block, width, dim, from_section, sections_used):
    shape = sizes()
    parts = []
    for step in (-1, 0, 1):
        size = block.shape[dim]
        span = {-1: (size - width, size), 0: (0, size), 1: (0, width)}[step]
        piece = lax.slice_in_dim(block, span[0], span[1], axis=dim)
        if from_section == 0 and step == 0:
            parts.append(piece)
            continue
        pairs = []
        for s in sections_used:
            for r in range(shape[1]):
                for c in range(shape[2]):
                    source = [s + from_section, r, c]
                    source[dim] += step
                    if all(0 <= source[k] < shape[k] for k in range(3)):
                        pairs.append((flat_index(source, shape), flat_index((s, r, c), shape)))
        parts.append(lax.ppermute(piece, AXES, pairs))
    return jnp.concatenate(parts, axis=dim)


def with_rim(block, width, from_section, sections_used):
    rows_done = from_neighbours(block, width, 1, from_section, sections_used)
    return from_neighbours(rows_done, width, 2, 0, sections_used)


def inside_mask(tile_rows, tile_cols, width):
    image_rows = tile_rows * lax.axis_size("row")
    image_cols = tile_cols * lax.axis_size("col")
    rows = lax.axis_index("row") * tile_rows - width + jnp.arange(tile_rows + 2 * width)
    cols = lax.axis_index("col") * tile_cols - width + jnp.arange(tile_cols + 2 * width)
    row_ok = (rows >= 0) & (rows < image_rows)
    col_ok = (cols >= 0) & (cols < image_cols)
    return (row_ok[:, None] & col_ok[None, :])[None, :, :, None]


def convolve(padded, kernel):
    return lax.conv_general_dilated(
        padded,
        kernel,
        (1, 1),
        "VALID",
        dimension_numbers=("NHWC", "HWIO", "NHWC"),
        preferred_element_type=jnp.float32,
    )


def kernel_terms(padded, signal):
    terms = lax.conv_general_dilated(
        padded,
        signal,
        (1, 1),
        "VALID",
        dimension_numbers=("CHWN", "IHWO", "NHWC"),
        preferred_element_type=jnp.float32,
    )
    return jnp.transpose(terms, (1, 2, 0, 3))


def crop(block, width):
    return block[:, width : block.shape[1] - width, width : block.shape[2] - width]


def summed_over_tiles(grads):
    shape = sizes()

    def distances(count):
        found, distance = [], 1
        while distance < count:
            found.append(distance)
            distance *= 2
        return found

    def exchange(values, axis, distance):
        count = lax.axis_size(axis)
        return lax.ppermute(values, axis, [(i, i ^ distance) for i in range(count)])

    current = grads.reshape(-1)
    kept = []
    for distance in distances(shape[1]):
        half = current.shape[0] // 2
        upper = (lax.axis_index("row") // distance) % 2 == 1
        low, high = current[:half], current[half:]
        send = jnp.where(upper, low, high).astype(jnp.bfloat16)
        mine = jnp.where(upper, high, low).astype(jnp.bfloat16)
        other = exchange(send, "row", distance)
        current = mine.astype(jnp.float32) + other.astype(jnp.float32)
        kept.append((distance, upper))
    for distance in distances(shape[2]):
        rounded = current.astype(jnp.bfloat16)
        other = exchange(rounded, "col", distance)
        upper = (lax.axis_index("col") // distance) % 2 == 1
        first = jnp.where(upper, other, rounded).astype(jnp.float32)
        second = jnp.where(upper, rounded, other).astype(jnp.float32)
        current = first + second
    current = current.astype(jnp.bfloat16)
    for distance, upper in reversed(kept):
        other = exchange(current, "row", distance)
        current = jnp.where(
            upper, jnp.concatenate([other, current]), jnp.concatenate([current, other])
        )
    return current.astype(jnp.float32).reshape(grads.shape)


def local(checkpoints, kernels, cotangent, plan):
    sections_count, row_count, col_count = sizes()
    section_index = lax.axis_index("section")
    batches, tile_rows, tile_cols, channels = checkpoints.shape[1:]
    layer_count = kernels.shape[0]
    flipped = jnp.transpose(kernels[:, ::-1, ::-1], (0, 1, 2, 4, 3))
    inverse = jnp.sum(
        jnp.arange(batches)[:, None] * (plan[:, None] == jnp.arange(batches)[None, :]), axis=0
    )
    top_cotangent = jnp.take(cotangent, inverse, axis=0)

    deep = layer_count * (sections_count + 1) <= min(tile_rows, tile_cols)
    if deep and sections_count == 2 and batches % 2 == 0:
        return local_split(checkpoints, kernels, cotangent, plan)
    if deep:
        top_rim = [layer_count * (s + 1) for s in range(sections_count)]
    else:
        top_rim = [layer_count] * sections_count
    rim = top_rim[-1] + layer_count
    first = with_rim(checkpoints[0], rim, 0, range(sections_count))
    top_ext = with_rim(top_cotangent, top_rim[-1], 0, (sections_count - 1,))
    inputs_list = [first]
    current = first
    for layer_idx in range(layer_count):
        width = rim - layer_idx - 1
        current = jnp.tanh(convolve(current, kernels[layer_idx]))
        current = jnp.where(inside_mask(tile_rows, tile_cols, width), current, 0.0)
        current = current.astype(jnp.bfloat16)
        inputs_list.append(current)

    def backward(top_ext, top_width):
        gradient = top_ext.astype(jnp.float32)
        terms = [None] * layer_count
        for layer_idx in reversed(range(layer_count)):
            width = top_width - (layer_count - 1 - layer_idx)
            output = crop(inputs_list[layer_idx + 1], rim - layer_idx - 1 - width)
            output = output.astype(jnp.float32)
            signal = gradient * (1.0 - output * output)
            signal = jnp.where(inside_mask(tile_rows, tile_cols, width), signal, 0.0)
            signal = signal.astype(jnp.bfloat16)
            terms[layer_idx] = crop(signal, width)
            gradient = convolve(signal, flipped[layer_idx])
        return gradient.astype(jnp.bfloat16), terms

    def products(signals):
        return jnp.stack(
            [
                kernel_terms(crop(inputs_list[layer_idx], rim - layer_idx - 1), signals[layer_idx])
                for layer_idx in range(layer_count)
            ]
        )

    boundary = jnp.zeros((batches, tile_rows, tile_cols, channels), jnp.bfloat16)
    gathered = jnp.zeros((layer_count, 3, 3, channels, channels), jnp.float32)
    for tick in range(sections_count):
        active = sections_count - 1 - tick
        is_active = section_index == active
        if tick + 1 < sections_count or sections_count > 4:
            result, signals = backward(top_ext, top_rim[active])
        else:
            shapes = jax.eval_shape(lambda top: backward(top, top_rim[active]), top_ext)
            result, signals = lax.cond(
                is_active,
                lambda top: backward(top, top_rim[active]),
                lambda top: jax.tree.map(lambda v: jnp.zeros(v.shape, v.dtype), shapes),
                top_ext,
            )
        result_width = top_rim[active] - layer_count
        boundary = jnp.where(is_active, crop(result, result_width), boundary)
        if tick + 1 < sections_count:
            if deep:
                pairs = [
                    (flat_index((active, r, c), sizes()), flat_index((active - 1, r, c), sizes()))
                    for r in range(row_count)
                    for c in range(col_count)
                ]
                top_ext = lax.ppermute(result, AXES, pairs)
            else:
                top_ext = with_rim(result, layer_count, 1, (active - 1,))
        if sections_count > 4:
            terms = products(signals)
        else:
            terms = lax.cond(
                is_active, products, lambda unused: jnp.zeros_like(gathered), signals
            )
        gathered = jnp.where(is_active, terms, gathered)
    gathered = summed_over_tiles(gathered)
    kernel_grad = gathered / batches
    return (boundary[None], kernel_grad)


def hw_crop(block, width):
    return block[width : block.shape[0] - width, width : block.shape[1] - width]


def hw_mask(tile_rows, tile_cols, width):
    return inside_mask(tile_rows, tile_cols, width)[0, :, :, :, None]


def hw_convolve(padded, kernel):
    return lax.conv_general_dilated(
        padded,
        kernel,
        (1, 1),
        "VALID",
        dimension_numbers=("HWNC", "HWIO", "HWNC"),
        preferred_element_type=jnp.float32,
    )


def hw_kernel_terms(padded, signal):
    terms = lax.conv_general_dilated(
        padded,
        signal,
        (1, 1),
        "VALID",
        dimension_numbers=("HWCN", "HWIO", "NHWC"),
        preferred_element_type=jnp.float32,
    )
    return jnp.transpose(terms, (1, 2, 0, 3))


def hw_with_rim(block, width):
    moved = jnp.transpose(block, (2, 0, 1, 3))
    return jnp.transpose(with_rim(moved, width, 0, range(lax.axis_size("section"))), (1, 2, 0, 3))


def section_chain(top_ext, top_width, inputs_list, rim, flipped_kernels):
    layer_count = len(flipped_kernels)
    tile_rows = inputs_list[0].shape[0] - 2 * rim
    tile_cols = inputs_list[0].shape[1] - 2 * rim
    gradient = top_ext.astype(jnp.float32)
    signals = [None] * layer_count
    for layer_idx in reversed(range(layer_count)):
        width = top_width - (layer_count - 1 - layer_idx)
        output = hw_crop(inputs_list[layer_idx + 1], rim - layer_idx - 1 - width)
        output = output.astype(jnp.float32)
        signal = gradient * (1.0 - output * output)
        signal = jnp.where(hw_mask(tile_rows, tile_cols, width), signal, 0.0)
        signal = signal.astype(jnp.bfloat16)
        signals[layer_idx] = hw_crop(signal, width)
        gradient = hw_convolve(signal, flipped_kernels[layer_idx])
    return gradient.astype(jnp.bfloat16), signals


def local_split(checkpoints, kernels, cotangent, plan):
    section_index = lax.axis_index("section")
    batches, tile_rows, tile_cols, channels = checkpoints.shape[1:]
    layer_count = kernels.shape[0]
    half = batches // 2
    inverse = jnp.sum(
        jnp.arange(batches)[:, None] * (plan[:, None] == jnp.arange(batches)[None, :]), axis=0
    )
    top_cotangent = jnp.take(cotangent, inverse, axis=0)

    def swap(values):
        return lax.ppermute(values, "section", [(0, 1), (1, 0)])

    def by_section(mine, theirs, section):
        return jnp.where(section_index == section, mine, theirs)

    own = checkpoints[0]
    mine = lax.dynamic_slice_in_dim(own, section_index * half, half, 0)
    theirs = swap(lax.dynamic_slice_in_dim(own, (1 - section_index) * half, half, 0))
    other_kernels = swap(kernels)
    section_kernels = [by_section(kernels, other_kernels, s) for s in range(2)]

    top_rim = [layer_count * (s + 1) for s in range(2)]
    rims = [r + layer_count for r in top_rim]
    group_cotangent = lax.dynamic_slice_in_dim(top_cotangent, section_index * half, half, 0)
    stacked = [by_section(mine, theirs, s) for s in range(2)] + [group_cotangent]
    stacked = jnp.transpose(jnp.concatenate(stacked, axis=0), (1, 2, 0, 3))
    stacked = hw_with_rim(stacked, rims[1])
    firsts = [hw_crop(stacked[:, :, :half], rims[1] - rims[0]), stacked[:, :, half : 2 * half]]
    top_ext = hw_crop(stacked[:, :, 2 * half :], rims[1] - top_rim[1])

    results, partials = [None, None], [None, None]
    for s in (1, 0):
        rim = rims[s]
        inputs_list = [firsts[s]]
        current = firsts[s]
        for layer_idx in range(layer_count):
            current = jnp.tanh(hw_convolve(current, section_kernels[s][layer_idx]))
            current = jnp.where(hw_mask(tile_rows, tile_cols, rim - layer_idx - 1), current, 0.0)
            current = current.astype(jnp.bfloat16)
            inputs_list.append(current)
        flipped = jnp.transpose(section_kernels[s][:, ::-1, ::-1], (0, 1, 2, 4, 3))
        top_ext, signals = section_chain(top_ext, top_rim[s], inputs_list, rim, flipped)
        results[s] = hw_crop(top_ext, top_rim[s] - layer_count)
        partials[s] = jnp.stack(
            [
                hw_kernel_terms(
                    hw_crop(inputs_list[layer_idx], rim - layer_idx - 1), signals[layer_idx]
                )
                for layer_idx in range(layer_count)
            ]
        )

    mine_terms = by_section(partials[0], partials[1], 0)
    other_terms = by_section(partials[1], partials[0], 0)
    gathered = summed_over_tiles(mine_terms + swap(other_terms))
    mine_back = by_section(results[0], results[1], 0)
    other_back = swap(by_section(results[1], results[0], 0))
    boundary = jnp.where(
        section_index == 0,
        jnp.concatenate([mine_back, other_back], axis=2),
        jnp.concatenate([other_back, mine_back], axis=2),
    )
    return (jnp.transpose(boundary, (2, 0, 1, 3))[None], gathered / batches)


def solution(mesh):
    return jax.shard_map(
        local,
        mesh=mesh,
        in_specs=(
            P("section", None, "row", "col", None),
            P("section", None, None, None, None),
            P(None, "row", "col", None),
            P(),
        ),
        out_specs=(P("section", None, "row", "col", None), P("section", None, None, None, None)),
        check_vma=False,
    )
```

```python
import jax
import jax.numpy as jnp
from jax import lax
from jax.sharding import PartitionSpec as P

AXES = ("section", "row", "col")


def sizes():
    return tuple(lax.axis_size(axis) for axis in AXES)


def flat_index(position, shape):
    section, row, col = position
    return (section * shape[1] + row) * shape[2] + col


def rim_piece(block, width, dr, dc):
    rows, cols = block.shape[1], block.shape[2]
    row_span = {-1: (rows - width, rows), 0: (0, rows), 1: (0, width)}[dr]
    col_span = {-1: (cols - width, cols), 0: (0, cols), 1: (0, width)}[dc]
    return block[:, row_span[0] : row_span[1], col_span[0] : col_span[1]]


def from_neighbours(block, width, dim, from_section, sections_used):
    shape = sizes()
    parts = []
    for step in (-1, 0, 1):
        size = block.shape[dim]
        span = {-1: (size - width, size), 0: (0, size), 1: (0, width)}[step]
        piece = lax.slice_in_dim(block, span[0], span[1], axis=dim)
        if from_section == 0 and step == 0:
            parts.append(piece)
            continue
        pairs = []
        for s in sections_used:
            for r in range(shape[1]):
                for c in range(shape[2]):
                    source = [s + from_section, r, c]
                    source[dim] += step
                    if all(0 <= source[k] < shape[k] for k in range(3)):
                        pairs.append((flat_index(source, shape), flat_index((s, r, c), shape)))
        parts.append(lax.ppermute(piece, AXES, pairs))
    return jnp.concatenate(parts, axis=dim)


def with_rim(block, width, from_section, sections_used):
    rows_done = from_neighbours(block, width, 1, from_section, sections_used)
    return from_neighbours(rows_done, width, 2, 0, sections_used)


def inside_mask(tile_rows, tile_cols, width):
    image_rows = tile_rows * lax.axis_size("row")
    image_cols = tile_cols * lax.axis_size("col")
    rows = lax.axis_index("row") * tile_rows - width + jnp.arange(tile_rows + 2 * width)
    cols = lax.axis_index("col") * tile_cols - width + jnp.arange(tile_cols + 2 * width)
    row_ok = (rows >= 0) & (rows < image_rows)
    col_ok = (cols >= 0) & (cols < image_cols)
    return (row_ok[:, None] & col_ok[None, :])[None, :, :, None]


def convolve(padded, kernel):
    return lax.conv_general_dilated(
        padded,
        kernel,
        (1, 1),
        "VALID",
        dimension_numbers=("NHWC", "HWIO", "NHWC"),
        preferred_element_type=jnp.float32,
    )


def kernel_terms(padded, signal):
    terms = lax.conv_general_dilated(
        padded,
        signal,
        (1, 1),
        "VALID",
        dimension_numbers=("CHWN", "IHWO", "NHWC"),
        preferred_element_type=jnp.float32,
    )
    return jnp.transpose(terms, (1, 2, 0, 3))


def crop(block, width):
    return block[:, width : block.shape[1] - width, width : block.shape[2] - width]


def summed_over_tiles(grads):
    shape = sizes()

    def distances(count):
        found, distance = [], 1
        while distance < count:
            found.append(distance)
            distance *= 2
        return found

    def exchange(values, axis, distance):
        count = lax.axis_size(axis)
        return lax.ppermute(values, axis, [(i, i ^ distance) for i in range(count)])

    current = grads.reshape(-1)
    kept = []
    for distance in distances(shape[1]):
        half = current.shape[0] // 2
        upper = (lax.axis_index("row") // distance) % 2 == 1
        low, high = current[:half], current[half:]
        send = jnp.where(upper, low, high).astype(jnp.bfloat16)
        mine = jnp.where(upper, high, low).astype(jnp.bfloat16)
        other = exchange(send, "row", distance)
        current = mine.astype(jnp.float32) + other.astype(jnp.float32)
        kept.append((distance, upper))
    for distance in distances(shape[2]):
        rounded = current.astype(jnp.bfloat16)
        other = exchange(rounded, "col", distance)
        upper = (lax.axis_index("col") // distance) % 2 == 1
        first = jnp.where(upper, other, rounded).astype(jnp.float32)
        second = jnp.where(upper, rounded, other).astype(jnp.float32)
        current = first + second
    current = current.astype(jnp.bfloat16)
    for distance, upper in reversed(kept):
        other = exchange(current, "row", distance)
        current = jnp.where(
            upper, jnp.concatenate([other, current]), jnp.concatenate([current, other])
        )
    return current.astype(jnp.float32).reshape(grads.shape)


def local(checkpoints, kernels, cotangent, plan):
    sections_count, row_count, col_count = sizes()
    section_index = lax.axis_index("section")
    batches, tile_rows, tile_cols, channels = checkpoints.shape[1:]
    layer_count = kernels.shape[0]
    flipped = jnp.transpose(kernels[:, ::-1, ::-1], (0, 1, 2, 4, 3))
    inverse = jnp.sum(
        jnp.arange(batches)[:, None] * (plan[:, None] == jnp.arange(batches)[None, :]), axis=0
    )
    top_cotangent = jnp.take(cotangent, inverse, axis=0)

    deep = layer_count * (sections_count + 1) <= min(tile_rows, tile_cols)
    if deep and sections_count == 2 and batches % 2 == 0:
        return local_split(checkpoints, kernels, cotangent, plan)
    if deep:
        top_rim = [layer_count * (s + 1) for s in range(sections_count)]
    else:
        top_rim = [layer_count] * sections_count
    rim = top_rim[-1] + layer_count
    first = with_rim(checkpoints[0], rim, 0, range(sections_count))
    top_ext = with_rim(top_cotangent, top_rim[-1], 0, (sections_count - 1,))
    inputs_list = [first]
    current = first
    for layer_idx in range(layer_count):
        width = rim - layer_idx - 1
        current = jnp.tanh(convolve(current, kernels[layer_idx]))
        current = jnp.where(inside_mask(tile_rows, tile_cols, width), current, 0.0)
        current = current.astype(jnp.bfloat16)
        inputs_list.append(current)

    def backward(top_ext, top_width):
        gradient = top_ext.astype(jnp.float32)
        terms = [None] * layer_count
        for layer_idx in reversed(range(layer_count)):
            width = top_width - (layer_count - 1 - layer_idx)
            output = crop(inputs_list[layer_idx + 1], rim - layer_idx - 1 - width)
            output = output.astype(jnp.float32)
            signal = gradient * (1.0 - output * output)
            signal = jnp.where(inside_mask(tile_rows, tile_cols, width), signal, 0.0)
            signal = signal.astype(jnp.bfloat16)
            terms[layer_idx] = crop(signal, width)
            gradient = convolve(signal, flipped[layer_idx])
        return gradient.astype(jnp.bfloat16), terms

    def products(signals):
        return jnp.stack(
            [
                kernel_terms(crop(inputs_list[layer_idx], rim - layer_idx - 1), signals[layer_idx])
                for layer_idx in range(layer_count)
            ]
        )

    boundary = jnp.zeros((batches, tile_rows, tile_cols, channels), jnp.bfloat16)
    gathered = jnp.zeros((layer_count, 3, 3, channels, channels), jnp.float32)
    for tick in range(sections_count):
        active = sections_count - 1 - tick
        is_active = section_index == active
        if tick + 1 < sections_count or sections_count > 4:
            result, signals = backward(top_ext, top_rim[active])
        else:
            shapes = jax.eval_shape(lambda top: backward(top, top_rim[active]), top_ext)
            result, signals = lax.cond(
                is_active,
                lambda top: backward(top, top_rim[active]),
                lambda top: jax.tree.map(lambda v: jnp.zeros(v.shape, v.dtype), shapes),
                top_ext,
            )
        result_width = top_rim[active] - layer_count
        boundary = jnp.where(is_active, crop(result, result_width), boundary)
        if tick + 1 < sections_count:
            if deep:
                pairs = [
                    (flat_index((active, r, c), sizes()), flat_index((active - 1, r, c), sizes()))
                    for r in range(row_count)
                    for c in range(col_count)
                ]
                top_ext = lax.ppermute(result, AXES, pairs)
            else:
                top_ext = with_rim(result, layer_count, 1, (active - 1,))
        if sections_count > 4:
            terms = products(signals)
        else:
            terms = lax.cond(
                is_active, products, lambda unused: jnp.zeros_like(gathered), signals
            )
        gathered = jnp.where(is_active, terms, gathered)
    gathered = summed_over_tiles(gathered)
    kernel_grad = gathered / batches
    return (boundary[None], kernel_grad)


def section_chain(top_ext, top_width, inputs_list, rim, flipped_kernels):
    layer_count = len(flipped_kernels)
    tile_rows = inputs_list[0].shape[1] - 2 * rim
    tile_cols = inputs_list[0].shape[2] - 2 * rim
    gradient = top_ext.astype(jnp.float32)
    signals = [None] * layer_count
    for layer_idx in reversed(range(layer_count)):
        width = top_width - (layer_count - 1 - layer_idx)
        output = crop(inputs_list[layer_idx + 1], rim - layer_idx - 1 - width)
        output = output.astype(jnp.float32)
        signal = gradient * (1.0 - output * output)
        signal = jnp.where(inside_mask(tile_rows, tile_cols, width), signal, 0.0)
        signal = signal.astype(jnp.bfloat16)
        signals[layer_idx] = crop(signal, width)
        gradient = convolve(signal, flipped_kernels[layer_idx])
    return gradient.astype(jnp.bfloat16), signals


def local_split(checkpoints, kernels, cotangent, plan):
    section_index = lax.axis_index("section")
    batches, tile_rows, tile_cols, channels = checkpoints.shape[1:]
    layer_count = kernels.shape[0]
    half = batches // 2
    inverse = jnp.sum(
        jnp.arange(batches)[:, None] * (plan[:, None] == jnp.arange(batches)[None, :]), axis=0
    )
    top_cotangent = jnp.take(cotangent, inverse, axis=0)

    def swap(values):
        return lax.ppermute(values, "section", [(0, 1), (1, 0)])

    def by_section(mine, theirs, section):
        return jnp.where(section_index == section, mine, theirs)

    own = checkpoints[0]
    mine = lax.dynamic_slice_in_dim(own, section_index * half, half, 0)
    theirs = swap(lax.dynamic_slice_in_dim(own, (1 - section_index) * half, half, 0))
    other_kernels = swap(kernels)
    section_kernels = [by_section(kernels, other_kernels, s) for s in range(2)]

    top_rim = [layer_count * (s + 1) for s in range(2)]
    rims = [r + layer_count for r in top_rim]
    group_cotangent = lax.dynamic_slice_in_dim(top_cotangent, section_index * half, half, 0)
    stacked = [by_section(mine, theirs, s) for s in range(2)] + [group_cotangent]
    stacked = with_rim(jnp.concatenate(stacked, axis=0), rims[1], 0, range(2))
    firsts = [crop(stacked[:half], rims[1] - rims[0]), stacked[half : 2 * half]]
    top_ext = crop(stacked[2 * half :], rims[1] - top_rim[1])

    results, partials = [None, None], [None, None]
    for s in (1, 0):
        rim = rims[s]
        inputs_list = [firsts[s]]
        current = firsts[s]
        for layer_idx in range(layer_count):
            current = jnp.tanh(convolve(current, section_kernels[s][layer_idx]))
            current = jnp.where(
                inside_mask(tile_rows, tile_cols, rim - layer_idx - 1), current, 0.0
            )
            current = current.astype(jnp.bfloat16)
            inputs_list.append(current)
        flipped = jnp.transpose(section_kernels[s][:, ::-1, ::-1], (0, 1, 2, 4, 3))
        top_ext, signals = section_chain(top_ext, top_rim[s], inputs_list, rim, flipped)
        results[s] = crop(top_ext, top_rim[s] - layer_count)
        partials[s] = jnp.stack(
            [
                kernel_terms(crop(inputs_list[layer_idx], rim - layer_idx - 1), signals[layer_idx])
                for layer_idx in range(layer_count)
            ]
        )

    mine_terms = by_section(partials[0], partials[1], 0)
    other_terms = by_section(partials[1], partials[0], 0)
    scale = 1.0 / batches
    other_terms = swap((other_terms * scale).astype(jnp.bfloat16)).astype(jnp.float32)
    gathered = summed_over_tiles(mine_terms * scale + other_terms)
    mine_back = by_section(results[0], results[1], 0)
    other_back = swap(by_section(results[1], results[0], 0))
    boundary = jnp.where(
        section_index == 0,
        jnp.concatenate([mine_back, other_back], axis=0),
        jnp.concatenate([other_back, mine_back], axis=0),
    )
    return (boundary[None], gathered)


def solution(mesh):
    return jax.shard_map(
        local,
        mesh=mesh,
        in_specs=(
            P("section", None, "row", "col", None),
            P("section", None, None, None, None),
            P(None, "row", "col", None),
            P(),
        ),
        out_specs=(P("section", None, "row", "col", None), P("section", None, None, None, None)),
        check_vma=False,
    )
```

```python
import jax
import jax.numpy as jnp
from jax import lax
from jax.sharding import PartitionSpec as P

AXES = ("section", "row", "col")


def sizes():
    return tuple(lax.axis_size(axis) for axis in AXES)


def flat_index(position, shape):
    section, row, col = position
    return (section * shape[1] + row) * shape[2] + col


def rim_piece(block, width, dr, dc):
    rows, cols = block.shape[1], block.shape[2]
    row_span = {-1: (rows - width, rows), 0: (0, rows), 1: (0, width)}[dr]
    col_span = {-1: (cols - width, cols), 0: (0, cols), 1: (0, width)}[dc]
    return block[:, row_span[0] : row_span[1], col_span[0] : col_span[1]]


def from_neighbours(block, width, dim, from_section, sections_used):
    shape = sizes()
    parts = []
    for step in (-1, 0, 1):
        size = block.shape[dim]
        span = {-1: (size - width, size), 0: (0, size), 1: (0, width)}[step]
        piece = lax.slice_in_dim(block, span[0], span[1], axis=dim)
        if from_section == 0 and step == 0:
            parts.append(piece)
            continue
        pairs = []
        for s in sections_used:
            for r in range(shape[1]):
                for c in range(shape[2]):
                    source = [s + from_section, r, c]
                    source[dim] += step
                    if all(0 <= source[k] < shape[k] for k in range(3)):
                        pairs.append((flat_index(source, shape), flat_index((s, r, c), shape)))
        parts.append(lax.ppermute(piece, AXES, pairs))
    return jnp.concatenate(parts, axis=dim)


def with_rim(block, width, from_section, sections_used):
    rows_done = from_neighbours(block, width, 1, from_section, sections_used)
    return from_neighbours(rows_done, width, 2, 0, sections_used)


def inside_mask(tile_rows, tile_cols, width):
    image_rows = tile_rows * lax.axis_size("row")
    image_cols = tile_cols * lax.axis_size("col")
    rows = lax.axis_index("row") * tile_rows - width + jnp.arange(tile_rows + 2 * width)
    cols = lax.axis_index("col") * tile_cols - width + jnp.arange(tile_cols + 2 * width)
    row_ok = (rows >= 0) & (rows < image_rows)
    col_ok = (cols >= 0) & (cols < image_cols)
    return (row_ok[:, None] & col_ok[None, :])[None, :, :, None]


def convolve(padded, kernel):
    return lax.conv_general_dilated(
        padded,
        kernel,
        (1, 1),
        "VALID",
        dimension_numbers=("NHWC", "HWIO", "NHWC"),
        preferred_element_type=jnp.float32,
    )


def kernel_terms(padded, signal):
    terms = lax.conv_general_dilated(
        padded,
        signal,
        (1, 1),
        "VALID",
        dimension_numbers=("CHWN", "IHWO", "NHWC"),
        preferred_element_type=jnp.float32,
    )
    return jnp.transpose(terms, (1, 2, 0, 3))


def crop(block, width):
    return block[:, width : block.shape[1] - width, width : block.shape[2] - width]


def summed_over_tiles(grads):
    shape = sizes()
    halving, doubling = [], []
    for axis, dim in (("row", 1), ("col", 2)):
        distance = 1
        while distance < shape[dim]:
            (halving if distance == 1 else doubling).append((axis, distance))
            distance *= 2

    def exchange(values, axis, distance):
        count = lax.axis_size(axis)
        return lax.ppermute(values, axis, [(i, i ^ distance) for i in range(count)])

    current = grads.reshape(-1)
    kept = []
    for axis, distance in halving:
        half = current.shape[0] // 2
        upper = (lax.axis_index(axis) // distance) % 2 == 1
        low, high = current[:half], current[half:]
        send = jnp.where(upper, low, high).astype(jnp.bfloat16)
        mine = jnp.where(upper, high, low).astype(jnp.bfloat16)
        other = exchange(send, axis, distance)
        current = mine.astype(jnp.float32) + other.astype(jnp.float32)
        kept.append((axis, distance, upper))
    for axis, distance in doubling:
        rounded = current.astype(jnp.bfloat16)
        other = exchange(rounded, axis, distance)
        upper = (lax.axis_index(axis) // distance) % 2 == 1
        first = jnp.where(upper, other, rounded).astype(jnp.float32)
        second = jnp.where(upper, rounded, other).astype(jnp.float32)
        current = first + second
    current = current.astype(jnp.bfloat16)
    for axis, distance, upper in reversed(kept):
        other = exchange(current, axis, distance)
        current = jnp.where(
            upper, jnp.concatenate([other, current]), jnp.concatenate([current, other])
        )
    return current.astype(jnp.float32).reshape(grads.shape)


def local(checkpoints, kernels, cotangent, plan):
    sections_count, row_count, col_count = sizes()
    section_index = lax.axis_index("section")
    batches, tile_rows, tile_cols, channels = checkpoints.shape[1:]
    layer_count = kernels.shape[0]
    flipped = jnp.transpose(kernels[:, ::-1, ::-1], (0, 1, 2, 4, 3))
    inverse = jnp.sum(
        jnp.arange(batches)[:, None] * (plan[:, None] == jnp.arange(batches)[None, :]), axis=0
    )
    top_cotangent = jnp.take(cotangent, inverse, axis=0)

    deep = layer_count * (sections_count + 1) <= min(tile_rows, tile_cols)
    if deep and sections_count == 2 and batches % 2 == 0:
        return local_split(checkpoints, kernels, cotangent, plan)
    if deep:
        top_rim = [layer_count * (s + 1) for s in range(sections_count)]
    else:
        top_rim = [layer_count] * sections_count
    rim = top_rim[-1] + layer_count
    first = with_rim(checkpoints[0], rim, 0, range(sections_count))
    top_ext = with_rim(top_cotangent, top_rim[-1], 0, (sections_count - 1,))
    inputs_list = [first]
    current = first
    for layer_idx in range(layer_count):
        width = rim - layer_idx - 1
        current = jnp.tanh(convolve(current, kernels[layer_idx]))
        current = jnp.where(inside_mask(tile_rows, tile_cols, width), current, 0.0)
        current = current.astype(jnp.bfloat16)
        inputs_list.append(current)

    def backward(top_ext, top_width):
        gradient = top_ext.astype(jnp.float32)
        terms = [None] * layer_count
        for layer_idx in reversed(range(layer_count)):
            width = top_width - (layer_count - 1 - layer_idx)
            output = crop(inputs_list[layer_idx + 1], rim - layer_idx - 1 - width)
            output = output.astype(jnp.float32)
            signal = gradient * (1.0 - output * output)
            signal = jnp.where(inside_mask(tile_rows, tile_cols, width), signal, 0.0)
            signal = signal.astype(jnp.bfloat16)
            terms[layer_idx] = crop(signal, width)
            gradient = convolve(signal, flipped[layer_idx])
        return gradient.astype(jnp.bfloat16), terms

    def products(signals):
        return jnp.stack(
            [
                kernel_terms(crop(inputs_list[layer_idx], rim - layer_idx - 1), signals[layer_idx])
                for layer_idx in range(layer_count)
            ]
        )

    boundary = jnp.zeros((batches, tile_rows, tile_cols, channels), jnp.bfloat16)
    gathered = jnp.zeros((layer_count, 3, 3, channels, channels), jnp.float32)
    for tick in range(sections_count):
        active = sections_count - 1 - tick
        is_active = section_index == active
        if tick + 1 < sections_count or sections_count > 4:
            result, signals = backward(top_ext, top_rim[active])
        else:
            shapes = jax.eval_shape(lambda top: backward(top, top_rim[active]), top_ext)
            result, signals = lax.cond(
                is_active,
                lambda top: backward(top, top_rim[active]),
                lambda top: jax.tree.map(lambda v: jnp.zeros(v.shape, v.dtype), shapes),
                top_ext,
            )
        result_width = top_rim[active] - layer_count
        boundary = jnp.where(is_active, crop(result, result_width), boundary)
        if tick + 1 < sections_count:
            if deep:
                pairs = [
                    (flat_index((active, r, c), sizes()), flat_index((active - 1, r, c), sizes()))
                    for r in range(row_count)
                    for c in range(col_count)
                ]
                top_ext = lax.ppermute(result, AXES, pairs)
            else:
                top_ext = with_rim(result, layer_count, 1, (active - 1,))
        if sections_count > 4:
            terms = products(signals)
        else:
            terms = lax.cond(
                is_active, products, lambda unused: jnp.zeros_like(gathered), signals
            )
        gathered = jnp.where(is_active, terms, gathered)
    gathered = summed_over_tiles(gathered)
    kernel_grad = gathered / batches
    return (boundary[None], kernel_grad)


def section_chain(top_ext, top_width, inputs_list, rim, flipped_kernels):
    layer_count = len(flipped_kernels)
    tile_rows = inputs_list[0].shape[1] - 2 * rim
    tile_cols = inputs_list[0].shape[2] - 2 * rim
    gradient = top_ext.astype(jnp.float32)
    signals = [None] * layer_count
    for layer_idx in reversed(range(layer_count)):
        width = top_width - (layer_count - 1 - layer_idx)
        output = crop(inputs_list[layer_idx + 1], rim - layer_idx - 1 - width)
        output = output.astype(jnp.float32)
        signal = gradient * (1.0 - output * output)
        signal = jnp.where(inside_mask(tile_rows, tile_cols, width), signal, 0.0)
        signal = signal.astype(jnp.bfloat16)
        signals[layer_idx] = crop(signal, width)
        gradient = convolve(signal, flipped_kernels[layer_idx])
    return gradient.astype(jnp.bfloat16), signals


def local_split(checkpoints, kernels, cotangent, plan):
    section_index = lax.axis_index("section")
    batches, tile_rows, tile_cols, channels = checkpoints.shape[1:]
    layer_count = kernels.shape[0]
    half = batches // 2
    inverse = jnp.sum(
        jnp.arange(batches)[:, None] * (plan[:, None] == jnp.arange(batches)[None, :]), axis=0
    )
    top_cotangent = jnp.take(cotangent, inverse, axis=0)

    def swap(values):
        return lax.ppermute(values, "section", [(0, 1), (1, 0)])

    def by_section(mine, theirs, section):
        return jnp.where(section_index == section, mine, theirs)

    own = checkpoints[0]
    mine = lax.dynamic_slice_in_dim(own, section_index * half, half, 0)
    theirs = swap(lax.dynamic_slice_in_dim(own, (1 - section_index) * half, half, 0))
    other_kernels = swap(kernels)
    section_kernels = [by_section(kernels, other_kernels, s) for s in range(2)]

    top_rim = [layer_count * (s + 1) for s in range(2)]
    rims = [r + layer_count for r in top_rim]
    group_cotangent = lax.dynamic_slice_in_dim(top_cotangent, section_index * half, half, 0)
    stacked = [by_section(mine, theirs, s) for s in range(2)] + [group_cotangent]
    stacked = with_rim(jnp.concatenate(stacked, axis=0), rims[1], 0, range(2))
    firsts = [crop(stacked[:half], rims[1] - rims[0]), stacked[half : 2 * half]]
    top_ext = crop(stacked[2 * half :], rims[1] - top_rim[1])

    results, partials = [None, None], [None, None]
    for s in (1, 0):
        rim = rims[s]
        inputs_list = [firsts[s]]
        current = firsts[s]
        for layer_idx in range(layer_count):
            current = jnp.tanh(convolve(current, section_kernels[s][layer_idx]))
            current = jnp.where(
                inside_mask(tile_rows, tile_cols, rim - layer_idx - 1), current, 0.0
            )
            current = current.astype(jnp.bfloat16)
            inputs_list.append(current)
        flipped = jnp.transpose(section_kernels[s][:, ::-1, ::-1], (0, 1, 2, 4, 3))
        top_ext, signals = section_chain(top_ext, top_rim[s], inputs_list, rim, flipped)
        results[s] = crop(top_ext, top_rim[s] - layer_count)
        partials[s] = jnp.stack(
            [
                kernel_terms(crop(inputs_list[layer_idx], rim - layer_idx - 1), signals[layer_idx])
                for layer_idx in range(layer_count)
            ]
        )

    mine_terms = by_section(partials[0], partials[1], 0)
    other_terms = by_section(partials[1], partials[0], 0)
    scale = 1.0 / batches
    other_terms = swap((other_terms * scale).astype(jnp.bfloat16)).astype(jnp.float32)
    gathered = summed_over_tiles(mine_terms * scale + other_terms)
    mine_back = by_section(results[0], results[1], 0)
    other_back = swap(by_section(results[1], results[0], 0))
    boundary = jnp.where(
        section_index == 0,
        jnp.concatenate([mine_back, other_back], axis=0),
        jnp.concatenate([other_back, mine_back], axis=0),
    )
    return (boundary[None], gathered)


def solution(mesh):
    return jax.shard_map(
        local,
        mesh=mesh,
        in_specs=(
            P("section", None, "row", "col", None),
            P("section", None, None, None, None),
            P(None, "row", "col", None),
            P(),
        ),
        out_specs=(P("section", None, "row", "col", None), P("section", None, None, None, None)),
        check_vma=False,
    )
```

```python
import jax
import jax.numpy as jnp
from jax import lax
from jax.sharding import PartitionSpec as P

AXES = ("section", "row", "col")


def sizes():
    return tuple(lax.axis_size(axis) for axis in AXES)


def flat_index(position, shape):
    section, row, col = position
    return (section * shape[1] + row) * shape[2] + col


def rim_piece(block, width, dr, dc):
    rows, cols = block.shape[1], block.shape[2]
    row_span = {-1: (rows - width, rows), 0: (0, rows), 1: (0, width)}[dr]
    col_span = {-1: (cols - width, cols), 0: (0, cols), 1: (0, width)}[dc]
    return block[:, row_span[0] : row_span[1], col_span[0] : col_span[1]]


def from_neighbours(block, width, dim, from_section, sections_used):
    shape = sizes()
    parts = []
    for step in (-1, 0, 1):
        size = block.shape[dim]
        span = {-1: (size - width, size), 0: (0, size), 1: (0, width)}[step]
        piece = lax.slice_in_dim(block, span[0], span[1], axis=dim)
        if from_section == 0 and step == 0:
            parts.append(piece)
            continue
        pairs = []
        for s in sections_used:
            for r in range(shape[1]):
                for c in range(shape[2]):
                    source = [s + from_section, r, c]
                    source[dim] += step
                    if all(0 <= source[k] < shape[k] for k in range(3)):
                        pairs.append((flat_index(source, shape), flat_index((s, r, c), shape)))
        parts.append(lax.ppermute(piece, AXES, pairs))
    return jnp.concatenate(parts, axis=dim)


def with_rim(block, width, from_section, sections_used):
    rows_done = from_neighbours(block, width, 1, from_section, sections_used)
    return from_neighbours(rows_done, width, 2, 0, sections_used)


def inside_mask(tile_rows, tile_cols, width):
    image_rows = tile_rows * lax.axis_size("row")
    image_cols = tile_cols * lax.axis_size("col")
    rows = lax.axis_index("row") * tile_rows - width + jnp.arange(tile_rows + 2 * width)
    cols = lax.axis_index("col") * tile_cols - width + jnp.arange(tile_cols + 2 * width)
    row_ok = (rows >= 0) & (rows < image_rows)
    col_ok = (cols >= 0) & (cols < image_cols)
    return (row_ok[:, None] & col_ok[None, :])[None, :, :, None]


def convolve(padded, kernel):
    return lax.conv_general_dilated(
        padded,
        kernel,
        (1, 1),
        "VALID",
        dimension_numbers=("NHWC", "HWIO", "NHWC"),
        preferred_element_type=jnp.float32,
    )


def kernel_terms(padded, signal):
    terms = lax.conv_general_dilated(
        padded,
        signal,
        (1, 1),
        "VALID",
        dimension_numbers=("CHWN", "IHWO", "NHWC"),
        preferred_element_type=jnp.float32,
    )
    return jnp.transpose(terms, (1, 2, 0, 3))


def crop(block, width):
    return block[:, width : block.shape[1] - width, width : block.shape[2] - width]


def summed_over_tiles(grads):
    shape = sizes()
    halving, doubling = [], []
    for axis, dim in (("row", 1), ("col", 2)):
        distance = 1
        while distance < shape[dim]:
            (halving if distance == 1 else doubling).append((axis, distance))
            distance *= 2

    def exchange(values, axis, distance):
        count = lax.axis_size(axis)
        return lax.ppermute(values, axis, [(i, i ^ distance) for i in range(count)])

    current = grads.reshape(-1)
    kept = []
    for axis, distance in halving:
        half = current.shape[0] // 2
        upper = (lax.axis_index(axis) // distance) % 2 == 1
        low, high = current[:half], current[half:]
        send = jnp.where(upper, low, high).astype(jnp.bfloat16)
        mine = jnp.where(upper, high, low).astype(jnp.bfloat16)
        other = exchange(send, axis, distance)
        current = mine.astype(jnp.float32) + other.astype(jnp.float32)
        kept.append((axis, distance, upper))
    for axis, distance in doubling:
        rounded = current.astype(jnp.bfloat16)
        other = exchange(rounded, axis, distance)
        upper = (lax.axis_index(axis) // distance) % 2 == 1
        first = jnp.where(upper, other, rounded).astype(jnp.float32)
        second = jnp.where(upper, rounded, other).astype(jnp.float32)
        current = first + second
    current = current.astype(jnp.bfloat16)
    for axis, distance, upper in reversed(kept):
        other = exchange(current, axis, distance)
        current = jnp.where(
            upper, jnp.concatenate([other, current]), jnp.concatenate([current, other])
        )
    return current.astype(jnp.float32).reshape(grads.shape)


def local(checkpoints, kernels, cotangent, plan):
    sections_count, row_count, col_count = sizes()
    section_index = lax.axis_index("section")
    batches, tile_rows, tile_cols, channels = checkpoints.shape[1:]
    layer_count = kernels.shape[0]
    flipped = jnp.transpose(kernels[:, ::-1, ::-1], (0, 1, 2, 4, 3))
    inverse = jnp.sum(
        jnp.arange(batches)[:, None] * (plan[:, None] == jnp.arange(batches)[None, :]), axis=0
    )
    top_cotangent = jnp.take(cotangent, inverse, axis=0)

    deep = layer_count * (sections_count + 1) <= min(tile_rows, tile_cols)
    if deep and sections_count == 2 and batches % 2 == 0:
        return local_split(checkpoints, kernels, cotangent, plan)
    if deep:
        top_rim = [layer_count * (s + 1) for s in range(sections_count)]
    else:
        top_rim = [layer_count] * sections_count
    rim = top_rim[-1] + layer_count
    first = with_rim(checkpoints[0], rim, 0, range(sections_count))
    top_ext = with_rim(top_cotangent, top_rim[-1], 0, (sections_count - 1,))
    inputs_list = [first]
    current = first
    for layer_idx in range(layer_count):
        width = rim - layer_idx - 1
        current = jnp.tanh(convolve(current, kernels[layer_idx]))
        current = jnp.where(inside_mask(tile_rows, tile_cols, width), current, 0.0)
        current = current.astype(jnp.bfloat16)
        inputs_list.append(current)

    def backward(top_ext, top_width):
        gradient = top_ext.astype(jnp.float32)
        terms = [None] * layer_count
        for layer_idx in reversed(range(layer_count)):
            width = top_width - (layer_count - 1 - layer_idx)
            output = crop(inputs_list[layer_idx + 1], rim - layer_idx - 1 - width)
            output = output.astype(jnp.float32)
            signal = gradient * (1.0 - output * output)
            signal = jnp.where(inside_mask(tile_rows, tile_cols, width), signal, 0.0)
            signal = signal.astype(jnp.bfloat16)
            terms[layer_idx] = crop(signal, width)
            gradient = convolve(signal, flipped[layer_idx])
        return gradient.astype(jnp.bfloat16), terms

    def products(signals):
        return jnp.stack(
            [
                kernel_terms(crop(inputs_list[layer_idx], rim - layer_idx - 1), signals[layer_idx])
                for layer_idx in range(layer_count)
            ]
        )

    boundary = jnp.zeros((batches, tile_rows, tile_cols, channels), jnp.bfloat16)
    gathered = jnp.zeros((layer_count, 3, 3, channels, channels), jnp.float32)
    for tick in range(sections_count):
        active = sections_count - 1 - tick
        is_active = section_index == active
        if tick + 1 < sections_count or sections_count > 4:
            result, signals = backward(top_ext, top_rim[active])
        else:
            shapes = jax.eval_shape(lambda top: backward(top, top_rim[active]), top_ext)
            result, signals = lax.cond(
                is_active,
                lambda top: backward(top, top_rim[active]),
                lambda top: jax.tree.map(lambda v: jnp.zeros(v.shape, v.dtype), shapes),
                top_ext,
            )
        result_width = top_rim[active] - layer_count
        boundary = jnp.where(is_active, crop(result, result_width), boundary)
        if tick + 1 < sections_count:
            if deep:
                pairs = [
                    (flat_index((active, r, c), sizes()), flat_index((active - 1, r, c), sizes()))
                    for r in range(row_count)
                    for c in range(col_count)
                ]
                top_ext = lax.ppermute(result, AXES, pairs)
            else:
                top_ext = with_rim(result, layer_count, 1, (active - 1,))
        if sections_count > 4:
            terms = products(signals)
        else:
            terms = lax.cond(
                is_active, products, lambda unused: jnp.zeros_like(gathered), signals
            )
        gathered = jnp.where(is_active, terms, gathered)
    gathered = summed_over_tiles(gathered)
    kernel_grad = gathered / batches
    return (boundary[None], kernel_grad)


def section_chain(top_ext, top_width, inputs_list, rim, flipped_kernels):
    layer_count = len(flipped_kernels)
    tile_rows = inputs_list[0].shape[1] - 2 * rim
    tile_cols = inputs_list[0].shape[2] - 2 * rim
    gradient = top_ext.astype(jnp.float32)
    signals = [None] * layer_count
    for layer_idx in reversed(range(layer_count)):
        width = top_width - (layer_count - 1 - layer_idx)
        output = crop(inputs_list[layer_idx + 1], rim - layer_idx - 1 - width)
        output = output.astype(jnp.float32)
        signal = gradient * (1.0 - output * output)
        signal = jnp.where(inside_mask(tile_rows, tile_cols, width), signal, 0.0)
        signal = signal.astype(jnp.bfloat16)
        signals[layer_idx] = crop(signal, width)
        gradient = convolve(signal, flipped_kernels[layer_idx])
    return gradient.astype(jnp.bfloat16), signals


def local_split(checkpoints, kernels, cotangent, plan):
    section_index = lax.axis_index("section")
    batches, tile_rows, tile_cols, channels = checkpoints.shape[1:]
    layer_count = kernels.shape[0]
    half = batches // 2
    inverse = jnp.sum(
        jnp.arange(batches)[:, None] * (plan[:, None] == jnp.arange(batches)[None, :]), axis=0
    )
    top_cotangent = jnp.take(cotangent, inverse, axis=0)

    def swap(values):
        return lax.ppermute(values, "section", [(0, 1), (1, 0)])

    def by_section(mine, theirs, section):
        return jnp.where(section_index == section, mine, theirs)

    own = checkpoints[0]
    mine = lax.dynamic_slice_in_dim(own, section_index * half, half, 0)
    theirs = swap(lax.dynamic_slice_in_dim(own, (1 - section_index) * half, half, 0))
    other_kernels = swap(kernels)
    section_kernels = [by_section(kernels, other_kernels, s) for s in range(2)]

    top_rim = [layer_count * (s + 1) for s in range(2)]
    rims = [r + layer_count for r in top_rim]
    group_cotangent = lax.dynamic_slice_in_dim(top_cotangent, section_index * half, half, 0)
    stacked = [by_section(mine, theirs, s) for s in range(2)] + [group_cotangent]
    stacked = with_rim(jnp.concatenate(stacked, axis=0), rims[1], 0, range(2))
    firsts = [crop(stacked[:half], rims[1] - rims[0]), stacked[half : 2 * half]]
    top_ext = crop(stacked[2 * half :], rims[1] - top_rim[1])

    results, partials = [None, None], [None, None]
    for s in (1, 0):
        rim = rims[s]
        inputs_list = [firsts[s]]
        current = firsts[s]
        for layer_idx in range(layer_count):
            current = jnp.tanh(convolve(current, section_kernels[s][layer_idx]))
            current = jnp.where(
                inside_mask(tile_rows, tile_cols, rim - layer_idx - 1), current, 0.0
            )
            current = current.astype(jnp.bfloat16)
            inputs_list.append(current)
        flipped = jnp.transpose(section_kernels[s][:, ::-1, ::-1], (0, 1, 2, 4, 3))
        top_ext, signals = section_chain(top_ext, top_rim[s], inputs_list, rim, flipped)
        results[s] = crop(top_ext, top_rim[s] - layer_count)
        partials[s] = [
            kernel_terms(crop(inputs_list[layer_idx], rim - layer_idx - 1), signals[layer_idx])
            for layer_idx in range(layer_count)
        ]

    scale = 1.0 / batches
    summed = []
    for layer_idx in reversed(range(layer_count)):
        mine_terms = by_section(partials[0][layer_idx], partials[1][layer_idx], 0)
        other_terms = by_section(partials[1][layer_idx], partials[0][layer_idx], 0)
        other_terms = swap((other_terms * scale).astype(jnp.bfloat16)).astype(jnp.float32)
        summed.insert(0, summed_over_tiles(mine_terms * scale + other_terms))
    gathered = jnp.stack(summed)
    mine_back = by_section(results[0], results[1], 0)
    other_back = swap(by_section(results[1], results[0], 0))
    boundary = jnp.where(
        section_index == 0,
        jnp.concatenate([mine_back, other_back], axis=0),
        jnp.concatenate([other_back, mine_back], axis=0),
    )
    return (boundary[None], gathered)


def solution(mesh):
    return jax.shard_map(
        local,
        mesh=mesh,
        in_specs=(
            P("section", None, "row", "col", None),
            P("section", None, None, None, None),
            P(None, "row", "col", None),
            P(),
        ),
        out_specs=(P("section", None, "row", "col", None), P("section", None, None, None, None)),
        check_vma=False,
    )
```

```python
import jax
import jax.numpy as jnp
from jax import lax
from jax.sharding import PartitionSpec as P

AXES = ("section", "row", "col")


def sizes():
    return tuple(lax.axis_size(axis) for axis in AXES)


def flat_index(position, shape):
    section, row, col = position
    return (section * shape[1] + row) * shape[2] + col


def rim_piece(block, width, dr, dc):
    rows, cols = block.shape[1], block.shape[2]
    row_span = {-1: (rows - width, rows), 0: (0, rows), 1: (0, width)}[dr]
    col_span = {-1: (cols - width, cols), 0: (0, cols), 1: (0, width)}[dc]
    return block[:, row_span[0] : row_span[1], col_span[0] : col_span[1]]


def from_neighbours(block, width, dim, from_section, sections_used):
    shape = sizes()
    parts = []
    for step in (-1, 0, 1):
        size = block.shape[dim]
        span = {-1: (size - width, size), 0: (0, size), 1: (0, width)}[step]
        piece = lax.slice_in_dim(block, span[0], span[1], axis=dim)
        if from_section == 0 and step == 0:
            parts.append(piece)
            continue
        pairs = []
        for s in sections_used:
            for r in range(shape[1]):
                for c in range(shape[2]):
                    source = [s + from_section, r, c]
                    source[dim] += step
                    if all(0 <= source[k] < shape[k] for k in range(3)):
                        pairs.append((flat_index(source, shape), flat_index((s, r, c), shape)))
        parts.append(lax.ppermute(piece, AXES, pairs))
    return jnp.concatenate(parts, axis=dim)


def with_rim(block, width, from_section, sections_used):
    rows_done = from_neighbours(block, width, 1, from_section, sections_used)
    return from_neighbours(rows_done, width, 2, 0, sections_used)


def inside_mask(tile_rows, tile_cols, width):
    image_rows = tile_rows * lax.axis_size("row")
    image_cols = tile_cols * lax.axis_size("col")
    rows = lax.axis_index("row") * tile_rows - width + jnp.arange(tile_rows + 2 * width)
    cols = lax.axis_index("col") * tile_cols - width + jnp.arange(tile_cols + 2 * width)
    row_ok = (rows >= 0) & (rows < image_rows)
    col_ok = (cols >= 0) & (cols < image_cols)
    return (row_ok[:, None] & col_ok[None, :])[None, :, :, None]


def convolve(padded, kernel):
    return lax.conv_general_dilated(
        padded,
        kernel,
        (1, 1),
        "VALID",
        dimension_numbers=("NHWC", "HWIO", "NHWC"),
        preferred_element_type=jnp.float32,
    )


def kernel_terms(padded, signal):
    terms = lax.conv_general_dilated(
        padded,
        signal,
        (1, 1),
        "VALID",
        dimension_numbers=("CHWN", "IHWO", "NHWC"),
        preferred_element_type=jnp.float32,
    )
    return jnp.transpose(terms, (1, 2, 0, 3))


def crop(block, width):
    return block[:, width : block.shape[1] - width, width : block.shape[2] - width]


def summed_over_tiles(grads):
    shape = sizes()
    halving, doubling = [], []
    for axis, dim in (("row", 1), ("col", 2)):
        distance = 1
        while distance < shape[dim]:
            (halving if distance == 1 else doubling).append((axis, distance))
            distance *= 2

    def exchange(values, axis, distance):
        count = lax.axis_size(axis)
        return lax.ppermute(values, axis, [(i, i ^ distance) for i in range(count)])

    current = grads.reshape(-1)
    kept = []
    for axis, distance in halving:
        half = current.shape[0] // 2
        upper = (lax.axis_index(axis) // distance) % 2 == 1
        low, high = current[:half], current[half:]
        send = jnp.where(upper, low, high).astype(jnp.bfloat16)
        mine = jnp.where(upper, high, low).astype(jnp.bfloat16)
        other = exchange(send, axis, distance)
        current = mine.astype(jnp.float32) + other.astype(jnp.float32)
        kept.append((axis, distance, upper))
    for axis, distance in doubling:
        rounded = current.astype(jnp.bfloat16)
        other = exchange(rounded, axis, distance)
        upper = (lax.axis_index(axis) // distance) % 2 == 1
        first = jnp.where(upper, other, rounded).astype(jnp.float32)
        second = jnp.where(upper, rounded, other).astype(jnp.float32)
        current = first + second
    current = current.astype(jnp.bfloat16)
    for axis, distance, upper in reversed(kept):
        other = exchange(current, axis, distance)
        current = jnp.where(
            upper, jnp.concatenate([other, current]), jnp.concatenate([current, other])
        )
    return current.astype(jnp.float32).reshape(grads.shape)


def local(checkpoints, kernels, cotangent, plan):
    sections_count, row_count, col_count = sizes()
    section_index = lax.axis_index("section")
    batches, tile_rows, tile_cols, channels = checkpoints.shape[1:]
    layer_count = kernels.shape[0]
    flipped = jnp.transpose(kernels[:, ::-1, ::-1], (0, 1, 2, 4, 3))
    inverse = jnp.sum(
        jnp.arange(batches)[:, None] * (plan[:, None] == jnp.arange(batches)[None, :]), axis=0
    )
    top_cotangent = jnp.take(cotangent, inverse, axis=0)

    deep = layer_count * (sections_count + 1) <= min(tile_rows, tile_cols)
    if deep and sections_count == 2 and batches % 2 == 0:
        return local_split(checkpoints, kernels, cotangent, plan)
    if deep:
        top_rim = [layer_count * (s + 1) for s in range(sections_count)]
    else:
        top_rim = [layer_count] * sections_count
    rim = top_rim[-1] + layer_count
    first = with_rim(checkpoints[0], rim, 0, range(sections_count))
    top_ext = with_rim(top_cotangent, top_rim[-1], 0, (sections_count - 1,))
    inputs_list = [first]
    current = first
    for layer_idx in range(layer_count):
        width = rim - layer_idx - 1
        current = jnp.tanh(convolve(current, kernels[layer_idx]))
        current = jnp.where(inside_mask(tile_rows, tile_cols, width), current, 0.0)
        current = current.astype(jnp.bfloat16)
        inputs_list.append(current)

    def backward(top_ext, top_width):
        gradient = top_ext.astype(jnp.float32)
        terms = [None] * layer_count
        for layer_idx in reversed(range(layer_count)):
            width = top_width - (layer_count - 1 - layer_idx)
            output = crop(inputs_list[layer_idx + 1], rim - layer_idx - 1 - width)
            output = output.astype(jnp.float32)
            signal = gradient * (1.0 - output * output)
            signal = jnp.where(inside_mask(tile_rows, tile_cols, width), signal, 0.0)
            signal = signal.astype(jnp.bfloat16)
            terms[layer_idx] = crop(signal, width)
            gradient = convolve(signal, flipped[layer_idx])
        return gradient.astype(jnp.bfloat16), terms

    def products(signals):
        return jnp.stack(
            [
                kernel_terms(crop(inputs_list[layer_idx], rim - layer_idx - 1), signals[layer_idx])
                for layer_idx in range(layer_count)
            ]
        )

    boundary = jnp.zeros((batches, tile_rows, tile_cols, channels), jnp.bfloat16)
    gathered = jnp.zeros((layer_count, 3, 3, channels, channels), jnp.float32)
    for tick in range(sections_count):
        active = sections_count - 1 - tick
        is_active = section_index == active
        if tick + 1 < sections_count or sections_count > 4:
            result, signals = backward(top_ext, top_rim[active])
        else:
            shapes = jax.eval_shape(lambda top: backward(top, top_rim[active]), top_ext)
            result, signals = lax.cond(
                is_active,
                lambda top: backward(top, top_rim[active]),
                lambda top: jax.tree.map(lambda v: jnp.zeros(v.shape, v.dtype), shapes),
                top_ext,
            )
        result_width = top_rim[active] - layer_count
        boundary = jnp.where(is_active, crop(result, result_width), boundary)
        if tick + 1 < sections_count:
            if deep:
                pairs = [
                    (flat_index((active, r, c), sizes()), flat_index((active - 1, r, c), sizes()))
                    for r in range(row_count)
                    for c in range(col_count)
                ]
                top_ext = lax.ppermute(result, AXES, pairs)
            else:
                top_ext = with_rim(result, layer_count, 1, (active - 1,))
        if sections_count > 4:
            terms = products(signals)
        else:
            terms = lax.cond(
                is_active, products, lambda unused: jnp.zeros_like(gathered), signals
            )
        gathered = jnp.where(is_active, terms, gathered)
    gathered = summed_over_tiles(gathered)
    kernel_grad = gathered / batches
    return (boundary[None], kernel_grad)


def section_chain(top_ext, top_width, inputs_list, rim, flipped_kernels):
    layer_count = len(flipped_kernels)
    tile_rows = inputs_list[0].shape[1] - 2 * rim
    tile_cols = inputs_list[0].shape[2] - 2 * rim
    gradient = top_ext.astype(jnp.float32)
    signals = [None] * layer_count
    for layer_idx in reversed(range(layer_count)):
        width = top_width - (layer_count - 1 - layer_idx)
        output = crop(inputs_list[layer_idx + 1], rim - layer_idx - 1 - width)
        output = output.astype(jnp.float32)
        signal = gradient * (1.0 - output * output)
        signal = jnp.where(inside_mask(tile_rows, tile_cols, width), signal, 0.0)
        signal = signal.astype(jnp.bfloat16)
        signals[layer_idx] = crop(signal, width)
        gradient = convolve(signal, flipped_kernels[layer_idx])
    return gradient.astype(jnp.bfloat16), signals


def local_split(checkpoints, kernels, cotangent, plan):
    section_index = lax.axis_index("section")
    batches, tile_rows, tile_cols, channels = checkpoints.shape[1:]
    layer_count = kernels.shape[0]
    half = batches // 2
    inverse = jnp.sum(
        jnp.arange(batches)[:, None] * (plan[:, None] == jnp.arange(batches)[None, :]), axis=0
    )
    top_cotangent = jnp.take(cotangent, inverse, axis=0)

    def swap(values):
        return lax.ppermute(values, "section", [(0, 1), (1, 0)])

    def by_section(mine, theirs, section):
        return jnp.where(section_index == section, mine, theirs)

    own = checkpoints[0]
    mine = lax.dynamic_slice_in_dim(own, section_index * half, half, 0)
    theirs = swap(lax.dynamic_slice_in_dim(own, (1 - section_index) * half, half, 0))
    other_kernels = swap(kernels)
    section_kernels = [by_section(kernels, other_kernels, s) for s in range(2)]

    top_rim = [layer_count * (s + 1) for s in range(2)]
    rims = [r + layer_count for r in top_rim]
    group_cotangent = lax.dynamic_slice_in_dim(top_cotangent, section_index * half, half, 0)
    stacked = [by_section(mine, theirs, s) for s in range(2)] + [group_cotangent]
    stacked = with_rim(jnp.concatenate(stacked, axis=0), rims[1], 0, range(2))
    firsts = [crop(stacked[:half], rims[1] - rims[0]), stacked[half : 2 * half]]
    top_ext = crop(stacked[2 * half :], rims[1] - top_rim[1])

    results, partials = [None, None], [None, None]
    for s in (1, 0):
        rim = rims[s]
        inputs_list = [firsts[s]]
        current = firsts[s]
        for layer_idx in range(layer_count):
            current = jnp.tanh(convolve(current, section_kernels[s][layer_idx]))
            current = jnp.where(
                inside_mask(tile_rows, tile_cols, rim - layer_idx - 1), current, 0.0
            )
            current = current.astype(jnp.bfloat16)
            inputs_list.append(current)
        flipped = jnp.transpose(section_kernels[s][:, ::-1, ::-1], (0, 1, 2, 4, 3))
        top_ext, signals = section_chain(top_ext, top_rim[s], inputs_list, rim, flipped)
        results[s] = crop(top_ext, top_rim[s] - layer_count)
        partials[s] = [
            kernel_terms(crop(inputs_list[layer_idx], rim - layer_idx - 1), signals[layer_idx])
            for layer_idx in range(layer_count)
        ]

    scale = 1.0 / batches
    summed = []
    for layer_idx in reversed(range(layer_count)):
        mine_terms = by_section(partials[0][layer_idx], partials[1][layer_idx], 0)
        other_terms = by_section(partials[1][layer_idx], partials[0][layer_idx], 0)
        other_terms = swap((other_terms * scale).astype(jnp.bfloat16)).astype(jnp.float32)
        total = (mine_terms * scale + other_terms).reshape(2, -1)
        parts = [summed_over_tiles(total[part]) for part in range(2)]
        summed.insert(0, jnp.concatenate(parts).reshape(mine_terms.shape))
    gathered = jnp.stack(summed)
    mine_back = by_section(results[0], results[1], 0)
    other_back = swap(by_section(results[1], results[0], 0))
    boundary = jnp.where(
        section_index == 0,
        jnp.concatenate([mine_back, other_back], axis=0),
        jnp.concatenate([other_back, mine_back], axis=0),
    )
    return (boundary[None], gathered)


def solution(mesh):
    return jax.shard_map(
        local,
        mesh=mesh,
        in_specs=(
            P("section", None, "row", "col", None),
            P("section", None, None, None, None),
            P(None, "row", "col", None),
            P(),
        ),
        out_specs=(P("section", None, "row", "col", None), P("section", None, None, None, None)),
        check_vma=False,
    )
```

```python
import jax
import jax.numpy as jnp
from jax import lax
from jax.sharding import PartitionSpec as P

AXES = ("section", "row", "col")


def sizes():
    return tuple(lax.axis_size(axis) for axis in AXES)


def flat_index(position, shape):
    section, row, col = position
    return (section * shape[1] + row) * shape[2] + col


def rim_piece(block, width, dr, dc):
    rows, cols = block.shape[1], block.shape[2]
    row_span = {-1: (rows - width, rows), 0: (0, rows), 1: (0, width)}[dr]
    col_span = {-1: (cols - width, cols), 0: (0, cols), 1: (0, width)}[dc]
    return block[:, row_span[0] : row_span[1], col_span[0] : col_span[1]]


def from_neighbours(block, width, dim, from_section, sections_used):
    shape = sizes()
    parts = []
    for step in (-1, 0, 1):
        size = block.shape[dim]
        span = {-1: (size - width, size), 0: (0, size), 1: (0, width)}[step]
        piece = lax.slice_in_dim(block, span[0], span[1], axis=dim)
        if from_section == 0 and step == 0:
            parts.append(piece)
            continue
        pairs = []
        for s in sections_used:
            for r in range(shape[1]):
                for c in range(shape[2]):
                    source = [s + from_section, r, c]
                    source[dim] += step
                    if all(0 <= source[k] < shape[k] for k in range(3)):
                        pairs.append((flat_index(source, shape), flat_index((s, r, c), shape)))
        parts.append(lax.ppermute(piece, AXES, pairs))
    return jnp.concatenate(parts, axis=dim)


def with_rim(block, width, from_section, sections_used):
    rows_done = from_neighbours(block, width, 1, from_section, sections_used)
    return from_neighbours(rows_done, width, 2, 0, sections_used)


def inside_mask(tile_rows, tile_cols, width):
    image_rows = tile_rows * lax.axis_size("row")
    image_cols = tile_cols * lax.axis_size("col")
    rows = lax.axis_index("row") * tile_rows - width + jnp.arange(tile_rows + 2 * width)
    cols = lax.axis_index("col") * tile_cols - width + jnp.arange(tile_cols + 2 * width)
    row_ok = (rows >= 0) & (rows < image_rows)
    col_ok = (cols >= 0) & (cols < image_cols)
    return (row_ok[:, None] & col_ok[None, :])[None, :, :, None]


def convolve(padded, kernel):
    return lax.conv_general_dilated(
        padded,
        kernel,
        (1, 1),
        "VALID",
        dimension_numbers=("NHWC", "HWIO", "NHWC"),
        preferred_element_type=jnp.float32,
    )


def kernel_terms(padded, signal):
    terms = lax.conv_general_dilated(
        padded,
        signal,
        (1, 1),
        "VALID",
        dimension_numbers=("CHWN", "IHWO", "NHWC"),
        preferred_element_type=jnp.float32,
    )
    return jnp.transpose(terms, (1, 2, 0, 3))


def crop(block, width):
    return block[:, width : block.shape[1] - width, width : block.shape[2] - width]


def summed_over_tiles(grads):
    shape = sizes()
    halving, doubling = [], []
    for axis, dim in (("row", 1), ("col", 2)):
        distance = 1
        while distance < shape[dim]:
            (halving if distance == 1 else doubling).append((axis, distance))
            distance *= 2

    def exchange(values, axis, distance):
        count = lax.axis_size(axis)
        return lax.ppermute(values, axis, [(i, i ^ distance) for i in range(count)])

    current = grads.reshape(-1)
    kept = []
    for axis, distance in halving:
        half = current.shape[0] // 2
        upper = (lax.axis_index(axis) // distance) % 2 == 1
        low, high = current[:half], current[half:]
        send = jnp.where(upper, low, high).astype(jnp.bfloat16)
        mine = jnp.where(upper, high, low).astype(jnp.bfloat16)
        other = exchange(send, axis, distance)
        current = mine.astype(jnp.float32) + other.astype(jnp.float32)
        kept.append((axis, distance, upper))
    for axis, distance in doubling:
        rounded = current.astype(jnp.bfloat16)
        other = exchange(rounded, axis, distance)
        upper = (lax.axis_index(axis) // distance) % 2 == 1
        first = jnp.where(upper, other, rounded).astype(jnp.float32)
        second = jnp.where(upper, rounded, other).astype(jnp.float32)
        current = first + second
    current = current.astype(jnp.bfloat16)
    for axis, distance, upper in reversed(kept):
        other = exchange(current, axis, distance)
        current = jnp.where(
            upper, jnp.concatenate([other, current]), jnp.concatenate([current, other])
        )
    return current.astype(jnp.float32).reshape(grads.shape)


def local(checkpoints, kernels, cotangent, plan):
    sections_count, row_count, col_count = sizes()
    section_index = lax.axis_index("section")
    batches, tile_rows, tile_cols, channels = checkpoints.shape[1:]
    layer_count = kernels.shape[0]
    flipped = jnp.transpose(kernels[:, ::-1, ::-1], (0, 1, 2, 4, 3))
    inverse = jnp.sum(
        jnp.arange(batches)[:, None] * (plan[:, None] == jnp.arange(batches)[None, :]), axis=0
    )
    top_cotangent = jnp.take(cotangent, inverse, axis=0)

    deep = layer_count * (sections_count + 1) <= min(tile_rows, tile_cols)
    if deep and sections_count == 2 and batches % 2 == 0:
        return local_split(checkpoints, kernels, cotangent, plan)
    if deep:
        top_rim = [layer_count * (s + 1) for s in range(sections_count)]
    else:
        top_rim = [layer_count] * sections_count
    rim = top_rim[-1] + layer_count
    first = with_rim(checkpoints[0], rim, 0, range(sections_count))
    top_ext = with_rim(top_cotangent, top_rim[-1], 0, (sections_count - 1,))
    inputs_list = [first]
    current = first
    for layer_idx in range(layer_count):
        width = rim - layer_idx - 1
        current = jnp.tanh(convolve(current, kernels[layer_idx]))
        current = jnp.where(inside_mask(tile_rows, tile_cols, width), current, 0.0)
        current = current.astype(jnp.bfloat16)
        inputs_list.append(current)

    def backward(top_ext, top_width):
        gradient = top_ext.astype(jnp.float32)
        terms = [None] * layer_count
        for layer_idx in reversed(range(layer_count)):
            width = top_width - (layer_count - 1 - layer_idx)
            output = crop(inputs_list[layer_idx + 1], rim - layer_idx - 1 - width)
            output = output.astype(jnp.float32)
            signal = gradient * (1.0 - output * output)
            signal = jnp.where(inside_mask(tile_rows, tile_cols, width), signal, 0.0)
            signal = signal.astype(jnp.bfloat16)
            terms[layer_idx] = crop(signal, width)
            gradient = convolve(signal, flipped[layer_idx])
        return gradient.astype(jnp.bfloat16), terms

    def products(signals):
        return jnp.stack(
            [
                kernel_terms(crop(inputs_list[layer_idx], rim - layer_idx - 1), signals[layer_idx])
                for layer_idx in range(layer_count)
            ]
        )

    boundary = jnp.zeros((batches, tile_rows, tile_cols, channels), jnp.bfloat16)
    gathered = jnp.zeros((layer_count, 3, 3, channels, channels), jnp.float32)
    for tick in range(sections_count):
        active = sections_count - 1 - tick
        is_active = section_index == active
        if tick + 1 < sections_count or sections_count > 4:
            result, signals = backward(top_ext, top_rim[active])
        else:
            shapes = jax.eval_shape(lambda top: backward(top, top_rim[active]), top_ext)
            result, signals = lax.cond(
                is_active,
                lambda top: backward(top, top_rim[active]),
                lambda top: jax.tree.map(lambda v: jnp.zeros(v.shape, v.dtype), shapes),
                top_ext,
            )
        result_width = top_rim[active] - layer_count
        boundary = jnp.where(is_active, crop(result, result_width), boundary)
        if tick + 1 < sections_count:
            if deep:
                pairs = [
                    (flat_index((active, r, c), sizes()), flat_index((active - 1, r, c), sizes()))
                    for r in range(row_count)
                    for c in range(col_count)
                ]
                top_ext = lax.ppermute(result, AXES, pairs)
            else:
                top_ext = with_rim(result, layer_count, 1, (active - 1,))
        if sections_count > 4:
            terms = products(signals)
        else:
            terms = lax.cond(
                is_active, products, lambda unused: jnp.zeros_like(gathered), signals
            )
        gathered = jnp.where(is_active, terms, gathered)
    gathered = summed_over_tiles(gathered)
    kernel_grad = gathered / batches
    return (boundary[None], kernel_grad)


def section_chain(top_ext, top_width, inputs_list, rim, flipped_kernels, early=None):
    layer_count = len(flipped_kernels)
    tile_rows = inputs_list[0].shape[1] - 2 * rim
    tile_cols = inputs_list[0].shape[2] - 2 * rim
    gradient = top_ext.astype(jnp.float32)
    signals = [None] * layer_count
    for layer_idx in reversed(range(layer_count)):
        width = top_width - (layer_count - 1 - layer_idx)
        output = crop(inputs_list[layer_idx + 1], rim - layer_idx - 1 - width)
        output = output.astype(jnp.float32)
        signal = gradient * (1.0 - output * output)
        signal = jnp.where(inside_mask(tile_rows, tile_cols, width), signal, 0.0)
        signal = signal.astype(jnp.bfloat16)
        signals[layer_idx] = crop(signal, width)
        if early is not None and layer_idx == layer_count - 1:
            started = early(signals[layer_idx])
            signal, started = lax.optimization_barrier((signal, started))
        gradient = convolve(signal, flipped_kernels[layer_idx])
    if early is not None:
        return gradient.astype(jnp.bfloat16), signals, started
    return gradient.astype(jnp.bfloat16), signals


def local_split(checkpoints, kernels, cotangent, plan):
    section_index = lax.axis_index("section")
    batches, tile_rows, tile_cols, channels = checkpoints.shape[1:]
    layer_count = kernels.shape[0]
    half = batches // 2
    inverse = jnp.sum(
        jnp.arange(batches)[:, None] * (plan[:, None] == jnp.arange(batches)[None, :]), axis=0
    )
    top_cotangent = jnp.take(cotangent, inverse, axis=0)

    def swap(values):
        return lax.ppermute(values, "section", [(0, 1), (1, 0)])

    def by_section(mine, theirs, section):
        return jnp.where(section_index == section, mine, theirs)

    own = checkpoints[0]
    mine = lax.dynamic_slice_in_dim(own, section_index * half, half, 0)
    theirs = swap(lax.dynamic_slice_in_dim(own, (1 - section_index) * half, half, 0))
    other_kernels = swap(kernels)
    section_kernels = [by_section(kernels, other_kernels, s) for s in range(2)]

    top_rim = [layer_count * (s + 1) for s in range(2)]
    rims = [r + layer_count for r in top_rim]
    group_cotangent = lax.dynamic_slice_in_dim(top_cotangent, section_index * half, half, 0)
    stacked = [by_section(mine, theirs, s) for s in range(2)] + [group_cotangent]
    stacked = with_rim(jnp.concatenate(stacked, axis=0), rims[1], 0, range(2))
    firsts = [crop(stacked[:half], rims[1] - rims[0]), stacked[half : 2 * half]]
    top_ext = crop(stacked[2 * half :], rims[1] - top_rim[1])

    scale = 1.0 / batches

    def sum_input(section_one, section_zero):
        mine_terms = by_section(section_zero, section_one, 0)
        other_terms = by_section(section_one, section_zero, 0)
        other_terms = swap((other_terms * scale).astype(jnp.bfloat16)).astype(jnp.float32)
        return mine_terms * scale + other_terms

    results, partials = [None, None], [None, None]
    for s in (1, 0):
        rim = rims[s]
        inputs_list = [firsts[s]]
        current = firsts[s]
        for layer_idx in range(layer_count):
            current = jnp.tanh(convolve(current, section_kernels[s][layer_idx]))
            current = jnp.where(
                inside_mask(tile_rows, tile_cols, rim - layer_idx - 1), current, 0.0
            )
            current = current.astype(jnp.bfloat16)
            inputs_list.append(current)
        flipped = jnp.transpose(section_kernels[s][:, ::-1, ::-1], (0, 1, 2, 4, 3))

        def product(layer_idx, signal, inputs_list=inputs_list, rim=rim):
            return kernel_terms(crop(inputs_list[layer_idx], rim - layer_idx - 1), signal)

        if s == 1:
            top_ext, signals = section_chain(top_ext, top_rim[s], inputs_list, rim, flipped)
            partials[s] = [product(l, signals[l]) for l in range(layer_count)]
        else:
            top_ext, signals, early_total = section_chain(
                top_ext,
                top_rim[s],
                inputs_list,
                rim,
                flipped,
                lambda signal: sum_input(partials[1][-1], product(layer_count - 1, signal)),
            )
            partials[s] = [product(l, signals[l]) for l in range(layer_count - 1)] + [None]
        results[s] = crop(top_ext, top_rim[s] - layer_count)

    summed = [summed_over_tiles(sum_input(partials[1][l], partials[0][l])) for l in range(layer_count - 1)]
    gathered = jnp.stack(summed + [summed_over_tiles(early_total)])
    mine_back = by_section(results[0], results[1], 0)
    other_back = swap(by_section(results[1], results[0], 0))
    boundary = jnp.where(
        section_index == 0,
        jnp.concatenate([mine_back, other_back], axis=0),
        jnp.concatenate([other_back, mine_back], axis=0),
    )
    return (boundary[None], gathered)


def solution(mesh):
    return jax.shard_map(
        local,
        mesh=mesh,
        in_specs=(
            P("section", None, "row", "col", None),
            P("section", None, None, None, None),
            P(None, "row", "col", None),
            P(),
        ),
        out_specs=(P("section", None, "row", "col", None), P("section", None, None, None, None)),
        check_vma=False,
    )
```

```python
import jax
import jax.numpy as jnp
from jax import lax
from jax.sharding import PartitionSpec as P

AXES = ("section", "row", "col")


def sizes():
    return tuple(lax.axis_size(axis) for axis in AXES)


def flat_index(position, shape):
    section, row, col = position
    return (section * shape[1] + row) * shape[2] + col


def rim_piece(block, width, dr, dc):
    rows, cols = block.shape[1], block.shape[2]
    row_span = {-1: (rows - width, rows), 0: (0, rows), 1: (0, width)}[dr]
    col_span = {-1: (cols - width, cols), 0: (0, cols), 1: (0, width)}[dc]
    return block[:, row_span[0] : row_span[1], col_span[0] : col_span[1]]


def from_neighbours(block, width, dim, from_section, sections_used):
    shape = sizes()
    parts = []
    for step in (-1, 0, 1):
        size = block.shape[dim]
        span = {-1: (size - width, size), 0: (0, size), 1: (0, width)}[step]
        piece = lax.slice_in_dim(block, span[0], span[1], axis=dim)
        if from_section == 0 and step == 0:
            parts.append(piece)
            continue
        pairs = []
        for s in sections_used:
            for r in range(shape[1]):
                for c in range(shape[2]):
                    source = [s + from_section, r, c]
                    source[dim] += step
                    if all(0 <= source[k] < shape[k] for k in range(3)):
                        pairs.append((flat_index(source, shape), flat_index((s, r, c), shape)))
        parts.append(lax.ppermute(piece, AXES, pairs))
    return jnp.concatenate(parts, axis=dim)


def with_rim(block, width, from_section, sections_used):
    rows_done = from_neighbours(block, width, 1, from_section, sections_used)
    return from_neighbours(rows_done, width, 2, 0, sections_used)


def inside_mask(tile_rows, tile_cols, width):
    image_rows = tile_rows * lax.axis_size("row")
    image_cols = tile_cols * lax.axis_size("col")
    rows = lax.axis_index("row") * tile_rows - width + jnp.arange(tile_rows + 2 * width)
    cols = lax.axis_index("col") * tile_cols - width + jnp.arange(tile_cols + 2 * width)
    row_ok = (rows >= 0) & (rows < image_rows)
    col_ok = (cols >= 0) & (cols < image_cols)
    return (row_ok[:, None] & col_ok[None, :])[None, :, :, None]


def convolve(padded, kernel):
    return lax.conv_general_dilated(
        padded,
        kernel,
        (1, 1),
        "VALID",
        dimension_numbers=("NHWC", "HWIO", "NHWC"),
        preferred_element_type=jnp.float32,
    )


def kernel_terms(padded, signal):
    terms = lax.conv_general_dilated(
        padded,
        signal,
        (1, 1),
        "VALID",
        dimension_numbers=("CHWN", "IHWO", "NHWC"),
        preferred_element_type=jnp.float32,
    )
    return jnp.transpose(terms, (1, 2, 0, 3))


def crop(block, width):
    return block[:, width : block.shape[1] - width, width : block.shape[2] - width]


def summed_over_tiles(grads):
    shape = sizes()
    halving, doubling = [], []
    for axis, dim in (("row", 1), ("col", 2)):
        distance = 1
        while distance < shape[dim]:
            (halving if distance == 1 else doubling).append((axis, distance))
            distance *= 2

    def exchange(values, axis, distance):
        count = lax.axis_size(axis)
        return lax.ppermute(values, axis, [(i, i ^ distance) for i in range(count)])

    current = grads.reshape(-1)
    kept = []
    for axis, distance in halving:
        half = current.shape[0] // 2
        upper = (lax.axis_index(axis) // distance) % 2 == 1
        low, high = current[:half], current[half:]
        send = jnp.where(upper, low, high).astype(jnp.bfloat16)
        mine = jnp.where(upper, high, low).astype(jnp.bfloat16)
        other = exchange(send, axis, distance)
        current = mine.astype(jnp.float32) + other.astype(jnp.float32)
        kept.append((axis, distance, upper))
    for axis, distance in doubling:
        rounded = current.astype(jnp.bfloat16)
        other = exchange(rounded, axis, distance)
        upper = (lax.axis_index(axis) // distance) % 2 == 1
        first = jnp.where(upper, other, rounded).astype(jnp.float32)
        second = jnp.where(upper, rounded, other).astype(jnp.float32)
        current = first + second
    current = current.astype(jnp.bfloat16)
    for axis, distance, upper in reversed(kept):
        other = exchange(current, axis, distance)
        current = jnp.where(
            upper, jnp.concatenate([other, current]), jnp.concatenate([current, other])
        )
    return current.astype(jnp.float32).reshape(grads.shape)


def local(checkpoints, kernels, cotangent, plan):
    sections_count, row_count, col_count = sizes()
    section_index = lax.axis_index("section")
    batches, tile_rows, tile_cols, channels = checkpoints.shape[1:]
    layer_count = kernels.shape[0]
    flipped = jnp.transpose(kernels[:, ::-1, ::-1], (0, 1, 2, 4, 3))
    inverse = jnp.sum(
        jnp.arange(batches)[:, None] * (plan[:, None] == jnp.arange(batches)[None, :]), axis=0
    )
    top_cotangent = jnp.take(cotangent, inverse, axis=0)

    deep = layer_count * (sections_count + 1) <= min(tile_rows, tile_cols)
    if deep and sections_count == 2 and batches % 2 == 0:
        return local_split(checkpoints, kernels, cotangent, plan)
    if deep:
        top_rim = [layer_count * (s + 1) for s in range(sections_count)]
    else:
        top_rim = [layer_count] * sections_count
    rim = top_rim[-1] + layer_count
    first = with_rim(checkpoints[0], rim, 0, range(sections_count))
    top_ext = with_rim(top_cotangent, top_rim[-1], 0, (sections_count - 1,))
    inputs_list = [first]
    current = first
    for layer_idx in range(layer_count):
        width = rim - layer_idx - 1
        current = jnp.tanh(convolve(current, kernels[layer_idx]))
        current = jnp.where(inside_mask(tile_rows, tile_cols, width), current, 0.0)
        current = current.astype(jnp.bfloat16)
        inputs_list.append(current)

    def backward(top_ext, top_width):
        gradient = top_ext.astype(jnp.float32)
        terms = [None] * layer_count
        for layer_idx in reversed(range(layer_count)):
            width = top_width - (layer_count - 1 - layer_idx)
            output = crop(inputs_list[layer_idx + 1], rim - layer_idx - 1 - width)
            output = output.astype(jnp.float32)
            signal = gradient * (1.0 - output * output)
            signal = jnp.where(inside_mask(tile_rows, tile_cols, width), signal, 0.0)
            signal = signal.astype(jnp.bfloat16)
            terms[layer_idx] = crop(signal, width)
            gradient = convolve(signal, flipped[layer_idx])
        return gradient.astype(jnp.bfloat16), terms

    def products(signals):
        return jnp.stack(
            [
                kernel_terms(crop(inputs_list[layer_idx], rim - layer_idx - 1), signals[layer_idx])
                for layer_idx in range(layer_count)
            ]
        )

    boundary = jnp.zeros((batches, tile_rows, tile_cols, channels), jnp.bfloat16)
    gathered = jnp.zeros((layer_count, 3, 3, channels, channels), jnp.float32)
    for tick in range(sections_count):
        active = sections_count - 1 - tick
        is_active = section_index == active
        if tick + 1 < sections_count or sections_count > 4:
            result, signals = backward(top_ext, top_rim[active])
        else:
            shapes = jax.eval_shape(lambda top: backward(top, top_rim[active]), top_ext)
            result, signals = lax.cond(
                is_active,
                lambda top: backward(top, top_rim[active]),
                lambda top: jax.tree.map(lambda v: jnp.zeros(v.shape, v.dtype), shapes),
                top_ext,
            )
        result_width = top_rim[active] - layer_count
        boundary = jnp.where(is_active, crop(result, result_width), boundary)
        if tick + 1 < sections_count:
            if deep:
                pairs = [
                    (flat_index((active, r, c), sizes()), flat_index((active - 1, r, c), sizes()))
                    for r in range(row_count)
                    for c in range(col_count)
                ]
                top_ext = lax.ppermute(result, AXES, pairs)
            else:
                top_ext = with_rim(result, layer_count, 1, (active - 1,))
        if sections_count > 4:
            terms = products(signals)
        else:
            terms = lax.cond(
                is_active, products, lambda unused: jnp.zeros_like(gathered), signals
            )
        gathered = jnp.where(is_active, terms, gathered)
    gathered = summed_over_tiles(gathered)
    kernel_grad = gathered / batches
    return (boundary[None], kernel_grad)


def section_chain(top_ext, top_width, inputs_list, rim, flipped_kernels):
    layer_count = len(flipped_kernels)
    tile_rows = inputs_list[0].shape[1] - 2 * rim
    tile_cols = inputs_list[0].shape[2] - 2 * rim
    gradient = top_ext.astype(jnp.float32)
    signals = [None] * layer_count
    for layer_idx in reversed(range(layer_count)):
        width = top_width - (layer_count - 1 - layer_idx)
        output = crop(inputs_list[layer_idx + 1], rim - layer_idx - 1 - width)
        output = output.astype(jnp.float32)
        signal = gradient * (1.0 - output * output)
        signal = jnp.where(inside_mask(tile_rows, tile_cols, width), signal, 0.0)
        signal = signal.astype(jnp.bfloat16)
        signals[layer_idx] = crop(signal, width)
        gradient = convolve(signal, flipped_kernels[layer_idx])
    return gradient.astype(jnp.bfloat16), signals


def local_split(checkpoints, kernels, cotangent, plan):
    section_index = lax.axis_index("section")
    batches, tile_rows, tile_cols, channels = checkpoints.shape[1:]
    layer_count = kernels.shape[0]
    half = batches // 2
    inverse = jnp.sum(
        jnp.arange(batches)[:, None] * (plan[:, None] == jnp.arange(batches)[None, :]), axis=0
    )
    top_cotangent = jnp.take(cotangent, inverse, axis=0)

    def swap(values):
        return lax.ppermute(values, "section", [(0, 1), (1, 0)])

    def by_section(mine, theirs, section):
        return jnp.where(section_index == section, mine, theirs)

    own = checkpoints[0]
    mine = lax.dynamic_slice_in_dim(own, section_index * half, half, 0)
    theirs = swap(lax.dynamic_slice_in_dim(own, (1 - section_index) * half, half, 0))
    other_kernels = swap(kernels)
    section_kernels = [by_section(kernels, other_kernels, s) for s in range(2)]

    top_rim = [layer_count * (s + 1) for s in range(2)]
    rims = [r + layer_count for r in top_rim]
    group_cotangent = lax.dynamic_slice_in_dim(top_cotangent, section_index * half, half, 0)
    stacked = [by_section(mine, theirs, s) for s in range(2)] + [group_cotangent]
    stacked = jnp.concatenate(stacked, axis=0)
    middle = stacked.shape[0] // 2
    stacked = jnp.concatenate(
        [with_rim(stacked[:middle], rims[1], 0, range(2)),
         with_rim(stacked[middle:], rims[1], 0, range(2))],
        axis=0,
    )
    firsts = [crop(stacked[:half], rims[1] - rims[0]), stacked[half : 2 * half]]
    top_ext = crop(stacked[2 * half :], rims[1] - top_rim[1])

    results, partials = [None, None], [None, None]
    for s in (1, 0):
        rim = rims[s]
        inputs_list = [firsts[s]]
        current = firsts[s]
        for layer_idx in range(layer_count):
            current = jnp.tanh(convolve(current, section_kernels[s][layer_idx]))
            current = jnp.where(
                inside_mask(tile_rows, tile_cols, rim - layer_idx - 1), current, 0.0
            )
            current = current.astype(jnp.bfloat16)
            inputs_list.append(current)
        flipped = jnp.transpose(section_kernels[s][:, ::-1, ::-1], (0, 1, 2, 4, 3))
        top_ext, signals = section_chain(top_ext, top_rim[s], inputs_list, rim, flipped)
        results[s] = crop(top_ext, top_rim[s] - layer_count)
        partials[s] = [
            kernel_terms(crop(inputs_list[layer_idx], rim - layer_idx - 1), signals[layer_idx])
            for layer_idx in range(layer_count)
        ]

    scale = 1.0 / batches
    summed = []
    for layer_idx in reversed(range(layer_count)):
        mine_terms = by_section(partials[0][layer_idx], partials[1][layer_idx], 0)
        other_terms = by_section(partials[1][layer_idx], partials[0][layer_idx], 0)
        other_terms = swap((other_terms * scale).astype(jnp.bfloat16)).astype(jnp.float32)
        summed.insert(0, summed_over_tiles(mine_terms * scale + other_terms))
    gathered = jnp.stack(summed)
    mine_back = by_section(results[0], results[1], 0)
    other_back = swap(by_section(results[1], results[0], 0))
    boundary = jnp.where(
        section_index == 0,
        jnp.concatenate([mine_back, other_back], axis=0),
        jnp.concatenate([other_back, mine_back], axis=0),
    )
    return (boundary[None], gathered)


def solution(mesh):
    return jax.shard_map(
        local,
        mesh=mesh,
        in_specs=(
            P("section", None, "row", "col", None),
            P("section", None, None, None, None),
            P(None, "row", "col", None),
            P(),
        ),
        out_specs=(P("section", None, "row", "col", None), P("section", None, None, None, None)),
        check_vma=False,
    )
```

```python
import jax
import jax.numpy as jnp
from jax import lax
from jax.sharding import PartitionSpec as P

AXES = ("section", "row", "col")


def sizes():
    return tuple(lax.axis_size(axis) for axis in AXES)


def flat_index(position, shape):
    section, row, col = position
    return (section * shape[1] + row) * shape[2] + col


def rim_piece(block, width, dr, dc):
    rows, cols = block.shape[1], block.shape[2]
    row_span = {-1: (rows - width, rows), 0: (0, rows), 1: (0, width)}[dr]
    col_span = {-1: (cols - width, cols), 0: (0, cols), 1: (0, width)}[dc]
    return block[:, row_span[0] : row_span[1], col_span[0] : col_span[1]]


def from_neighbours(block, width, dim, from_section, sections_used):
    shape = sizes()
    parts = []
    for step in (-1, 0, 1):
        size = block.shape[dim]
        span = {-1: (size - width, size), 0: (0, size), 1: (0, width)}[step]
        piece = lax.slice_in_dim(block, span[0], span[1], axis=dim)
        if from_section == 0 and step == 0:
            parts.append(piece)
            continue
        pairs = []
        for s in sections_used:
            for r in range(shape[1]):
                for c in range(shape[2]):
                    source = [s + from_section, r, c]
                    source[dim] += step
                    if all(0 <= source[k] < shape[k] for k in range(3)):
                        pairs.append((flat_index(source, shape), flat_index((s, r, c), shape)))
        parts.append(lax.ppermute(piece, AXES, pairs))
    return jnp.concatenate(parts, axis=dim)


def with_rim(block, width, from_section, sections_used):
    rows_done = from_neighbours(block, width, 1, from_section, sections_used)
    return from_neighbours(rows_done, width, 2, 0, sections_used)


def inside_mask(tile_rows, tile_cols, width):
    image_rows = tile_rows * lax.axis_size("row")
    image_cols = tile_cols * lax.axis_size("col")
    rows = lax.axis_index("row") * tile_rows - width + jnp.arange(tile_rows + 2 * width)
    cols = lax.axis_index("col") * tile_cols - width + jnp.arange(tile_cols + 2 * width)
    row_ok = (rows >= 0) & (rows < image_rows)
    col_ok = (cols >= 0) & (cols < image_cols)
    return (row_ok[:, None] & col_ok[None, :])[None, :, :, None]


def convolve(padded, kernel):
    return lax.conv_general_dilated(
        padded,
        kernel,
        (1, 1),
        "VALID",
        dimension_numbers=("NHWC", "HWIO", "NHWC"),
        preferred_element_type=jnp.float32,
    )


def kernel_terms(padded, signal):
    terms = lax.conv_general_dilated(
        padded,
        signal,
        (1, 1),
        "VALID",
        dimension_numbers=("CHWN", "IHWO", "NHWC"),
        preferred_element_type=jnp.float32,
    )
    return jnp.transpose(terms, (1, 2, 0, 3))


def crop(block, width):
    return block[:, width : block.shape[1] - width, width : block.shape[2] - width]


def summed_over_tiles(grads):
    shape = sizes()
    halving, doubling = [], []
    for axis, dim in (("row", 1), ("col", 2)):
        distance = 1
        while distance < shape[dim]:
            (halving if axis == "row" else doubling).append((axis, distance))
            distance *= 2

    def exchange(values, axis, distance):
        count = lax.axis_size(axis)
        return lax.ppermute(values, axis, [(i, i ^ distance) for i in range(count)])

    current = grads.reshape(-1)
    kept = []
    for axis, distance in halving:
        half = current.shape[0] // 2
        upper = (lax.axis_index(axis) // distance) % 2 == 1
        low, high = current[:half], current[half:]
        send = jnp.where(upper, low, high).astype(jnp.bfloat16)
        mine = jnp.where(upper, high, low).astype(jnp.bfloat16)
        other = exchange(send, axis, distance)
        current = mine.astype(jnp.float32) + other.astype(jnp.float32)
        kept.append((axis, distance, upper))
    for axis, distance in doubling:
        rounded = current.astype(jnp.bfloat16)
        other = exchange(rounded, axis, distance)
        upper = (lax.axis_index(axis) // distance) % 2 == 1
        first = jnp.where(upper, other, rounded).astype(jnp.float32)
        second = jnp.where(upper, rounded, other).astype(jnp.float32)
        current = first + second
    current = current.astype(jnp.bfloat16)
    for axis, distance, upper in reversed(kept):
        other = exchange(current, axis, distance)
        current = jnp.where(
            upper, jnp.concatenate([other, current]), jnp.concatenate([current, other])
        )
    return current.astype(jnp.float32).reshape(grads.shape)


def local(checkpoints, kernels, cotangent, plan):
    sections_count, row_count, col_count = sizes()
    section_index = lax.axis_index("section")
    batches, tile_rows, tile_cols, channels = checkpoints.shape[1:]
    layer_count = kernels.shape[0]
    flipped = jnp.transpose(kernels[:, ::-1, ::-1], (0, 1, 2, 4, 3))
    inverse = jnp.sum(
        jnp.arange(batches)[:, None] * (plan[:, None] == jnp.arange(batches)[None, :]), axis=0
    )
    top_cotangent = jnp.take(cotangent, inverse, axis=0)

    deep = layer_count * (sections_count + 1) <= min(tile_rows, tile_cols)
    if deep and sections_count == 2 and batches % 2 == 0:
        return local_split(checkpoints, kernels, cotangent, plan)
    if deep:
        top_rim = [layer_count * (s + 1) for s in range(sections_count)]
    else:
        top_rim = [layer_count] * sections_count
    rim = top_rim[-1] + layer_count
    first = with_rim(checkpoints[0], rim, 0, range(sections_count))
    top_ext = with_rim(top_cotangent, top_rim[-1], 0, (sections_count - 1,))
    inputs_list = [first]
    current = first
    for layer_idx in range(layer_count):
        width = rim - layer_idx - 1
        current = jnp.tanh(convolve(current, kernels[layer_idx]))
        current = jnp.where(inside_mask(tile_rows, tile_cols, width), current, 0.0)
        current = current.astype(jnp.bfloat16)
        inputs_list.append(current)

    def backward(top_ext, top_width):
        gradient = top_ext.astype(jnp.float32)
        terms = [None] * layer_count
        for layer_idx in reversed(range(layer_count)):
            width = top_width - (layer_count - 1 - layer_idx)
            output = crop(inputs_list[layer_idx + 1], rim - layer_idx - 1 - width)
            output = output.astype(jnp.float32)
            signal = gradient * (1.0 - output * output)
            signal = jnp.where(inside_mask(tile_rows, tile_cols, width), signal, 0.0)
            signal = signal.astype(jnp.bfloat16)
            terms[layer_idx] = crop(signal, width)
            gradient = convolve(signal, flipped[layer_idx])
        return gradient.astype(jnp.bfloat16), terms

    def products(signals):
        return jnp.stack(
            [
                kernel_terms(crop(inputs_list[layer_idx], rim - layer_idx - 1), signals[layer_idx])
                for layer_idx in range(layer_count)
            ]
        )

    boundary = jnp.zeros((batches, tile_rows, tile_cols, channels), jnp.bfloat16)
    gathered = jnp.zeros((layer_count, 3, 3, channels, channels), jnp.float32)
    for tick in range(sections_count):
        active = sections_count - 1 - tick
        is_active = section_index == active
        if tick + 1 < sections_count or sections_count > 4:
            result, signals = backward(top_ext, top_rim[active])
        else:
            shapes = jax.eval_shape(lambda top: backward(top, top_rim[active]), top_ext)
            result, signals = lax.cond(
                is_active,
                lambda top: backward(top, top_rim[active]),
                lambda top: jax.tree.map(lambda v: jnp.zeros(v.shape, v.dtype), shapes),
                top_ext,
            )
        result_width = top_rim[active] - layer_count
        boundary = jnp.where(is_active, crop(result, result_width), boundary)
        if tick + 1 < sections_count:
            if deep:
                pairs = [
                    (flat_index((active, r, c), sizes()), flat_index((active - 1, r, c), sizes()))
                    for r in range(row_count)
                    for c in range(col_count)
                ]
                top_ext = lax.ppermute(result, AXES, pairs)
            else:
                top_ext = with_rim(result, layer_count, 1, (active - 1,))
        if sections_count > 4:
            terms = products(signals)
        else:
            terms = lax.cond(
                is_active, products, lambda unused: jnp.zeros_like(gathered), signals
            )
        gathered = jnp.where(is_active, terms, gathered)
    gathered = summed_over_tiles(gathered)
    kernel_grad = gathered / batches
    return (boundary[None], kernel_grad)


def section_chain(top_ext, top_width, inputs_list, rim, flipped_kernels):
    layer_count = len(flipped_kernels)
    tile_rows = inputs_list[0].shape[1] - 2 * rim
    tile_cols = inputs_list[0].shape[2] - 2 * rim
    gradient = top_ext.astype(jnp.float32)
    signals = [None] * layer_count
    for layer_idx in reversed(range(layer_count)):
        width = top_width - (layer_count - 1 - layer_idx)
        output = crop(inputs_list[layer_idx + 1], rim - layer_idx - 1 - width)
        output = output.astype(jnp.float32)
        signal = gradient * (1.0 - output * output)
        signal = jnp.where(inside_mask(tile_rows, tile_cols, width), signal, 0.0)
        signal = signal.astype(jnp.bfloat16)
        signals[layer_idx] = crop(signal, width)
        gradient = convolve(signal, flipped_kernels[layer_idx])
    return gradient.astype(jnp.bfloat16), signals


def local_split(checkpoints, kernels, cotangent, plan):
    section_index = lax.axis_index("section")
    batches, tile_rows, tile_cols, channels = checkpoints.shape[1:]
    layer_count = kernels.shape[0]
    half = batches // 2
    inverse = jnp.sum(
        jnp.arange(batches)[:, None] * (plan[:, None] == jnp.arange(batches)[None, :]), axis=0
    )
    top_cotangent = jnp.take(cotangent, inverse, axis=0)

    def swap(values):
        return lax.ppermute(values, "section", [(0, 1), (1, 0)])

    def by_section(mine, theirs, section):
        return jnp.where(section_index == section, mine, theirs)

    own = checkpoints[0]
    mine = lax.dynamic_slice_in_dim(own, section_index * half, half, 0)
    theirs = swap(lax.dynamic_slice_in_dim(own, (1 - section_index) * half, half, 0))
    other_kernels = swap(kernels)
    section_kernels = [by_section(kernels, other_kernels, s) for s in range(2)]

    top_rim = [layer_count * (s + 1) for s in range(2)]
    rims = [r + layer_count for r in top_rim]
    group_cotangent = lax.dynamic_slice_in_dim(top_cotangent, section_index * half, half, 0)
    stacked = [by_section(mine, theirs, s) for s in range(2)] + [group_cotangent]
    stacked = with_rim(jnp.concatenate(stacked, axis=0), rims[1], 0, range(2))
    firsts = [crop(stacked[:half], rims[1] - rims[0]), stacked[half : 2 * half]]
    top_ext = crop(stacked[2 * half :], rims[1] - top_rim[1])

    results, partials = [None, None], [None, None]
    for s in (1, 0):
        rim = rims[s]
        inputs_list = [firsts[s]]
        current = firsts[s]
        for layer_idx in range(layer_count):
            current = jnp.tanh(convolve(current, section_kernels[s][layer_idx]))
            current = jnp.where(
                inside_mask(tile_rows, tile_cols, rim - layer_idx - 1), current, 0.0
            )
            current = current.astype(jnp.bfloat16)
            inputs_list.append(current)
        flipped = jnp.transpose(section_kernels[s][:, ::-1, ::-1], (0, 1, 2, 4, 3))
        top_ext, signals = section_chain(top_ext, top_rim[s], inputs_list, rim, flipped)
        results[s] = crop(top_ext, top_rim[s] - layer_count)
        partials[s] = [
            kernel_terms(crop(inputs_list[layer_idx], rim - layer_idx - 1), signals[layer_idx])
            for layer_idx in range(layer_count)
        ]

    scale = 1.0 / batches
    summed = []
    for layer_idx in reversed(range(layer_count)):
        mine_terms = by_section(partials[0][layer_idx], partials[1][layer_idx], 0)
        other_terms = by_section(partials[1][layer_idx], partials[0][layer_idx], 0)
        other_terms = swap((other_terms * scale).astype(jnp.bfloat16)).astype(jnp.float32)
        summed.insert(0, summed_over_tiles(mine_terms * scale + other_terms))
    gathered = jnp.stack(summed)
    mine_back = by_section(results[0], results[1], 0)
    other_back = swap(by_section(results[1], results[0], 0))
    boundary = jnp.where(
        section_index == 0,
        jnp.concatenate([mine_back, other_back], axis=0),
        jnp.concatenate([other_back, mine_back], axis=0),
    )
    return (boundary[None], gathered)


def solution(mesh):
    return jax.shard_map(
        local,
        mesh=mesh,
        in_specs=(
            P("section", None, "row", "col", None),
            P("section", None, None, None, None),
            P(None, "row", "col", None),
            P(),
        ),
        out_specs=(P("section", None, "row", "col", None), P("section", None, None, None, None)),
        check_vma=False,
    )
```

```python
import jax
import jax.numpy as jnp
from jax import lax
from jax.sharding import PartitionSpec as P

AXES = ("section", "row", "col")


def sizes():
    return tuple(lax.axis_size(axis) for axis in AXES)


def flat_index(position, shape):
    section, row, col = position
    return (section * shape[1] + row) * shape[2] + col


def rim_piece(block, width, dr, dc):
    rows, cols = block.shape[1], block.shape[2]
    row_span = {-1: (rows - width, rows), 0: (0, rows), 1: (0, width)}[dr]
    col_span = {-1: (cols - width, cols), 0: (0, cols), 1: (0, width)}[dc]
    return block[:, row_span[0] : row_span[1], col_span[0] : col_span[1]]


def from_neighbours(block, width, dim, from_section, sections_used):
    shape = sizes()
    parts = []
    for step in (-1, 0, 1):
        size = block.shape[dim]
        span = {-1: (size - width, size), 0: (0, size), 1: (0, width)}[step]
        piece = lax.slice_in_dim(block, span[0], span[1], axis=dim)
        if from_section == 0 and step == 0:
            parts.append(piece)
            continue
        pairs = []
        for s in sections_used:
            for r in range(shape[1]):
                for c in range(shape[2]):
                    source = [s + from_section, r, c]
                    source[dim] += step
                    if all(0 <= source[k] < shape[k] for k in range(3)):
                        pairs.append((flat_index(source, shape), flat_index((s, r, c), shape)))
        parts.append(lax.ppermute(piece, AXES, pairs))
    return jnp.concatenate(parts, axis=dim)


def with_rim(block, width, from_section, sections_used):
    rows_done = from_neighbours(block, width, 1, from_section, sections_used)
    return from_neighbours(rows_done, width, 2, 0, sections_used)


def inside_mask(tile_rows, tile_cols, width):
    image_rows = tile_rows * lax.axis_size("row")
    image_cols = tile_cols * lax.axis_size("col")
    rows = lax.axis_index("row") * tile_rows - width + jnp.arange(tile_rows + 2 * width)
    cols = lax.axis_index("col") * tile_cols - width + jnp.arange(tile_cols + 2 * width)
    row_ok = (rows >= 0) & (rows < image_rows)
    col_ok = (cols >= 0) & (cols < image_cols)
    return (row_ok[:, None] & col_ok[None, :])[None, :, :, None]


def convolve(padded, kernel):
    return lax.conv_general_dilated(
        padded,
        kernel,
        (1, 1),
        "VALID",
        dimension_numbers=("NHWC", "HWIO", "NHWC"),
        preferred_element_type=jnp.float32,
    )


def kernel_terms(padded, signal):
    terms = lax.conv_general_dilated(
        padded,
        signal,
        (1, 1),
        "VALID",
        dimension_numbers=("CHWN", "IHWO", "NHWC"),
        preferred_element_type=jnp.float32,
    )
    return jnp.transpose(terms, (1, 2, 0, 3))


def crop(block, width):
    return block[:, width : block.shape[1] - width, width : block.shape[2] - width]


def summed_over_tiles(grads):
    shape = sizes()
    halving, doubling = [], []
    for axis, dim in (("row", 1), ("col", 2)):
        distance = 1
        while distance < shape[dim]:
            (halving if distance == 1 else doubling).append((axis, distance))
            distance *= 2

    def exchange(values, axis, distance):
        count = lax.axis_size(axis)
        return lax.ppermute(values, axis, [(i, i ^ distance) for i in range(count)])

    current = grads.reshape(-1)
    kept = []
    for axis, distance in halving:
        half = current.shape[0] // 2
        upper = (lax.axis_index(axis) // distance) % 2 == 1
        low, high = current[:half], current[half:]
        send = jnp.where(upper, low, high).astype(jnp.bfloat16)
        mine = jnp.where(upper, high, low).astype(jnp.bfloat16)
        other = exchange(send, axis, distance)
        current = mine.astype(jnp.float32) + other.astype(jnp.float32)
        kept.append((axis, distance, upper))
    for axis, distance in doubling:
        rounded = current.astype(jnp.bfloat16)
        other = exchange(rounded, axis, distance)
        upper = (lax.axis_index(axis) // distance) % 2 == 1
        first = jnp.where(upper, other, rounded).astype(jnp.float32)
        second = jnp.where(upper, rounded, other).astype(jnp.float32)
        current = first + second
    current = current.astype(jnp.bfloat16)
    for axis, distance, upper in reversed(kept):
        other = exchange(current, axis, distance)
        current = jnp.where(
            upper, jnp.concatenate([other, current]), jnp.concatenate([current, other])
        )
    return current.astype(jnp.float32).reshape(grads.shape)


def local(checkpoints, kernels, cotangent, plan):
    sections_count, row_count, col_count = sizes()
    section_index = lax.axis_index("section")
    batches, tile_rows, tile_cols, channels = checkpoints.shape[1:]
    layer_count = kernels.shape[0]
    flipped = jnp.transpose(kernels[:, ::-1, ::-1], (0, 1, 2, 4, 3))
    inverse = jnp.sum(
        jnp.arange(batches)[:, None] * (plan[:, None] == jnp.arange(batches)[None, :]), axis=0
    )
    top_cotangent = jnp.take(cotangent, inverse, axis=0)

    deep = layer_count * (sections_count + 1) <= min(tile_rows, tile_cols)
    if deep and sections_count == 2 and batches % 2 == 0:
        return local_split(checkpoints, kernels, cotangent, plan)
    if deep:
        top_rim = [layer_count * (s + 1) for s in range(sections_count)]
    else:
        top_rim = [layer_count] * sections_count
    rim = top_rim[-1] + layer_count
    first = with_rim(checkpoints[0], rim, 0, range(sections_count))
    top_ext = with_rim(top_cotangent, top_rim[-1], 0, (sections_count - 1,))
    inputs_list = [first]
    current = first
    for layer_idx in range(layer_count):
        width = rim - layer_idx - 1
        current = jnp.tanh(convolve(current, kernels[layer_idx]))
        current = jnp.where(inside_mask(tile_rows, tile_cols, width), current, 0.0)
        current = current.astype(jnp.bfloat16)
        inputs_list.append(current)

    def backward(top_ext, top_width):
        gradient = top_ext.astype(jnp.float32)
        terms = [None] * layer_count
        for layer_idx in reversed(range(layer_count)):
            width = top_width - (layer_count - 1 - layer_idx)
            output = crop(inputs_list[layer_idx + 1], rim - layer_idx - 1 - width)
            output = output.astype(jnp.float32)
            signal = gradient * (1.0 - output * output)
            signal = jnp.where(inside_mask(tile_rows, tile_cols, width), signal, 0.0)
            signal = signal.astype(jnp.bfloat16)
            terms[layer_idx] = crop(signal, width)
            gradient = convolve(signal, flipped[layer_idx])
        return gradient.astype(jnp.bfloat16), terms

    def products(signals):
        return jnp.stack(
            [
                kernel_terms(crop(inputs_list[layer_idx], rim - layer_idx - 1), signals[layer_idx])
                for layer_idx in range(layer_count)
            ]
        )

    boundary = jnp.zeros((batches, tile_rows, tile_cols, channels), jnp.bfloat16)
    gathered = jnp.zeros((layer_count, 3, 3, channels, channels), jnp.float32)
    for tick in range(sections_count):
        active = sections_count - 1 - tick
        is_active = section_index == active
        if tick + 1 < sections_count or sections_count > 4:
            result, signals = backward(top_ext, top_rim[active])
        else:
            shapes = jax.eval_shape(lambda top: backward(top, top_rim[active]), top_ext)
            result, signals = lax.cond(
                is_active,
                lambda top: backward(top, top_rim[active]),
                lambda top: jax.tree.map(lambda v: jnp.zeros(v.shape, v.dtype), shapes),
                top_ext,
            )
        result_width = top_rim[active] - layer_count
        boundary = jnp.where(is_active, crop(result, result_width), boundary)
        if tick + 1 < sections_count:
            if deep:
                pairs = [
                    (flat_index((active, r, c), sizes()), flat_index((active - 1, r, c), sizes()))
                    for r in range(row_count)
                    for c in range(col_count)
                ]
                top_ext = lax.ppermute(result, AXES, pairs)
            else:
                top_ext = with_rim(result, layer_count, 1, (active - 1,))
        if sections_count > 4:
            terms = products(signals)
        else:
            terms = lax.cond(
                is_active, products, lambda unused: jnp.zeros_like(gathered), signals
            )
        gathered = jnp.where(is_active, terms, gathered)
    gathered = summed_over_tiles(gathered)
    kernel_grad = gathered / batches
    return (boundary[None], kernel_grad)


def section_chain(top_ext, top_width, inputs_list, rim, flipped_kernels):
    layer_count = len(flipped_kernels)
    tile_rows = inputs_list[0].shape[1] - 2 * rim
    tile_cols = inputs_list[0].shape[2] - 2 * rim
    gradient = top_ext.astype(jnp.float32)
    signals = [None] * layer_count
    for layer_idx in reversed(range(layer_count)):
        width = top_width - (layer_count - 1 - layer_idx)
        output = crop(inputs_list[layer_idx + 1], rim - layer_idx - 1 - width)
        output = output.astype(jnp.float32)
        signal = gradient * (1.0 - output * output)
        signal = jnp.where(inside_mask(tile_rows, tile_cols, width), signal, 0.0)
        signal = signal.astype(jnp.bfloat16)
        signals[layer_idx] = crop(signal, width)
        gradient = convolve(signal, flipped_kernels[layer_idx])
    return gradient.astype(jnp.bfloat16), signals


def local_split(checkpoints, kernels, cotangent, plan):
    section_index = lax.axis_index("section")
    batches, tile_rows, tile_cols, channels = checkpoints.shape[1:]
    layer_count = kernels.shape[0]
    half = batches // 2
    inverse = jnp.sum(
        jnp.arange(batches)[:, None] * (plan[:, None] == jnp.arange(batches)[None, :]), axis=0
    )
    top_cotangent = jnp.take(cotangent, inverse, axis=0)

    def swap(values):
        return lax.ppermute(values, "section", [(0, 1), (1, 0)])

    def by_section(mine, theirs, section):
        return jnp.where(section_index == section, mine, theirs)

    own = checkpoints[0]
    mine = lax.dynamic_slice_in_dim(own, section_index * half, half, 0)
    theirs = swap(lax.dynamic_slice_in_dim(own, (1 - section_index) * half, half, 0))
    other_kernels = swap(kernels)
    section_kernels = [by_section(kernels, other_kernels, s) for s in range(2)]

    top_rim = [layer_count * (s + 1) for s in range(2)]
    rims = [r + layer_count for r in top_rim]
    group_cotangent = lax.dynamic_slice_in_dim(top_cotangent, section_index * half, half, 0)
    stacked = [by_section(mine, theirs, s) for s in range(2)] + [group_cotangent]
    stacked = with_rim(jnp.concatenate(stacked, axis=0), rims[1], 0, range(2))
    firsts = [crop(stacked[:half], rims[1] - rims[0]), stacked[half : 2 * half]]
    top_ext = crop(stacked[2 * half :], rims[1] - top_rim[1])

    results, partials = [None, None], [None, None]
    for s in (1, 0):
        rim = rims[s]
        inputs_list = [firsts[s]]
        current = firsts[s]
        for layer_idx in range(layer_count):
            current = jnp.tanh(convolve(current, section_kernels[s][layer_idx]))
            current = jnp.where(
                inside_mask(tile_rows, tile_cols, rim - layer_idx - 1), current, 0.0
            )
            current = current.astype(jnp.bfloat16)
            inputs_list.append(current)
        flipped = jnp.transpose(section_kernels[s][:, ::-1, ::-1], (0, 1, 2, 4, 3))
        top_ext, signals = section_chain(top_ext, top_rim[s], inputs_list, rim, flipped)
        results[s] = crop(top_ext, top_rim[s] - layer_count)
        partials[s] = [
            kernel_terms(crop(inputs_list[layer_idx], rim - layer_idx - 1), signals[layer_idx])
            for layer_idx in range(layer_count)
        ]

    scale = 1.0 / batches
    mine_terms = by_section(jnp.stack(partials[0]), jnp.stack(partials[1]), 0)
    other_terms = by_section(jnp.stack(partials[1]), jnp.stack(partials[0]), 0)
    other_terms = swap((other_terms * scale).astype(jnp.bfloat16)).astype(jnp.float32)
    total = mine_terms * scale + other_terms
    gathered = jnp.stack([summed_over_tiles(total[layer_idx]) for layer_idx in range(layer_count)])
    mine_back = by_section(results[0], results[1], 0)
    other_back = swap(by_section(results[1], results[0], 0))
    boundary = jnp.where(
        section_index == 0,
        jnp.concatenate([mine_back, other_back], axis=0),
        jnp.concatenate([other_back, mine_back], axis=0),
    )
    return (boundary[None], gathered)


def solution(mesh):
    return jax.shard_map(
        local,
        mesh=mesh,
        in_specs=(
            P("section", None, "row", "col", None),
            P("section", None, None, None, None),
            P(None, "row", "col", None),
            P(),
        ),
        out_specs=(P("section", None, "row", "col", None), P("section", None, None, None, None)),
        check_vma=False,
    )
```

```python
import jax
import jax.numpy as jnp
from jax import lax
from jax.sharding import PartitionSpec as P

AXES = ("section", "row", "col")


def sizes():
    return tuple(lax.axis_size(axis) for axis in AXES)


def flat_index(position, shape):
    section, row, col = position
    return (section * shape[1] + row) * shape[2] + col


def rim_piece(block, width, dr, dc):
    rows, cols = block.shape[1], block.shape[2]
    row_span = {-1: (rows - width, rows), 0: (0, rows), 1: (0, width)}[dr]
    col_span = {-1: (cols - width, cols), 0: (0, cols), 1: (0, width)}[dc]
    return block[:, row_span[0] : row_span[1], col_span[0] : col_span[1]]


def from_neighbours(block, width, dim, from_section, sections_used):
    shape = sizes()
    parts = []
    for step in (-1, 0, 1):
        size = block.shape[dim]
        span = {-1: (size - width, size), 0: (0, size), 1: (0, width)}[step]
        piece = lax.slice_in_dim(block, span[0], span[1], axis=dim)
        if from_section == 0 and step == 0:
            parts.append(piece)
            continue
        pairs = []
        for s in sections_used:
            for r in range(shape[1]):
                for c in range(shape[2]):
                    source = [s + from_section, r, c]
                    source[dim] += step
                    if all(0 <= source[k] < shape[k] for k in range(3)):
                        pairs.append((flat_index(source, shape), flat_index((s, r, c), shape)))
        parts.append(lax.ppermute(piece, AXES, pairs))
    return jnp.concatenate(parts, axis=dim)


def with_rim(block, width, from_section, sections_used):
    rows_done = from_neighbours(block, width, 1, from_section, sections_used)
    return from_neighbours(rows_done, width, 2, 0, sections_used)


def inside_mask(tile_rows, tile_cols, width):
    image_rows = tile_rows * lax.axis_size("row")
    image_cols = tile_cols * lax.axis_size("col")
    rows = lax.axis_index("row") * tile_rows - width + jnp.arange(tile_rows + 2 * width)
    cols = lax.axis_index("col") * tile_cols - width + jnp.arange(tile_cols + 2 * width)
    row_ok = (rows >= 0) & (rows < image_rows)
    col_ok = (cols >= 0) & (cols < image_cols)
    return (row_ok[:, None] & col_ok[None, :])[None, :, :, None]


def convolve(padded, kernel):
    return lax.conv_general_dilated(
        padded,
        kernel,
        (1, 1),
        "VALID",
        dimension_numbers=("NHWC", "HWIO", "NHWC"),
        preferred_element_type=jnp.float32,
    )


def kernel_terms(padded, signal):
    terms = lax.conv_general_dilated(
        padded,
        signal,
        (1, 1),
        "VALID",
        dimension_numbers=("CHWN", "IHWO", "NHWC"),
        preferred_element_type=jnp.float32,
    )
    return jnp.transpose(terms, (1, 2, 0, 3))


def crop(block, width):
    return block[:, width : block.shape[1] - width, width : block.shape[2] - width]


def summed_over_tiles(grads):
    shape = sizes()
    halving, doubling = [], []
    for axis, dim in (("row", 1), ("col", 2)):
        distance = 1
        while distance < shape[dim]:
            (halving if distance == 1 else doubling).append((axis, distance))
            distance *= 2

    def exchange(values, axis, distance):
        count = lax.axis_size(axis)
        return lax.ppermute(values, axis, [(i, i ^ distance) for i in range(count)])

    current = grads.reshape(-1)
    kept = []
    for axis, distance in halving:
        half = current.shape[0] // 2
        upper = (lax.axis_index(axis) // distance) % 2 == 1
        low, high = current[:half], current[half:]
        send = jnp.where(upper, low, high).astype(jnp.bfloat16)
        mine = jnp.where(upper, high, low).astype(jnp.bfloat16)
        other = exchange(send, axis, distance)
        current = mine.astype(jnp.float32) + other.astype(jnp.float32)
        kept.append((axis, distance, upper))
    for axis, distance in doubling:
        rounded = current.astype(jnp.bfloat16)
        other = exchange(rounded, axis, distance)
        upper = (lax.axis_index(axis) // distance) % 2 == 1
        first = jnp.where(upper, other, rounded).astype(jnp.float32)
        second = jnp.where(upper, rounded, other).astype(jnp.float32)
        current = first + second
    current = current.astype(jnp.bfloat16)
    for axis, distance, upper in reversed(kept):
        other = exchange(current, axis, distance)
        current = jnp.where(
            upper, jnp.concatenate([other, current]), jnp.concatenate([current, other])
        )
    return current.astype(jnp.float32).reshape(grads.shape)


def local(checkpoints, kernels, cotangent, plan):
    sections_count, row_count, col_count = sizes()
    section_index = lax.axis_index("section")
    batches, tile_rows, tile_cols, channels = checkpoints.shape[1:]
    layer_count = kernels.shape[0]
    flipped = jnp.transpose(kernels[:, ::-1, ::-1], (0, 1, 2, 4, 3))
    inverse = jnp.sum(
        jnp.arange(batches)[:, None] * (plan[:, None] == jnp.arange(batches)[None, :]), axis=0
    )
    top_cotangent = jnp.take(cotangent, inverse, axis=0)

    deep = layer_count * (sections_count + 1) <= min(tile_rows, tile_cols)
    if deep and sections_count == 2 and batches % 2 == 0:
        return local_split(checkpoints, kernels, cotangent, plan)
    if deep:
        top_rim = [layer_count * (s + 1) for s in range(sections_count)]
    else:
        top_rim = [layer_count] * sections_count
    rim = top_rim[-1] + layer_count
    first = with_rim(checkpoints[0], rim, 0, range(sections_count))
    top_ext = with_rim(top_cotangent, top_rim[-1], 0, (sections_count - 1,))
    inputs_list = [first]
    current = first
    for layer_idx in range(layer_count):
        width = rim - layer_idx - 1
        current = jnp.tanh(convolve(current, kernels[layer_idx]))
        current = jnp.where(inside_mask(tile_rows, tile_cols, width), current, 0.0)
        current = current.astype(jnp.bfloat16)
        inputs_list.append(current)

    def backward(top_ext, top_width):
        gradient = top_ext.astype(jnp.float32)
        terms = [None] * layer_count
        for layer_idx in reversed(range(layer_count)):
            width = top_width - (layer_count - 1 - layer_idx)
            output = crop(inputs_list[layer_idx + 1], rim - layer_idx - 1 - width)
            output = output.astype(jnp.float32)
            signal = gradient * (1.0 - output * output)
            signal = jnp.where(inside_mask(tile_rows, tile_cols, width), signal, 0.0)
            signal = signal.astype(jnp.bfloat16)
            terms[layer_idx] = crop(signal, width)
            gradient = convolve(signal, flipped[layer_idx])
        return gradient.astype(jnp.bfloat16), terms

    def products(signals):
        return jnp.stack(
            [
                kernel_terms(crop(inputs_list[layer_idx], rim - layer_idx - 1), signals[layer_idx])
                for layer_idx in range(layer_count)
            ]
        )

    boundary = jnp.zeros((batches, tile_rows, tile_cols, channels), jnp.bfloat16)
    gathered = jnp.zeros((layer_count, 3, 3, channels, channels), jnp.float32)
    for tick in range(sections_count):
        active = sections_count - 1 - tick
        is_active = section_index == active
        if tick + 1 < sections_count or sections_count > 4:
            result, signals = backward(top_ext, top_rim[active])
        else:
            shapes = jax.eval_shape(lambda top: backward(top, top_rim[active]), top_ext)
            result, signals = lax.cond(
                is_active,
                lambda top: backward(top, top_rim[active]),
                lambda top: jax.tree.map(lambda v: jnp.zeros(v.shape, v.dtype), shapes),
                top_ext,
            )
        result_width = top_rim[active] - layer_count
        boundary = jnp.where(is_active, crop(result, result_width), boundary)
        if tick + 1 < sections_count:
            if deep:
                pairs = [
                    (flat_index((active, r, c), sizes()), flat_index((active - 1, r, c), sizes()))
                    for r in range(row_count)
                    for c in range(col_count)
                ]
                top_ext = lax.ppermute(result, AXES, pairs)
            else:
                top_ext = with_rim(result, layer_count, 1, (active - 1,))
        if sections_count > 4:
            terms = products(signals)
        else:
            terms = lax.cond(
                is_active, products, lambda unused: jnp.zeros_like(gathered), signals
            )
        gathered = jnp.where(is_active, terms, gathered)
    gathered = summed_over_tiles(gathered)
    kernel_grad = gathered / batches
    return (boundary[None], kernel_grad)


def section_chain(top_ext, top_width, inputs_list, rim, flipped_kernels):
    layer_count = len(flipped_kernels)
    tile_rows = inputs_list[0].shape[1] - 2 * rim
    tile_cols = inputs_list[0].shape[2] - 2 * rim
    gradient = top_ext.astype(jnp.float32)
    signals = [None] * layer_count
    for layer_idx in reversed(range(layer_count)):
        width = top_width - (layer_count - 1 - layer_idx)
        output = crop(inputs_list[layer_idx + 1], rim - layer_idx - 1 - width)
        output = output.astype(jnp.float32)
        signal = gradient * (1.0 - output * output)
        signal = jnp.where(inside_mask(tile_rows, tile_cols, width), signal, 0.0)
        signal = signal.astype(jnp.bfloat16)
        signals[layer_idx] = crop(signal, width)
        gradient = convolve(signal, flipped_kernels[layer_idx])
    return gradient.astype(jnp.bfloat16), signals


def local_split(checkpoints, kernels, cotangent, plan):
    section_index = lax.axis_index("section")
    batches, tile_rows, tile_cols, channels = checkpoints.shape[1:]
    layer_count = kernels.shape[0]
    half = batches // 2
    inverse = jnp.sum(
        jnp.arange(batches)[:, None] * (plan[:, None] == jnp.arange(batches)[None, :]), axis=0
    )
    top_cotangent = jnp.take(cotangent, inverse, axis=0)

    def swap(values):
        return lax.ppermute(values, "section", [(0, 1), (1, 0)])

    def by_section(mine, theirs, section):
        return jnp.where(section_index == section, mine, theirs)

    own = checkpoints[0]
    mine = lax.dynamic_slice_in_dim(own, section_index * half, half, 0)
    theirs = swap(lax.dynamic_slice_in_dim(own, (1 - section_index) * half, half, 0))
    other_kernels = swap(kernels)
    section_kernels = [by_section(kernels, other_kernels, s) for s in range(2)]

    top_rim = [layer_count * (s + 1) for s in range(2)]
    rims = [r + layer_count for r in top_rim]
    group_cotangent = lax.dynamic_slice_in_dim(top_cotangent, section_index * half, half, 0)
    stacked = [by_section(mine, theirs, s) for s in range(2)] + [group_cotangent]
    stacked = with_rim(jnp.concatenate(stacked, axis=0), rims[1], 0, range(2))
    firsts = [crop(stacked[:half], rims[1] - rims[0]), stacked[half : 2 * half]]
    top_ext = crop(stacked[2 * half :], rims[1] - top_rim[1])

    results, partials = [None, None], [None, None]
    for s in (1, 0):
        rim = rims[s]
        inputs_list = [firsts[s]]
        current = firsts[s]
        for layer_idx in range(layer_count):
            current = jnp.tanh(convolve(current, section_kernels[s][layer_idx]))
            current = jnp.where(
                inside_mask(tile_rows, tile_cols, rim - layer_idx - 1), current, 0.0
            )
            current = current.astype(jnp.bfloat16)
            inputs_list.append(current)
        flipped = jnp.transpose(section_kernels[s][:, ::-1, ::-1], (0, 1, 2, 4, 3))
        top_ext, signals = section_chain(top_ext, top_rim[s], inputs_list, rim, flipped)
        results[s] = crop(top_ext, top_rim[s] - layer_count)
        partials[s] = [
            kernel_terms(crop(inputs_list[layer_idx], rim - layer_idx - 1), signals[layer_idx])
            for layer_idx in range(layer_count)
        ]

    scale = 1.0 / batches
    summed = []
    for layer_idx in range(layer_count):
        mine_terms = by_section(partials[0][layer_idx], partials[1][layer_idx], 0)
        other_terms = by_section(partials[1][layer_idx], partials[0][layer_idx], 0)
        other_terms = swap((other_terms * scale).astype(jnp.bfloat16)).astype(jnp.float32)
        summed.append(summed_over_tiles(mine_terms * scale + other_terms))
    gathered = jnp.stack(summed)
    mine_back = by_section(results[0], results[1], 0)
    other_back = swap(by_section(results[1], results[0], 0))
    boundary = jnp.where(
        section_index == 0,
        jnp.concatenate([mine_back, other_back], axis=0),
        jnp.concatenate([other_back, mine_back], axis=0),
    )
    return (boundary[None], gathered)


def solution(mesh):
    return jax.shard_map(
        local,
        mesh=mesh,
        in_specs=(
            P("section", None, "row", "col", None),
            P("section", None, None, None, None),
            P(None, "row", "col", None),
            P(),
        ),
        out_specs=(P("section", None, "row", "col", None), P("section", None, None, None, None)),
        check_vma=False,
    )
```

```python
import jax
import jax.numpy as jnp
from jax import lax
from jax.sharding import PartitionSpec as P

AXES = ("section", "row", "col")


def sizes():
    return tuple(lax.axis_size(axis) for axis in AXES)


def flat_index(position, shape):
    section, row, col = position
    return (section * shape[1] + row) * shape[2] + col


def rim_piece(block, width, dr, dc):
    rows, cols = block.shape[1], block.shape[2]
    row_span = {-1: (rows - width, rows), 0: (0, rows), 1: (0, width)}[dr]
    col_span = {-1: (cols - width, cols), 0: (0, cols), 1: (0, width)}[dc]
    return block[:, row_span[0] : row_span[1], col_span[0] : col_span[1]]


def from_neighbours(block, width, dim, from_section, sections_used):
    shape = sizes()
    parts = []
    for step in (-1, 0, 1):
        size = block.shape[dim]
        span = {-1: (size - width, size), 0: (0, size), 1: (0, width)}[step]
        piece = lax.slice_in_dim(block, span[0], span[1], axis=dim)
        if from_section == 0 and step == 0:
            parts.append(piece)
            continue
        pairs = []
        for s in sections_used:
            for r in range(shape[1]):
                for c in range(shape[2]):
                    source = [s + from_section, r, c]
                    source[dim] += step
                    if all(0 <= source[k] < shape[k] for k in range(3)):
                        pairs.append((flat_index(source, shape), flat_index((s, r, c), shape)))
        parts.append(lax.ppermute(piece, AXES, pairs))
    return jnp.concatenate(parts, axis=dim)


def with_rim(block, width, from_section, sections_used):
    rows_done = from_neighbours(block, width, 1, from_section, sections_used)
    return from_neighbours(rows_done, width, 2, 0, sections_used)


def inside_mask(tile_rows, tile_cols, width):
    image_rows = tile_rows * lax.axis_size("row")
    image_cols = tile_cols * lax.axis_size("col")
    rows = lax.axis_index("row") * tile_rows - width + jnp.arange(tile_rows + 2 * width)
    cols = lax.axis_index("col") * tile_cols - width + jnp.arange(tile_cols + 2 * width)
    row_ok = (rows >= 0) & (rows < image_rows)
    col_ok = (cols >= 0) & (cols < image_cols)
    return (row_ok[:, None] & col_ok[None, :])[None, :, :, None]


def convolve(padded, kernel):
    return lax.conv_general_dilated(
        padded,
        kernel,
        (1, 1),
        "VALID",
        dimension_numbers=("NHWC", "HWIO", "NHWC"),
        preferred_element_type=jnp.float32,
    )


def kernel_terms(padded, signal):
    terms = lax.conv_general_dilated(
        padded,
        signal,
        (1, 1),
        "VALID",
        dimension_numbers=("CHWN", "IHWO", "NHWC"),
        preferred_element_type=jnp.float32,
    )
    return jnp.transpose(terms, (1, 2, 0, 3))


def crop(block, width):
    return block[:, width : block.shape[1] - width, width : block.shape[2] - width]


def summed_over_tiles(grads):
    shape = sizes()
    halving, doubling = [], []
    for axis, dim in (("row", 1), ("col", 2)):
        distance = 1
        while distance < shape[dim]:
            (halving if distance == 1 else doubling).append((axis, distance))
            distance *= 2

    def exchange(values, axis, distance):
        count = lax.axis_size(axis)
        return lax.ppermute(values, axis, [(i, i ^ distance) for i in range(count)])

    current = grads.reshape(-1)
    kept = []
    for axis, distance in halving:
        half = current.shape[0] // 2
        upper = (lax.axis_index(axis) // distance) % 2 == 1
        low, high = current[:half], current[half:]
        send = jnp.where(upper, low, high).astype(jnp.bfloat16)
        mine = jnp.where(upper, high, low).astype(jnp.bfloat16)
        other = exchange(send, axis, distance)
        current = mine.astype(jnp.float32) + other.astype(jnp.float32)
        kept.append((axis, distance, upper))
    for axis, distance in doubling:
        rounded = current.astype(jnp.bfloat16)
        other = exchange(rounded, axis, distance)
        current = rounded.astype(jnp.float32) + other.astype(jnp.float32)
    current = current.astype(jnp.bfloat16)
    for axis, distance, upper in reversed(kept):
        other = exchange(current, axis, distance)
        current = jnp.where(
            upper, jnp.concatenate([other, current]), jnp.concatenate([current, other])
        )
    return current.astype(jnp.float32).reshape(grads.shape)


def local(checkpoints, kernels, cotangent, plan):
    sections_count, row_count, col_count = sizes()
    section_index = lax.axis_index("section")
    batches, tile_rows, tile_cols, channels = checkpoints.shape[1:]
    layer_count = kernels.shape[0]
    flipped = jnp.transpose(kernels[:, ::-1, ::-1], (0, 1, 2, 4, 3))
    inverse = jnp.sum(
        jnp.arange(batches)[:, None] * (plan[:, None] == jnp.arange(batches)[None, :]), axis=0
    )
    top_cotangent = jnp.take(cotangent, inverse, axis=0)

    deep = layer_count * (sections_count + 1) <= min(tile_rows, tile_cols)
    if deep and sections_count == 2 and batches % 2 == 0:
        return local_split(checkpoints, kernels, cotangent, plan)
    if deep:
        top_rim = [layer_count * (s + 1) for s in range(sections_count)]
    else:
        top_rim = [layer_count] * sections_count
    rim = top_rim[-1] + layer_count
    first = with_rim(checkpoints[0], rim, 0, range(sections_count))
    top_ext = with_rim(top_cotangent, top_rim[-1], 0, (sections_count - 1,))
    inputs_list = [first]
    current = first
    for layer_idx in range(layer_count):
        width = rim - layer_idx - 1
        current = jnp.tanh(convolve(current, kernels[layer_idx]))
        current = jnp.where(inside_mask(tile_rows, tile_cols, width), current, 0.0)
        current = current.astype(jnp.bfloat16)
        inputs_list.append(current)

    def backward(top_ext, top_width):
        gradient = top_ext.astype(jnp.float32)
        terms = [None] * layer_count
        for layer_idx in reversed(range(layer_count)):
            width = top_width - (layer_count - 1 - layer_idx)
            output = crop(inputs_list[layer_idx + 1], rim - layer_idx - 1 - width)
            output = output.astype(jnp.float32)
            signal = gradient * (1.0 - output * output)
            signal = jnp.where(inside_mask(tile_rows, tile_cols, width), signal, 0.0)
            signal = signal.astype(jnp.bfloat16)
            terms[layer_idx] = crop(signal, width)
            gradient = convolve(signal, flipped[layer_idx])
        return gradient.astype(jnp.bfloat16), terms

    def products(signals):
        return jnp.stack(
            [
                kernel_terms(crop(inputs_list[layer_idx], rim - layer_idx - 1), signals[layer_idx])
                for layer_idx in range(layer_count)
            ]
        )

    boundary = jnp.zeros((batches, tile_rows, tile_cols, channels), jnp.bfloat16)
    gathered = jnp.zeros((layer_count, 3, 3, channels, channels), jnp.float32)
    for tick in range(sections_count):
        active = sections_count - 1 - tick
        is_active = section_index == active
        if tick + 1 < sections_count or sections_count > 4:
            result, signals = backward(top_ext, top_rim[active])
        else:
            shapes = jax.eval_shape(lambda top: backward(top, top_rim[active]), top_ext)
            result, signals = lax.cond(
                is_active,
                lambda top: backward(top, top_rim[active]),
                lambda top: jax.tree.map(lambda v: jnp.zeros(v.shape, v.dtype), shapes),
                top_ext,
            )
        result_width = top_rim[active] - layer_count
        boundary = jnp.where(is_active, crop(result, result_width), boundary)
        if tick + 1 < sections_count:
            if deep:
                pairs = [
                    (flat_index((active, r, c), sizes()), flat_index((active - 1, r, c), sizes()))
                    for r in range(row_count)
                    for c in range(col_count)
                ]
                top_ext = lax.ppermute(result, AXES, pairs)
            else:
                top_ext = with_rim(result, layer_count, 1, (active - 1,))
        if sections_count > 4:
            terms = products(signals)
        else:
            terms = lax.cond(
                is_active, products, lambda unused: jnp.zeros_like(gathered), signals
            )
        gathered = jnp.where(is_active, terms, gathered)
    gathered = summed_over_tiles(gathered)
    kernel_grad = gathered / batches
    return (boundary[None], kernel_grad)


def section_chain(top_ext, top_width, inputs_list, rim, flipped_kernels):
    layer_count = len(flipped_kernels)
    tile_rows = inputs_list[0].shape[1] - 2 * rim
    tile_cols = inputs_list[0].shape[2] - 2 * rim
    gradient = top_ext.astype(jnp.float32)
    signals = [None] * layer_count
    for layer_idx in reversed(range(layer_count)):
        width = top_width - (layer_count - 1 - layer_idx)
        output = crop(inputs_list[layer_idx + 1], rim - layer_idx - 1 - width)
        output = output.astype(jnp.float32)
        signal = gradient * (1.0 - output * output)
        signal = jnp.where(inside_mask(tile_rows, tile_cols, width), signal, 0.0)
        signal = signal.astype(jnp.bfloat16)
        signals[layer_idx] = crop(signal, width)
        gradient = convolve(signal, flipped_kernels[layer_idx])
    return gradient.astype(jnp.bfloat16), signals


def local_split(checkpoints, kernels, cotangent, plan):
    section_index = lax.axis_index("section")
    batches, tile_rows, tile_cols, channels = checkpoints.shape[1:]
    layer_count = kernels.shape[0]
    half = batches // 2
    inverse = jnp.sum(
        jnp.arange(batches)[:, None] * (plan[:, None] == jnp.arange(batches)[None, :]), axis=0
    )
    top_cotangent = jnp.take(cotangent, inverse, axis=0)

    def swap(values):
        return lax.ppermute(values, "section", [(0, 1), (1, 0)])

    def by_section(mine, theirs, section):
        return jnp.where(section_index == section, mine, theirs)

    own = checkpoints[0]
    mine = lax.dynamic_slice_in_dim(own, section_index * half, half, 0)
    theirs = swap(lax.dynamic_slice_in_dim(own, (1 - section_index) * half, half, 0))
    other_kernels = swap(kernels)
    section_kernels = [by_section(kernels, other_kernels, s) for s in range(2)]

    top_rim = [layer_count * (s + 1) for s in range(2)]
    rims = [r + layer_count for r in top_rim]
    group_cotangent = lax.dynamic_slice_in_dim(top_cotangent, section_index * half, half, 0)
    stacked = [by_section(mine, theirs, s) for s in range(2)] + [group_cotangent]
    stacked = with_rim(jnp.concatenate(stacked, axis=0), rims[1], 0, range(2))
    firsts = [crop(stacked[:half], rims[1] - rims[0]), stacked[half : 2 * half]]
    top_ext = crop(stacked[2 * half :], rims[1] - top_rim[1])

    results, partials = [None, None], [None, None]
    for s in (1, 0):
        rim = rims[s]
        inputs_list = [firsts[s]]
        current = firsts[s]
        for layer_idx in range(layer_count):
            current = jnp.tanh(convolve(current, section_kernels[s][layer_idx]))
            current = jnp.where(
                inside_mask(tile_rows, tile_cols, rim - layer_idx - 1), current, 0.0
            )
            current = current.astype(jnp.bfloat16)
            inputs_list.append(current)
        flipped = jnp.transpose(section_kernels[s][:, ::-1, ::-1], (0, 1, 2, 4, 3))
        top_ext, signals = section_chain(top_ext, top_rim[s], inputs_list, rim, flipped)
        results[s] = crop(top_ext, top_rim[s] - layer_count)
        partials[s] = [
            kernel_terms(crop(inputs_list[layer_idx], rim - layer_idx - 1), signals[layer_idx])
            for layer_idx in range(layer_count)
        ]

    scale = 1.0 / batches
    summed = []
    for layer_idx in range(layer_count):
        mine_terms = by_section(partials[0][layer_idx], partials[1][layer_idx], 0)
        other_terms = by_section(partials[1][layer_idx], partials[0][layer_idx], 0)
        other_terms = swap((other_terms * scale).astype(jnp.bfloat16)).astype(jnp.float32)
        summed.append(summed_over_tiles(mine_terms * scale + other_terms))
    gathered = jnp.stack(summed)
    mine_back = by_section(results[0], results[1], 0)
    other_back = swap(by_section(results[1], results[0], 0))
    boundary = jnp.where(
        section_index == 0,
        jnp.concatenate([mine_back, other_back], axis=0),
        jnp.concatenate([other_back, mine_back], axis=0),
    )
    return (boundary[None], gathered)


def solution(mesh):
    return jax.shard_map(
        local,
        mesh=mesh,
        in_specs=(
            P("section", None, "row", "col", None),
            P("section", None, None, None, None),
            P(None, "row", "col", None),
            P(),
        ),
        out_specs=(P("section", None, "row", "col", None), P("section", None, None, None, None)),
        check_vma=False,
    )
```
